256 devices in a mesh: depth: 8 (over x, core), tile: 32 (over y, z).
Axes of the slice: x: 4, y: 4, z: 8, core: 2. Of those that a mesh axis runs over, the one named last changes fastest.
Arguments:
- volume: bfloat16 [512, 512, 1024], P('depth', 'tile'), may hold values from -6 to 6
- knot_pos: int32 [16], replicated, may hold values from 0 to 255, as said below
- knot_color: int32 [4, 16], replicated, may hold values from 0 to 255
Outputs:
- image: float32 [4, 512, 1024], P(None, 'tile', 'depth')
The draws below stay inside these ranges and needn't reach their ends.
Inputs may be any that keep to these rules, and one draw needn't show every extreme that they name: `knot_pos`: strictly increasing with neighbouring breakpoints 9 or more apart; the first is 0 and the last 255.
All inputs are finite; a program needn't handle non-finite values.
Results may differ from the reference program's by a relative error of at most 0.0003.
Values may be sent and summed in bfloat16 or wider, within the bound.
No kernel may reach another device: no remote copies, remote signals or barrier semaphores. Data moves between devices by JAX's collectives and lax.ppermute only.
A program may use at most 128 MiB of HBM per device.

```python
import jax
import jax.numpy as jnp
from jax import lax

NY = 1024
KNOTS = 16
CX = 16
NX = 512
NZ = 512
N_TILE = 32


def draw_knot_pos(key, part):
    offsets = jax.random.randint(key, (KNOTS - 2,), -4, 5).astype(jnp.int32)
    inner = (jnp.arange(1, KNOTS - 1, dtype=jnp.int32) * 17 + offsets).astype(jnp.int32)
    first = jnp.zeros((1,), jnp.int32)
    final = jnp.full((1,), 255, jnp.int32)
    return jnp.concatenate([first, inner, final]).astype(jnp.int32)


def touch_ends(entries, stream_key, smallest, top_value):
    place = [jax.random.randint(jax.random.fold_in(stream_key, axis), (), 0, length) for axis, length in enumerate(entries.shape)]
    main_axis = entries.shape.index(max(entries.shape))
    neighbour = place[:main_axis] + [(place[main_axis] + 1) % entries.shape[main_axis]] + place[main_axis + 1:]
    return entries.at[tuple(place)].set(smallest).at[tuple(neighbour)].set(top_value)


def shard_levels(stream_key, extent, pieces, smallest, high):
    factor_of = 1.0
    for position, parts in pieces:
        heights = jax.random.uniform(jax.random.fold_in(jax.random.fold_in(stream_key, 6), position), (parts,), jnp.float32, smallest / len(pieces), high / len(pieces))
        factor_of = factor_of * jnp.repeat(jnp.exp(heights), extent[position] // parts).reshape((-1,) + (1,) * (len(extent) - 1 - position))
    return factor_of


def gaussian(own_key, shape, deviation, reach, shards=(), held_as=jnp.bfloat16):
    gain = shard_levels(own_key, shape, shards, -0.22, 0.18) if shards else 1.0
    result = jax.random.normal(own_key, shape, jnp.float32) * deviation * gain
    return jnp.minimum(jnp.maximum(result, -reach), reach).astype(held_as)


def setup_inputs(seed: int = 0) -> dict:
    streams_of = jax.random.split(jax.random.key(seed), 4)
    return {
        "volume": gaussian(streams_of[0], (NZ, NX, NY), 1.0, 6.0, ((0, 8), (1, 32))),
        "knot_pos": draw_knot_pos(jax.random.fold_in(streams_of[3], 71), 0),
        "knot_color": touch_ends(jax.random.randint(streams_of[2], (4, KNOTS), 0, 256), jax.random.fold_in(streams_of[2], 1), 0, 255).astype(jnp.int32),
    }


def next_along(center):
    return jnp.pad(center[:, :, 1:], ((0, 0), (0, 0), (0, 1)))

def prior_along(center):
    return jnp.pad(center[:, :, :-1], ((0, 0), (0, 0), (1, 0)))

def smooth_block(extended):
    field = extended.astype(jnp.float32)
    center = field[1:-1, 1:-1]
    neighbours = field[2:, 1:-1] + field[:-2, 1:-1] + field[1:-1, 2:] + field[1:-1, :-2]
    neighbours = neighbours + next_along(center) + prior_along(center)
    return 0.4 * center + 0.1 * neighbours

def hat_colors(lookup, knot_pos, knot_color):
    knot_float = knot_pos.astype(jnp.float32)
    palette = knot_color.astype(jnp.float32) / 255.0
    count = knot_pos.shape[0]
    colors = [jnp.zeros_like(lookup) for c in range(3)]
    extinction = jnp.zeros_like(lookup)
    for k in range(count):
        if k == 0:
            weight = jnp.clip((knot_float[1] - lookup) / (knot_float[1] - knot_float[0]), 0.0, 1.0)
        elif k == count - 1:
            weight = jnp.clip((lookup - knot_float[k - 1]) / (knot_float[k] - knot_float[k - 1]), 0.0, 1.0)
        else:
            rising = (lookup - knot_float[k - 1]) / (knot_float[k] - knot_float[k - 1])
            falling = (knot_float[k + 1] - lookup) / (knot_float[k + 1] - knot_float[k])
            weight = jnp.maximum(0.0, jnp.minimum(rising, falling))
        colors = [colors[c] + weight * palette[c, k] for c in range(3)]
        extinction = extinction + weight * palette[3, k]
    return (colors, extinction)

def shade_classify(smooth_ext, knot_pos, knot_color, sigma_scale):
    field = smooth_ext.astype(jnp.float32)
    center = field[1:-1, 1:-1]
    slope_z = 0.5 * (field[2:, 1:-1] - field[:-2, 1:-1])
    slope_x = 0.5 * (field[1:-1, 2:] - field[1:-1, :-2])
    slope_y = 0.5 * (next_along(center) - prior_along(center))
    facing = jnp.abs(0.6 * slope_z + 0.8 * slope_x)
    shading = 0.3 + 0.7 * facing / jnp.sqrt(slope_z * slope_z + slope_x * slope_x + slope_y * slope_y + 0.1)
    knot_float = knot_pos.astype(jnp.float32)
    lookup = jnp.clip(127.5 + 70.0 * center, knot_float[0], knot_float[-1])
    colors, extinction = hat_colors(lookup, knot_pos, knot_color)
    return (shading, colors, extinction * sigma_scale)

def composite(shading, colors, extinction):
    before = jnp.cumsum(extinction, axis=0) - extinction
    weight = shading * (1.0 - jnp.exp(-extinction)) * jnp.exp(-before)
    brick_color = jnp.stack([lax.optimization_barrier(jnp.sum(weight * colors[c], axis=0)) for c in range(3)])
    return (brick_color, lax.optimization_barrier(jnp.sum(extinction, axis=0)))

def reference(volume, knot_pos, knot_color):
    sigma_scale = 4.0 / NZ
    padded = jnp.pad(volume, ((2, 2), (2, 2), (0, 0)))
    z_pos = jnp.arange(NZ + 2, dtype=jnp.int32) - 1
    z_inside = (z_pos >= 0) & (z_pos < NZ)

    def one_block(block):
        start = (block * CX).astype(jnp.int32)
        slab = lax.dynamic_slice_in_dim(padded, start, CX + 4, 1)
        smoothed = smooth_block(slab)
        x_pos = start - 1 + jnp.arange(CX + 2, dtype=jnp.int32)
        x_inside = (x_pos >= 0) & (x_pos < NX)
        inside = z_inside[:, None, None] & x_inside[None, :, None]
        smooth_ext = jnp.where(inside, smoothed, 0.0).astype(jnp.bfloat16)
        shading, colors, extinction = shade_classify(smooth_ext, knot_pos, knot_color, sigma_scale)
        brick_color, optical_depth = composite(shading, colors, extinction)
        return jnp.concatenate([brick_color, (1.0 - jnp.exp(-optical_depth))[None]], axis=0)
    blocks = lax.map(one_block, jnp.arange(N_TILE, dtype=jnp.int32))
    return jnp.transpose(blocks, (1, 0, 2, 3)).reshape(4, NX, NY)
```

```python
import jax
import jax.numpy as jnp
from jax import lax
from jax.experimental import pallas as pl
from jax.experimental.pallas import tpu as pltpu
from jax.sharding import PartitionSpec as P


def padded(block, sides, width):
    for axis, dim in sides:
        count = lax.axis_size(axis)
        forward = [(i, i + 1) for i in range(count - 1)]
        backward = [(target, source) for source, target in forward]
        low = lax.ppermute(
            lax.slice_in_dim(block, block.shape[dim] - width, None, axis=dim), axis, forward
        )
        high = lax.ppermute(lax.slice_in_dim(block, 0, width, axis=dim), axis, backward)
        block = jnp.concatenate([low, block, high], axis=dim)
    return block


def next_along(center):
    return jnp.pad(center[:, :, 1:], ((0, 0), (0, 0), (0, 1)))


def prior_along(center):
    return jnp.pad(center[:, :, :-1], ((0, 0), (0, 0), (1, 0)))


def smooth_block(extended):
    field = extended.astype(jnp.float32)
    center = field[1:-1, 1:-1]
    neighbours = field[2:, 1:-1] + field[:-2, 1:-1] + field[1:-1, 2:] + field[1:-1, :-2]
    neighbours = neighbours + next_along(center) + prior_along(center)
    return 0.4 * center + 0.1 * neighbours


def shade_lookup(smooth_ext, knot_pos):
    field = smooth_ext.astype(jnp.float32)
    center = field[1:-1, 1:-1]
    slope_z = 0.5 * (field[2:, 1:-1] - field[:-2, 1:-1])
    slope_x = 0.5 * (field[1:-1, 2:] - field[1:-1, :-2])
    slope_y = 0.5 * (next_along(center) - prior_along(center))
    facing = jnp.abs(0.6 * slope_z + 0.8 * slope_x)
    shading = 0.3 + 0.7 * facing / jnp.sqrt(
        slope_z * slope_z + slope_x * slope_x + slope_y * slope_y + 0.1
    )
    knot_float = knot_pos.astype(jnp.float32)
    lookup = jnp.clip(127.5 + 70.0 * center, knot_float[0], knot_float[-1])
    return shading, lookup


def ramp_table(knot_pos, knot_color, sigma_scale):
    knot_float = knot_pos.astype(jnp.float32)
    palette = knot_color.astype(jnp.float32) / 255.0
    palette = palette.at[3].multiply(sigma_scale)
    gaps = knot_float[1:] - knot_float[:-1]
    slopes = (palette[:, 1:] - palette[:, :-1]) / gaps[None]
    count = knot_pos.shape[0] - 1
    table = jnp.zeros((8, 128), jnp.float32)
    table = table.at[0, :count].set(knot_float[:-1])
    table = table.at[1, :count].set(gaps)
    table = table.at[2:6, :count].set(slopes)
    table = table.at[6, :4].set(palette[:, 0])
    return table


def composite_kernel(table, lookup_ref, shade_ref, color_ref, depth_ref, *, segments, rows):
    depth_len = lookup_ref.shape[0]
    width = lookup_ref.shape[2]
    knots = [table[0, k] for k in range(segments)]
    gaps = [table[1, k] for k in range(segments)]
    slopes = [[table[2 + c, k] for k in range(segments)] for c in range(4)]
    base = [table[6, c] for c in range(4)]
    for half in range(lookup_ref.shape[1] // rows):
        sl = pl.ds(half * rows, rows)

        def step(z, carry):
            trans, acc0, acc1, acc2, total = carry
            lookup = lookup_ref[z, sl, :]
            shade = shade_ref[z, sl, :]
            chan = [jnp.full_like(lookup, base[c]) for c in range(4)]
            for k in range(segments):
                t = jnp.minimum(jnp.maximum(lookup - knots[k], 0.0), gaps[k])
                chan = [chan[c] + t * slopes[c][k] for c in range(4)]
            ext = chan[3]
            fade = jnp.exp(-ext)
            weight = shade * (1.0 - fade) * trans
            acc0 = acc0 + weight * chan[0]
            acc1 = acc1 + weight * chan[1]
            acc2 = acc2 + weight * chan[2]
            return (trans * fade, acc0, acc1, acc2, total + ext)

        zeros = jnp.zeros((rows, width), jnp.float32)
        init = (jnp.ones((rows, width), jnp.float32), zeros, zeros, zeros, zeros)
        _, acc0, acc1, acc2, total = lax.fori_loop(0, depth_len, step, init, unroll=2)
        color_ref[0, sl, :] = acc0
        color_ref[1, sl, :] = acc1
        color_ref[2, sl, :] = acc2
        depth_ref[sl, :] = total


def composite_block(table, lookup, shading, segments):
    depth_len, rows_all, width_all = lookup.shape
    width = 256
    rows = 8
    kernel = lambda *refs: composite_kernel(*refs, segments=segments, rows=rows)
    grid_spec = pltpu.PrefetchScalarGridSpec(
        num_scalar_prefetch=1,
        grid=(width_all // width,),
        in_specs=[
            pl.BlockSpec((depth_len, rows_all, width), lambda j, t: (0, 0, j)),
            pl.BlockSpec((depth_len, rows_all, width), lambda j, t: (0, 0, j)),
        ],
        out_specs=[
            pl.BlockSpec((3, rows_all, width), lambda j, t: (0, 0, j)),
            pl.BlockSpec((rows_all, width), lambda j, t: (0, j)),
        ],
    )
    return pl.pallas_call(
        kernel,
        grid_spec=grid_spec,
        out_shape=[
            jax.ShapeDtypeStruct((3, rows_all, width_all), jnp.float32),
            jax.ShapeDtypeStruct((rows_all, width_all), jnp.float32),
        ],
    )(table, lookup, shading)


def body(volume, knot_pos, knot_color):
    depth_count = lax.axis_size("depth")
    brick_depth, brick_rows, row_width = volume.shape
    sigma_scale = 4.0 / (brick_depth * depth_count)
    extended = padded(volume, (("depth", 0), ("tile", 1)), 1)
    smoothed = smooth_block(extended).astype(jnp.bfloat16)
    smooth_ext = padded(smoothed, (("depth", 0), ("tile", 1)), 1)
    shading, lookup = shade_lookup(smooth_ext, knot_pos)
    table = ramp_table(knot_pos, knot_color, sigma_scale)
    brick_color, optical_depth = composite_block(table, lookup, shading, knot_pos.shape[0] - 1)
    piece = row_width // depth_count
    weighted = jnp.concatenate([brick_color, optical_depth[None]], axis=0)
    weighted = weighted.reshape(4, brick_rows, depth_count, piece).transpose(2, 0, 1, 3)
    blocks = lax.all_to_all(weighted, "depth", 0, 0, tiled=True)
    ahead = jnp.zeros((brick_rows, piece), jnp.float32)
    image = jnp.zeros((3, brick_rows, piece), jnp.float32)
    for b in range(depth_count):
        image = image + blocks[b, :3] * jnp.exp(-ahead)[None]
        ahead = ahead + blocks[b, 3]
    return jnp.concatenate([image, (1.0 - jnp.exp(-ahead))[None]], axis=0)


def solution(mesh):
    in_specs = (P("depth", "tile", None), P(), P())
    out_specs = P(None, "tile", "depth")
    return jax.shard_map(body, mesh=mesh, in_specs=in_specs, out_specs=out_specs, check_vma=False)
```

```python
import jax
import jax.numpy as jnp
from jax import lax
from jax.experimental import pallas as pl
from jax.experimental.pallas import tpu as pltpu
from jax.sharding import PartitionSpec as P


def padded(block, sides, width):
    for axis, dim in sides:
        count = lax.axis_size(axis)
        forward = [(i, i + 1) for i in range(count - 1)]
        backward = [(target, source) for source, target in forward]
        low = lax.ppermute(
            lax.slice_in_dim(block, block.shape[dim] - width, None, axis=dim), axis, forward
        )
        high = lax.ppermute(lax.slice_in_dim(block, 0, width, axis=dim), axis, backward)
        block = jnp.concatenate([low, block, high], axis=dim)
    return block


def shifted(block, axes, moves):
    sizes = [lax.axis_size(a) for a in axes]
    pairs = []
    for index in range(sizes[0] * (sizes[1] if len(sizes) > 1 else 1)):
        coords = [index] if len(sizes) == 1 else [index // sizes[1], index % sizes[1]]
        target = [c + m for c, m in zip(coords, moves)]
        if all(0 <= c < s for c, s in zip(target, sizes)):
            flat = target[0] if len(sizes) == 1 else target[0] * sizes[1] + target[1]
            pairs.append((index, flat))
    return lax.ppermute(block, axes if len(axes) > 1 else axes[0], pairs)


def extended_volume(volume):
    depth, rows, width = volume.shape
    dz = ("depth",)
    tx = ("tile",)
    both = ("depth", "tile")
    z_low = shifted(volume[depth - 2:], dz, (1,))
    z_high = shifted(volume[:2], dz, (-1,))
    x_low = shifted(volume[:, rows - 2:], tx, (1,))
    x_high = shifted(volume[:, :2], tx, (-1,))
    c_ll = shifted(volume[depth - 1:, rows - 1:], both, (1, 1))
    c_lh = shifted(volume[depth - 1:, :1], both, (1, -1))
    c_hl = shifted(volume[:1, rows - 1:], both, (-1, 1))
    c_hh = shifted(volume[:1, :1], both, (-1, -1))
    zero1 = jnp.zeros((1, 1, width), volume.dtype)
    zero2 = jnp.zeros((2, 2, width), volume.dtype)
    left = jnp.concatenate(
        [zero2[:1], jnp.concatenate([zero1, c_ll], 1), x_low,
         jnp.concatenate([zero1, c_hl], 1), zero2[:1]], axis=0)
    right = jnp.concatenate(
        [zero2[:1], jnp.concatenate([c_lh, zero1], 1), x_high,
         jnp.concatenate([c_hh, zero1], 1), zero2[:1]], axis=0)
    middle = jnp.concatenate([z_low, volume, z_high], axis=0)
    return jnp.concatenate([left, middle, right], axis=1)


def inside_mask(depth_len, rows):
    d = lax.axis_index("depth")
    t = lax.axis_index("tile")
    z = lax.broadcasted_iota(jnp.int32, (depth_len, rows, 1), 0)
    x = lax.broadcasted_iota(jnp.int32, (depth_len, rows, 1), 1)
    keep = jnp.ones((depth_len, rows, 1), jnp.bool_)
    keep = keep & ~((z == 0) & (d == 0))
    keep = keep & ~((z == depth_len - 1) & (d == lax.axis_size("depth") - 1))
    keep = keep & ~((x == 0) & (t == 0))
    keep = keep & ~((x == rows - 1) & (t == lax.axis_size("tile") - 1))
    return keep


def next_along(center):
    return jnp.pad(center[:, :, 1:], ((0, 0), (0, 0), (0, 1)))


def prior_along(center):
    return jnp.pad(center[:, :, :-1], ((0, 0), (0, 0), (1, 0)))


def smooth_block(extended):
    field = extended.astype(jnp.float32)
    center = field[1:-1, 1:-1]
    neighbours = field[2:, 1:-1] + field[:-2, 1:-1] + field[1:-1, 2:] + field[1:-1, :-2]
    neighbours = neighbours + next_along(center) + prior_along(center)
    return 0.4 * center + 0.1 * neighbours


def shade_lookup(smooth_ext, knot_pos):
    field = smooth_ext.astype(jnp.float32)
    center = field[1:-1, 1:-1]
    slope_z = 0.5 * (field[2:, 1:-1] - field[:-2, 1:-1])
    slope_x = 0.5 * (field[1:-1, 2:] - field[1:-1, :-2])
    slope_y = 0.5 * (next_along(center) - prior_along(center))
    facing = jnp.abs(0.6 * slope_z + 0.8 * slope_x)
    shading = 0.3 + 0.7 * facing / jnp.sqrt(
        slope_z * slope_z + slope_x * slope_x + slope_y * slope_y + 0.1
    )
    knot_float = knot_pos.astype(jnp.float32)
    lookup = jnp.clip(127.5 + 70.0 * center, knot_float[0], knot_float[-1])
    return shading, lookup


def ramp_table(knot_pos, knot_color, sigma_scale):
    knot_float = knot_pos.astype(jnp.float32)
    palette = knot_color.astype(jnp.float32) / 255.0
    palette = palette.at[3].multiply(sigma_scale)
    gaps = knot_float[1:] - knot_float[:-1]
    slopes = (palette[:, 1:] - palette[:, :-1]) / gaps[None]
    count = knot_pos.shape[0] - 1
    table = jnp.zeros((8, 128), jnp.float32)
    table = table.at[0, :count].set(knot_float[:-1])
    table = table.at[1, :count].set(gaps)
    table = table.at[2:6, :count].set(slopes)
    table = table.at[6, :4].set(palette[:, 0])
    return table


def composite_kernel(table, lookup_ref, shade_ref, color_ref, depth_ref, *, segments, rows):
    depth_len = lookup_ref.shape[0]
    width = lookup_ref.shape[2]
    knots = [table[0, k] for k in range(segments)]
    gaps = [table[1, k] for k in range(segments)]
    slopes = [[table[2 + c, k] for k in range(segments)] for c in range(4)]
    base = [table[6, c] for c in range(4)]
    for half in range(lookup_ref.shape[1] // rows):
        sl = pl.ds(half * rows, rows)

        def step(z, carry):
            trans, acc0, acc1, acc2, total = carry
            lookup = lookup_ref[z, sl, :]
            shade = shade_ref[z, sl, :]
            chan = [jnp.full_like(lookup, base[c]) for c in range(4)]
            for k in range(segments):
                t = jnp.minimum(jnp.maximum(lookup - knots[k], 0.0), gaps[k])
                chan = [chan[c] + t * slopes[c][k] for c in range(4)]
            ext = chan[3]
            fade = jnp.exp(-ext)
            weight = shade * (1.0 - fade) * trans
            acc0 = acc0 + weight * chan[0]
            acc1 = acc1 + weight * chan[1]
            acc2 = acc2 + weight * chan[2]
            return (trans * fade, acc0, acc1, acc2, total + ext)

        zeros = jnp.zeros((rows, width), jnp.float32)
        init = (jnp.ones((rows, width), jnp.float32), zeros, zeros, zeros, zeros)
        _, acc0, acc1, acc2, total = lax.fori_loop(0, depth_len, step, init, unroll=2)
        color_ref[0, sl, :] = acc0
        color_ref[1, sl, :] = acc1
        color_ref[2, sl, :] = acc2
        depth_ref[sl, :] = total


def composite_block(table, lookup, shading, segments):
    depth_len, rows_all, width_all = lookup.shape
    width = 256
    rows = 8
    kernel = lambda *refs: composite_kernel(*refs, segments=segments, rows=rows)
    grid_spec = pltpu.PrefetchScalarGridSpec(
        num_scalar_prefetch=1,
        grid=(width_all // width,),
        in_specs=[
            pl.BlockSpec((depth_len, rows_all, width), lambda j, t: (0, 0, j)),
            pl.BlockSpec((depth_len, rows_all, width), lambda j, t: (0, 0, j)),
        ],
        out_specs=[
            pl.BlockSpec((3, rows_all, width), lambda j, t: (0, 0, j)),
            pl.BlockSpec((rows_all, width), lambda j, t: (0, j)),
        ],
    )
    return pl.pallas_call(
        kernel,
        grid_spec=grid_spec,
        out_shape=[
            jax.ShapeDtypeStruct((3, rows_all, width_all), jnp.float32),
            jax.ShapeDtypeStruct((rows_all, width_all), jnp.float32),
        ],
    )(table, lookup, shading)


def body(volume, knot_pos, knot_color):
    depth_count = lax.axis_size("depth")
    brick_depth, brick_rows, row_width = volume.shape
    sigma_scale = 4.0 / (brick_depth * depth_count)
    extended = extended_volume(volume)
    smoothed = smooth_block(extended)
    keep = inside_mask(smoothed.shape[0], smoothed.shape[1])
    smooth_ext = jnp.where(keep, smoothed, 0.0).astype(jnp.bfloat16)
    shading, lookup = shade_lookup(smooth_ext, knot_pos)
    table = ramp_table(knot_pos, knot_color, sigma_scale)
    brick_color, optical_depth = composite_block(table, lookup, shading, knot_pos.shape[0] - 1)
    piece = row_width // depth_count
    weighted = jnp.concatenate([brick_color, optical_depth[None]], axis=0)
    weighted = weighted.reshape(4, brick_rows, depth_count, piece).transpose(2, 0, 1, 3)
    blocks = lax.all_to_all(weighted, "depth", 0, 0, tiled=True)
    ahead = jnp.zeros((brick_rows, piece), jnp.float32)
    image = jnp.zeros((3, brick_rows, piece), jnp.float32)
    for b in range(depth_count):
        image = image + blocks[b, :3] * jnp.exp(-ahead)[None]
        ahead = ahead + blocks[b, 3]
    return jnp.concatenate([image, (1.0 - jnp.exp(-ahead))[None]], axis=0)


def solution(mesh):
    in_specs = (P("depth", "tile", None), P(), P())
    out_specs = P(None, "tile", "depth")
    return jax.shard_map(body, mesh=mesh, in_specs=in_specs, out_specs=out_specs, check_vma=False)
```

```python
import jax
import jax.numpy as jnp
from jax import lax
from jax.experimental import pallas as pl
from jax.experimental.pallas import tpu as pltpu
from jax.sharding import PartitionSpec as P


def padded(block, sides, width):
    for axis, dim in sides:
        count = lax.axis_size(axis)
        forward = [(i, i + 1) for i in range(count - 1)]
        backward = [(target, source) for source, target in forward]
        low = lax.ppermute(
            lax.slice_in_dim(block, block.shape[dim] - width, None, axis=dim), axis, forward
        )
        high = lax.ppermute(lax.slice_in_dim(block, 0, width, axis=dim), axis, backward)
        block = jnp.concatenate([low, block, high], axis=dim)
    return block


def shifted(block, axes, moves):
    sizes = [lax.axis_size(a) for a in axes]
    pairs = []
    for index in range(sizes[0] * (sizes[1] if len(sizes) > 1 else 1)):
        coords = [index] if len(sizes) == 1 else [index // sizes[1], index % sizes[1]]
        target = [c + m for c, m in zip(coords, moves)]
        if all(0 <= c < s for c, s in zip(target, sizes)):
            flat = target[0] if len(sizes) == 1 else target[0] * sizes[1] + target[1]
            pairs.append((index, flat))
    return lax.ppermute(block, axes if len(axes) > 1 else axes[0], pairs)


def extended_volume(volume):
    depth, rows, width = volume.shape
    dz = ("depth",)
    tx = ("tile",)
    both = ("depth", "tile")
    z_low = shifted(volume[depth - 2:], dz, (1,))
    z_high = shifted(volume[:2], dz, (-1,))
    x_low = shifted(volume[:, rows - 2:], tx, (1,))
    x_high = shifted(volume[:, :2], tx, (-1,))
    c_ll = shifted(volume[depth - 1:, rows - 1:], both, (1, 1))
    c_lh = shifted(volume[depth - 1:, :1], both, (1, -1))
    c_hl = shifted(volume[:1, rows - 1:], both, (-1, 1))
    c_hh = shifted(volume[:1, :1], both, (-1, -1))
    zero1 = jnp.zeros((1, 1, width), volume.dtype)
    zero2 = jnp.zeros((2, 2, width), volume.dtype)
    left = jnp.concatenate(
        [zero2[:1], jnp.concatenate([zero1, c_ll], 1), x_low,
         jnp.concatenate([zero1, c_hl], 1), zero2[:1]], axis=0)
    right = jnp.concatenate(
        [zero2[:1], jnp.concatenate([c_lh, zero1], 1), x_high,
         jnp.concatenate([c_hh, zero1], 1), zero2[:1]], axis=0)
    middle = jnp.concatenate([z_low, volume, z_high], axis=0)
    gap = jnp.zeros((depth + 4, 4, width), volume.dtype)
    return jnp.concatenate([middle, right, gap, left], axis=1).astype(jnp.float32)


def inside_mask(depth_len, rows):
    d = lax.axis_index("depth")
    t = lax.axis_index("tile")
    z = lax.broadcasted_iota(jnp.int32, (depth_len, rows, 1), 0)
    x = lax.broadcasted_iota(jnp.int32, (depth_len, rows, 1), 1)
    keep = jnp.ones((depth_len, rows, 1), jnp.bool_)
    keep = keep & ~((z == 0) & (d == 0))
    keep = keep & ~((z == depth_len - 1) & (d == lax.axis_size("depth") - 1))
    keep = keep & ~((x == 0) & (t == 0))
    keep = keep & ~((x == rows - 1) & (t == lax.axis_size("tile") - 1))
    return keep


def next_along(center):
    return jnp.pad(center[:, :, 1:], ((0, 0), (0, 0), (0, 1)))


def prior_along(center):
    return jnp.pad(center[:, :, :-1], ((0, 0), (0, 0), (1, 0)))


def smooth_block(extended):
    field = extended.astype(jnp.float32)
    center = field[1:-1, 1:-1]
    neighbours = field[2:, 1:-1] + field[:-2, 1:-1] + field[1:-1, 2:] + field[1:-1, :-2]
    neighbours = neighbours + next_along(center) + prior_along(center)
    return 0.4 * center + 0.1 * neighbours


def shade_lookup(smooth_ext, knot_pos):
    field = smooth_ext.astype(jnp.float32)
    center = field[1:-1, 1:-1]
    slope_z = 0.5 * (field[2:, 1:-1] - field[:-2, 1:-1])
    slope_x = 0.5 * (field[1:-1, 2:] - field[1:-1, :-2])
    slope_y = 0.5 * (next_along(center) - prior_along(center))
    facing = jnp.abs(0.6 * slope_z + 0.8 * slope_x)
    shading = 0.3 + 0.7 * facing / jnp.sqrt(
        slope_z * slope_z + slope_x * slope_x + slope_y * slope_y + 0.1
    )
    knot_float = knot_pos.astype(jnp.float32)
    lookup = jnp.clip(127.5 + 70.0 * center, knot_float[0], knot_float[-1])
    return shading, lookup


def ramp_table(knot_pos, knot_color, sigma_scale):
    knot_float = knot_pos.astype(jnp.float32)
    palette = knot_color.astype(jnp.float32) / 255.0
    palette = palette.at[3].multiply(sigma_scale)
    gaps = knot_float[1:] - knot_float[:-1]
    slopes = (palette[:, 1:] - palette[:, :-1]) / gaps[None]
    count = knot_pos.shape[0] - 1
    table = jnp.zeros((8, 128), jnp.float32)
    table = table.at[0, :count].set(knot_float[:-1])
    table = table.at[1, :count].set(gaps)
    table = table.at[2:6, :count].set(slopes)
    table = table.at[6, :4].set(palette[:, 0])
    table = table.at[7, 0].set(knot_float[0])
    table = table.at[7, 1].set(knot_float[-1])
    return table


def render_kernel(table, flags, planes_ref, color_ref, depth_ref, smooth_ref, square_ref, facing_ref,
                  *, segments, rows, width):
    stack, tall, lanes = planes_ref.shape
    count = stack - 2
    row = lax.broadcasted_iota(jnp.int32, (tall, lanes), 0)
    keep_rows = ((row != tall - 1) | (flags[2] == 0)) & ((row != rows) | (flags[3] == 0))

    def y_prev(a):
        lane = lax.broadcasted_iota(jnp.int32, a.shape, 1)
        return jnp.where(lane == 0, 0.0, pltpu.roll(a, 1, 1))

    def y_next(a):
        lane = lax.broadcasted_iota(jnp.int32, a.shape, 1)
        return jnp.where(lane == lanes - 1, 0.0, pltpu.roll(a, lanes - 1, 1))

    def smooth_plane(i, carry):
        low = planes_ref[i]
        mid = planes_ref[i + 1]
        high = planes_ref[i + 2]
        x_prev = pltpu.roll(mid, 1, 0)
        x_next = pltpu.roll(mid, tall - 1, 0)
        near = low + high + x_next + x_prev
        near = near + y_prev(mid) + y_next(mid)
        smooth = 0.4 * mid + 0.1 * near
        inside = (i > 0) | (flags[0] == 0)
        inside = inside & ((i < count - 1) | (flags[1] == 0))
        smooth = jnp.where(keep_rows & inside, smooth, 0.0)
        smooth = smooth.astype(jnp.bfloat16).astype(jnp.float32)
        center = smooth[:rows]
        slope_x = 0.5 * (pltpu.roll(smooth, tall - 1, 0)[:rows] - pltpu.roll(smooth, 1, 0)[:rows])
        slope_y = 0.5 * (y_next(center) - y_prev(center))
        smooth_ref[i] = center
        square_ref[i] = slope_x * slope_x + slope_y * slope_y
        facing_ref[i] = 0.8 * slope_x
        return carry

    lax.fori_loop(0, count, smooth_plane, 0)

    knots = [table[0, k] for k in range(segments)]
    gaps = [table[1, k] for k in range(segments)]
    slopes = [[table[2 + c, k] for k in range(segments)] for c in range(4)]
    base = [table[6, c] for c in range(4)]
    lo = table[7, 0]
    hi = table[7, 1]
    sub = 8
    for r0 in range(0, rows, sub):
        for c0 in range(0, lanes, width):
            rs = pl.ds(r0, sub)
            cs = pl.ds(c0, width)

            def step(z, carry):
                trans, acc0, acc1, acc2, total = carry
                center = smooth_ref[z + 1, rs, cs]
                slope_z = 0.5 * (smooth_ref[z + 2, rs, cs] - smooth_ref[z, rs, cs])
                facing = jnp.abs(0.6 * slope_z + facing_ref[z + 1, rs, cs])
                norm = slope_z * slope_z + square_ref[z + 1, rs, cs] + 0.1
                shade = 0.3 + 0.7 * facing * lax.rsqrt(norm)
                lookup = jnp.clip(127.5 + 70.0 * center, lo, hi)
                chan = [jnp.full_like(lookup, base[c]) for c in range(4)]
                for k in range(segments):
                    t = jnp.minimum(jnp.maximum(lookup - knots[k], 0.0), gaps[k])
                    chan = [chan[c] + t * slopes[c][k] for c in range(4)]
                ext = chan[3]
                fade = jnp.exp(-ext)
                weight = shade * (1.0 - fade) * trans
                acc0 = acc0 + weight * chan[0]
                acc1 = acc1 + weight * chan[1]
                acc2 = acc2 + weight * chan[2]
                return (trans * fade, acc0, acc1, acc2, total + ext)

            zeros = jnp.zeros((sub, width), jnp.float32)
            init = (jnp.ones((sub, width), jnp.float32), zeros, zeros, zeros, zeros)
            _, acc0, acc1, acc2, total = lax.fori_loop(0, count - 2, step, init, unroll=2)
            color_ref[0, rs, cs] = acc0
            color_ref[1, rs, cs] = acc1
            color_ref[2, rs, cs] = acc2
            depth_ref[rs, cs] = total


def render_block(table, flags, planes, rows, segments):
    stack, tall, lanes = planes.shape
    count = stack - 2
    kernel = lambda *refs: render_kernel(*refs, segments=segments, rows=rows, width=256)
    return pl.pallas_call(
        kernel,
        in_specs=[
            pl.BlockSpec(memory_space=pltpu.SMEM),
            pl.BlockSpec(memory_space=pltpu.SMEM),
            pl.BlockSpec(memory_space=pltpu.VMEM),
        ],
        out_specs=[
            pl.BlockSpec(memory_space=pltpu.VMEM),
            pl.BlockSpec(memory_space=pltpu.VMEM),
        ],
        out_shape=[
            jax.ShapeDtypeStruct((3, rows, lanes), jnp.float32),
            jax.ShapeDtypeStruct((rows, lanes), jnp.float32),
        ],
        scratch_shapes=[pltpu.VMEM((count, rows, lanes), jnp.float32) for _ in range(3)],
        compiler_params=pltpu.CompilerParams(vmem_limit_bytes=48 * 1024 * 1024),
    )(table, flags, planes)


def body(volume, knot_pos, knot_color):
    depth_count = lax.axis_size("depth")
    brick_depth, brick_rows, row_width = volume.shape
    sigma_scale = 4.0 / (brick_depth * depth_count)
    planes = extended_volume(volume)
    d = lax.axis_index("depth")
    t = lax.axis_index("tile")
    flags = jnp.stack([d == 0, d == depth_count - 1, t == 0, t == lax.axis_size("tile") - 1])
    table = ramp_table(knot_pos, knot_color, sigma_scale)
    brick_color, optical_depth = render_block(
        table, flags.astype(jnp.int32), planes, brick_rows, knot_pos.shape[0] - 1)
    piece = row_width // depth_count
    weighted = jnp.concatenate([brick_color, optical_depth[None]], axis=0)
    weighted = weighted.reshape(4, brick_rows, depth_count, piece).transpose(2, 0, 1, 3)
    blocks = lax.all_to_all(weighted, "depth", 0, 0, tiled=True)
    ahead = jnp.zeros((brick_rows, piece), jnp.float32)
    image = jnp.zeros((3, brick_rows, piece), jnp.float32)
    for b in range(depth_count):
        image = image + blocks[b, :3] * jnp.exp(-ahead)[None]
        ahead = ahead + blocks[b, 3]
    return jnp.concatenate([image, (1.0 - jnp.exp(-ahead))[None]], axis=0)


def solution(mesh):
    in_specs = (P("depth", "tile", None), P(), P())
    out_specs = P(None, "tile", "depth")
    return jax.shard_map(body, mesh=mesh, in_specs=in_specs, out_specs=out_specs, check_vma=False)
```

```python
import jax
import jax.numpy as jnp
from jax import lax
from jax.experimental import pallas as pl
from jax.experimental.pallas import tpu as pltpu
from jax.sharding import PartitionSpec as P


def padded(block, sides, width):
    for axis, dim in sides:
        count = lax.axis_size(axis)
        forward = [(i, i + 1) for i in range(count - 1)]
        backward = [(target, source) for source, target in forward]
        low = lax.ppermute(
            lax.slice_in_dim(block, block.shape[dim] - width, None, axis=dim), axis, forward
        )
        high = lax.ppermute(lax.slice_in_dim(block, 0, width, axis=dim), axis, backward)
        block = jnp.concatenate([low, block, high], axis=dim)
    return block


def shifted(block, axes, moves):
    sizes = [lax.axis_size(a) for a in axes]
    pairs = []
    for index in range(sizes[0] * (sizes[1] if len(sizes) > 1 else 1)):
        coords = [index] if len(sizes) == 1 else [index // sizes[1], index % sizes[1]]
        target = [c + m for c, m in zip(coords, moves)]
        if all(0 <= c < s for c, s in zip(target, sizes)):
            flat = target[0] if len(sizes) == 1 else target[0] * sizes[1] + target[1]
            pairs.append((index, flat))
    return lax.ppermute(block, axes if len(axes) > 1 else axes[0], pairs)


def extended_volume(volume):
    depth, rows, width = volume.shape
    dz = ("depth",)
    tx = ("tile",)
    both = ("depth", "tile")
    z_low = shifted(volume[depth - 2:], dz, (1,))
    z_high = shifted(volume[:2], dz, (-1,))
    x_low = shifted(volume[:, rows - 2:], tx, (1,))
    x_high = shifted(volume[:, :2], tx, (-1,))
    c_ll = shifted(volume[depth - 1:, rows - 1:], both, (1, 1))
    c_lh = shifted(volume[depth - 1:, :1], both, (1, -1))
    c_hl = shifted(volume[:1, rows - 1:], both, (-1, 1))
    c_hh = shifted(volume[:1, :1], both, (-1, -1))
    zero1 = jnp.zeros((1, 1, width), volume.dtype)
    zero2 = jnp.zeros((2, 2, width), volume.dtype)
    left = jnp.concatenate(
        [zero2[:1], jnp.concatenate([zero1, c_ll], 1), x_low,
         jnp.concatenate([zero1, c_hl], 1), zero2[:1]], axis=0)
    right = jnp.concatenate(
        [zero2[:1], jnp.concatenate([c_lh, zero1], 1), x_high,
         jnp.concatenate([c_hh, zero1], 1), zero2[:1]], axis=0)
    middle = jnp.concatenate([z_low, volume, z_high], axis=0)
    gap = jnp.zeros((depth + 4, 4, width), volume.dtype)
    return jnp.concatenate([middle, right, gap, left], axis=1).astype(jnp.float32)


def inside_mask(depth_len, rows):
    d = lax.axis_index("depth")
    t = lax.axis_index("tile")
    z = lax.broadcasted_iota(jnp.int32, (depth_len, rows, 1), 0)
    x = lax.broadcasted_iota(jnp.int32, (depth_len, rows, 1), 1)
    keep = jnp.ones((depth_len, rows, 1), jnp.bool_)
    keep = keep & ~((z == 0) & (d == 0))
    keep = keep & ~((z == depth_len - 1) & (d == lax.axis_size("depth") - 1))
    keep = keep & ~((x == 0) & (t == 0))
    keep = keep & ~((x == rows - 1) & (t == lax.axis_size("tile") - 1))
    return keep


def next_along(center):
    return jnp.pad(center[:, :, 1:], ((0, 0), (0, 0), (0, 1)))


def prior_along(center):
    return jnp.pad(center[:, :, :-1], ((0, 0), (0, 0), (1, 0)))


def smooth_block(extended):
    field = extended.astype(jnp.float32)
    center = field[1:-1, 1:-1]
    neighbours = field[2:, 1:-1] + field[:-2, 1:-1] + field[1:-1, 2:] + field[1:-1, :-2]
    neighbours = neighbours + next_along(center) + prior_along(center)
    return 0.4 * center + 0.1 * neighbours


def shade_lookup(smooth_ext, knot_pos):
    field = smooth_ext.astype(jnp.float32)
    center = field[1:-1, 1:-1]
    slope_z = 0.5 * (field[2:, 1:-1] - field[:-2, 1:-1])
    slope_x = 0.5 * (field[1:-1, 2:] - field[1:-1, :-2])
    slope_y = 0.5 * (next_along(center) - prior_along(center))
    facing = jnp.abs(0.6 * slope_z + 0.8 * slope_x)
    shading = 0.3 + 0.7 * facing / jnp.sqrt(
        slope_z * slope_z + slope_x * slope_x + slope_y * slope_y + 0.1
    )
    knot_float = knot_pos.astype(jnp.float32)
    lookup = jnp.clip(127.5 + 70.0 * center, knot_float[0], knot_float[-1])
    return shading, lookup


def segment_tables(knot_pos, knot_color, sigma_scale):
    knot_float = knot_pos.astype(jnp.float32)
    palette = knot_color.astype(jnp.float32) / 255.0
    palette = palette.at[3].multiply(sigma_scale)
    count = knot_pos.shape[0]
    inner = knot_float[1:count - 1]
    bins = 32
    start = 8.0 * jnp.arange(bins, dtype=jnp.float32)
    in_bin = (inner[None, :] >= start[:, None]) & (inner[None, :] < start[:, None] + 8.0)
    threshold = jnp.where(in_bin.any(axis=1), jnp.sum(jnp.where(in_bin, inner[None, :], 0.0), axis=1), 1e30)
    below = jnp.sum((inner[None, :] < start[:, None]).astype(jnp.int32), axis=1)
    segment = jnp.minimum(jnp.stack([below, below + 1], axis=1).reshape(-1), count - 2)
    gaps = knot_float[1:] - knot_float[:-1]
    slopes = (palette[:, 1:] - palette[:, :-1]) / gaps[None]
    rows = [threshold, knot_float[segment]]
    rows += [palette[c, segment] for c in range(4)]
    rows += [slopes[c, segment] for c in range(4)]
    table = jnp.zeros((len(rows), 128), jnp.float32)
    for r, values in enumerate(rows):
        table = table.at[r, :values.shape[0]].set(values)
    bounds = jnp.zeros((8, 128), jnp.float32).at[0, 0].set(knot_float[0]).at[0, 1].set(knot_float[-1])
    return jnp.broadcast_to(table[:, None, :], (len(rows), 8, 128)), bounds


def render_kernel(table, flags, lanes_ref, planes_ref, color_ref, depth_ref, smooth_ref, square_ref, facing_ref,
                  *, segments, rows, width):
    stack, tall, lanes = planes_ref.shape
    count = stack - 2
    row = lax.broadcasted_iota(jnp.int32, (tall, lanes), 0)
    keep_rows = ((row != tall - 1) | (flags[2] == 0)) & ((row != rows) | (flags[3] == 0))

    def y_prev(a):
        lane = lax.broadcasted_iota(jnp.int32, a.shape, 1)
        return jnp.where(lane == 0, 0.0, pltpu.roll(a, 1, 1))

    def y_next(a):
        lane = lax.broadcasted_iota(jnp.int32, a.shape, 1)
        return jnp.where(lane == lanes - 1, 0.0, pltpu.roll(a, lanes - 1, 1))

    def smooth_plane(i, carry):
        low = planes_ref[i]
        mid = planes_ref[i + 1]
        high = planes_ref[i + 2]
        x_prev = pltpu.roll(mid, 1, 0)
        x_next = pltpu.roll(mid, tall - 1, 0)
        near = low + high + x_next + x_prev
        near = near + y_prev(mid) + y_next(mid)
        smooth = 0.4 * mid + 0.1 * near
        inside = (i > 0) | (flags[0] == 0)
        inside = inside & ((i < count - 1) | (flags[1] == 0))
        smooth = jnp.where(keep_rows & inside, smooth, 0.0)
        smooth = smooth.astype(jnp.bfloat16).astype(jnp.float32)
        center = smooth[:rows]
        slope_x = 0.5 * (pltpu.roll(smooth, tall - 1, 0)[:rows] - pltpu.roll(smooth, 1, 0)[:rows])
        slope_y = 0.5 * (y_next(center) - y_prev(center))
        smooth_ref[i] = center
        square_ref[i] = slope_x * slope_x + slope_y * slope_y
        facing_ref[i] = 0.8 * slope_x
        return carry

    lax.fori_loop(0, count, smooth_plane, 0)

    lo = table[0, 0]
    hi = table[0, 1]
    sub = 8
    for r0 in range(0, rows, sub):
        for c0 in range(0, lanes, width):
            rs = pl.ds(r0, sub)
            cs = pl.ds(c0, width)
            tabs = [lanes_ref[r] for r in range(lanes_ref.shape[0])]

            def classify(lookup):
                scaled = (lookup * 0.125).astype(jnp.int32)
                above = lookup >= jnp.take_along_axis(tabs[0], scaled, axis=1, mode="promise_in_bounds")
                index = scaled + scaled + above.astype(jnp.int32)
                pick = lambda r: jnp.take_along_axis(tabs[r], index, axis=1, mode="promise_in_bounds")
                offset = lookup - pick(1)
                return [pick(2 + c) + pick(6 + c) * offset for c in range(4)]

            def step(z, carry):
                trans, acc0, acc1, acc2, total = carry
                center = smooth_ref[z + 1, rs, cs]
                slope_z = 0.5 * (smooth_ref[z + 2, rs, cs] - smooth_ref[z, rs, cs])
                facing = jnp.abs(0.6 * slope_z + facing_ref[z + 1, rs, cs])
                norm = slope_z * slope_z + square_ref[z + 1, rs, cs] + 0.1
                shade = 0.3 + 0.7 * facing * lax.rsqrt(norm)
                lookup = jnp.clip(127.5 + 70.0 * center, lo, hi)
                parts = [classify(lookup[:, g:g + 128]) for g in range(0, width, 128)]
                chan = [jnp.concatenate([p[c] for p in parts], axis=1) for c in range(4)]
                ext = chan[3]
                fade = jnp.exp(-ext)
                weight = shade * (1.0 - fade) * trans
                acc0 = acc0 + weight * chan[0]
                acc1 = acc1 + weight * chan[1]
                acc2 = acc2 + weight * chan[2]
                return (trans * fade, acc0, acc1, acc2, total + ext)

            zeros = jnp.zeros((sub, width), jnp.float32)
            init = (jnp.ones((sub, width), jnp.float32), zeros, zeros, zeros, zeros)
            _, acc0, acc1, acc2, total = lax.fori_loop(0, count - 2, step, init, unroll=2)
            color_ref[0, rs, cs] = acc0
            color_ref[1, rs, cs] = acc1
            color_ref[2, rs, cs] = acc2
            depth_ref[rs, cs] = total


def render_block(table, flags, lane_tables, planes, rows, segments):
    stack, tall, lanes = planes.shape
    count = stack - 2
    kernel = lambda *refs: render_kernel(*refs, segments=segments, rows=rows, width=256)
    return pl.pallas_call(
        kernel,
        in_specs=[
            pl.BlockSpec(memory_space=pltpu.SMEM),
            pl.BlockSpec(memory_space=pltpu.SMEM),
            pl.BlockSpec(memory_space=pltpu.VMEM),
            pl.BlockSpec(memory_space=pltpu.VMEM),
        ],
        out_specs=[
            pl.BlockSpec(memory_space=pltpu.VMEM),
            pl.BlockSpec(memory_space=pltpu.VMEM),
        ],
        out_shape=[
            jax.ShapeDtypeStruct((3, rows, lanes), jnp.float32),
            jax.ShapeDtypeStruct((rows, lanes), jnp.float32),
        ],
        scratch_shapes=[pltpu.VMEM((count, rows, lanes), jnp.float32) for _ in range(3)],
        compiler_params=pltpu.CompilerParams(vmem_limit_bytes=48 * 1024 * 1024),
    )(table, flags, lane_tables, planes)


def body(volume, knot_pos, knot_color):
    depth_count = lax.axis_size("depth")
    brick_depth, brick_rows, row_width = volume.shape
    sigma_scale = 4.0 / (brick_depth * depth_count)
    planes = extended_volume(volume)
    d = lax.axis_index("depth")
    t = lax.axis_index("tile")
    flags = jnp.stack([d == 0, d == depth_count - 1, t == 0, t == lax.axis_size("tile") - 1])
    lane_tables, bounds = segment_tables(knot_pos, knot_color, sigma_scale)
    brick_color, optical_depth = render_block(
        bounds, flags.astype(jnp.int32), lane_tables, planes, brick_rows, knot_pos.shape[0] - 1)
    piece = row_width // depth_count
    weighted = jnp.concatenate([brick_color, optical_depth[None]], axis=0)
    weighted = weighted.reshape(4, brick_rows, depth_count, piece).transpose(2, 0, 1, 3)
    blocks = lax.all_to_all(weighted, "depth", 0, 0, tiled=True)
    ahead = jnp.zeros((brick_rows, piece), jnp.float32)
    image = jnp.zeros((3, brick_rows, piece), jnp.float32)
    for b in range(depth_count):
        image = image + blocks[b, :3] * jnp.exp(-ahead)[None]
        ahead = ahead + blocks[b, 3]
    return jnp.concatenate([image, (1.0 - jnp.exp(-ahead))[None]], axis=0)


def solution(mesh):
    in_specs = (P("depth", "tile", None), P(), P())
    out_specs = P(None, "tile", "depth")
    return jax.shard_map(body, mesh=mesh, in_specs=in_specs, out_specs=out_specs, check_vma=False)
```

```python
import jax
import jax.numpy as jnp
from jax import lax
from jax.experimental import pallas as pl
from jax.experimental.pallas import tpu as pltpu
from jax.sharding import PartitionSpec as P


def padded(block, sides, width):
    for axis, dim in sides:
        count = lax.axis_size(axis)
        forward = [(i, i + 1) for i in range(count - 1)]
        backward = [(target, source) for source, target in forward]
        low = lax.ppermute(
            lax.slice_in_dim(block, block.shape[dim] - width, None, axis=dim), axis, forward
        )
        high = lax.ppermute(lax.slice_in_dim(block, 0, width, axis=dim), axis, backward)
        block = jnp.concatenate([low, block, high], axis=dim)
    return block


def shifted(block, axes, moves):
    sizes = [lax.axis_size(a) for a in axes]
    pairs = []
    for index in range(sizes[0] * (sizes[1] if len(sizes) > 1 else 1)):
        coords = [index] if len(sizes) == 1 else [index // sizes[1], index % sizes[1]]
        target = [c + m for c, m in zip(coords, moves)]
        if all(0 <= c < s for c, s in zip(target, sizes)):
            flat = target[0] if len(sizes) == 1 else target[0] * sizes[1] + target[1]
            pairs.append((index, flat))
    return lax.ppermute(block, axes if len(axes) > 1 else axes[0], pairs)


def extended_volume(volume):
    depth, rows, width = volume.shape
    z_low = shifted(volume[depth - 2:], ("depth",), (1,))
    z_high = shifted(volume[:2], ("depth",), (-1,))
    middle = jnp.concatenate([z_low, volume, z_high], axis=0)
    x_low = shifted(middle[:, rows - 2:], ("tile",), (1,))
    x_high = shifted(middle[:, :2], ("tile",), (-1,))
    gap = jnp.zeros((depth + 4, 4, width), volume.dtype)
    return jnp.concatenate([middle, x_high, gap, x_low], axis=1).astype(jnp.float32)


def inside_mask(depth_len, rows):
    d = lax.axis_index("depth")
    t = lax.axis_index("tile")
    z = lax.broadcasted_iota(jnp.int32, (depth_len, rows, 1), 0)
    x = lax.broadcasted_iota(jnp.int32, (depth_len, rows, 1), 1)
    keep = jnp.ones((depth_len, rows, 1), jnp.bool_)
    keep = keep & ~((z == 0) & (d == 0))
    keep = keep & ~((z == depth_len - 1) & (d == lax.axis_size("depth") - 1))
    keep = keep & ~((x == 0) & (t == 0))
    keep = keep & ~((x == rows - 1) & (t == lax.axis_size("tile") - 1))
    return keep


def next_along(center):
    return jnp.pad(center[:, :, 1:], ((0, 0), (0, 0), (0, 1)))


def prior_along(center):
    return jnp.pad(center[:, :, :-1], ((0, 0), (0, 0), (1, 0)))


def smooth_block(extended):
    field = extended.astype(jnp.float32)
    center = field[1:-1, 1:-1]
    neighbours = field[2:, 1:-1] + field[:-2, 1:-1] + field[1:-1, 2:] + field[1:-1, :-2]
    neighbours = neighbours + next_along(center) + prior_along(center)
    return 0.4 * center + 0.1 * neighbours


def shade_lookup(smooth_ext, knot_pos):
    field = smooth_ext.astype(jnp.float32)
    center = field[1:-1, 1:-1]
    slope_z = 0.5 * (field[2:, 1:-1] - field[:-2, 1:-1])
    slope_x = 0.5 * (field[1:-1, 2:] - field[1:-1, :-2])
    slope_y = 0.5 * (next_along(center) - prior_along(center))
    facing = jnp.abs(0.6 * slope_z + 0.8 * slope_x)
    shading = 0.3 + 0.7 * facing / jnp.sqrt(
        slope_z * slope_z + slope_x * slope_x + slope_y * slope_y + 0.1
    )
    knot_float = knot_pos.astype(jnp.float32)
    lookup = jnp.clip(127.5 + 70.0 * center, knot_float[0], knot_float[-1])
    return shading, lookup


def ramp_table(knot_pos, knot_color, sigma_scale):
    knot_float = knot_pos.astype(jnp.float32)
    palette = knot_color.astype(jnp.float32) / 255.0
    palette = palette * jnp.array([1.0, 1.0, 1.0, sigma_scale], jnp.float32)[:, None]
    gaps = knot_float[1:] - knot_float[:-1]
    slopes = (palette[:, 1:] - palette[:, :-1]) / gaps[None]
    count = knot_pos.shape[0]
    pad = lambda v: jnp.pad(v, (0, count - v.shape[0]))
    bounds = jnp.stack([knot_float[0], knot_float[-1]])
    rows = [knot_float, pad(gaps)] + [pad(slopes[c]) for c in range(4)]
    rows += [pad(palette[:, 0]), pad(bounds)]
    return jnp.stack(rows)


def render_kernel(table, flags, planes_ref, color_ref, depth_ref, smooth_ref, square_ref, facing_ref,
                  *, segments, rows, width):
    stack, tall, lanes = planes_ref.shape
    count = stack - 2
    row = lax.broadcasted_iota(jnp.int32, (tall, lanes), 0)
    keep_rows = ((row != tall - 1) | (flags[2] == 0)) & ((row != rows) | (flags[3] == 0))

    def y_prev(a):
        lane = lax.broadcasted_iota(jnp.int32, a.shape, 1)
        return jnp.where(lane == 0, 0.0, pltpu.roll(a, 1, 1))

    def y_next(a):
        lane = lax.broadcasted_iota(jnp.int32, a.shape, 1)
        return jnp.where(lane == lanes - 1, 0.0, pltpu.roll(a, lanes - 1, 1))

    def smooth_plane(i, carry):
        low = planes_ref[i]
        mid = planes_ref[i + 1]
        high = planes_ref[i + 2]
        x_prev = pltpu.roll(mid, 1, 0)
        x_next = pltpu.roll(mid, tall - 1, 0)
        near = low + high + x_next + x_prev
        near = near + y_prev(mid) + y_next(mid)
        smooth = 0.4 * mid + 0.1 * near
        inside = (i > 0) | (flags[0] == 0)
        inside = inside & ((i < count - 1) | (flags[1] == 0))
        smooth = jnp.where(keep_rows & inside, smooth, 0.0)
        smooth = smooth.astype(jnp.bfloat16).astype(jnp.float32)
        center = smooth[:rows]
        slope_x = 0.5 * (pltpu.roll(smooth, tall - 1, 0)[:rows] - pltpu.roll(smooth, 1, 0)[:rows])
        slope_y = 0.5 * (y_next(center) - y_prev(center))
        smooth_ref[i] = center
        square_ref[i] = slope_x * slope_x + slope_y * slope_y
        facing_ref[i] = 0.8 * slope_x
        return carry

    lax.fori_loop(0, count, smooth_plane, 0)

    knots = [table[0, k] for k in range(segments)]
    gaps = [table[1, k] for k in range(segments)]
    slopes = [[table[2 + c, k] for k in range(segments)] for c in range(4)]
    base = [table[6, c] for c in range(4)]
    lo = table[7, 0]
    hi = table[7, 1]
    sub = 8
    for r0 in range(0, rows, sub):
        for c0 in range(0, lanes, width):
            rs = pl.ds(r0, sub)
            cs = pl.ds(c0, width)

            def step(z, carry):
                trans, acc0, acc1, acc2, total = carry
                center = smooth_ref[z + 1, rs, cs]
                slope_z = 0.5 * (smooth_ref[z + 2, rs, cs] - smooth_ref[z, rs, cs])
                facing = jnp.abs(0.6 * slope_z + facing_ref[z + 1, rs, cs])
                norm = slope_z * slope_z + square_ref[z + 1, rs, cs] + 0.1
                shade = 0.3 + 0.7 * facing * lax.rsqrt(norm)
                lookup = jnp.clip(127.5 + 70.0 * center, lo, hi)
                chan = [jnp.full_like(lookup, base[c]) for c in range(4)]
                for k in range(segments):
                    t = jnp.minimum(jnp.maximum(lookup - knots[k], 0.0), gaps[k])
                    chan = [chan[c] + t * slopes[c][k] for c in range(4)]
                ext = chan[3]
                fade = jnp.exp(-ext)
                weight = shade * (1.0 - fade) * trans
                acc0 = acc0 + weight * chan[0]
                acc1 = acc1 + weight * chan[1]
                acc2 = acc2 + weight * chan[2]
                return (trans * fade, acc0, acc1, acc2, total + ext)

            zeros = jnp.zeros((sub, width), jnp.float32)
            init = (jnp.ones((sub, width), jnp.float32), zeros, zeros, zeros, zeros)
            _, acc0, acc1, acc2, total = lax.fori_loop(0, count - 2, step, init, unroll=2)
            color_ref[0, rs, cs] = acc0
            color_ref[1, rs, cs] = acc1
            color_ref[2, rs, cs] = acc2
            depth_ref[rs, cs] = total


def render_block(table, flags, planes, rows, segments):
    stack, tall, lanes = planes.shape
    count = stack - 2
    kernel = lambda *refs: render_kernel(*refs, segments=segments, rows=rows, width=256)
    return pl.pallas_call(
        kernel,
        in_specs=[
            pl.BlockSpec(memory_space=pltpu.SMEM),
            pl.BlockSpec(memory_space=pltpu.SMEM),
            pl.BlockSpec(memory_space=pltpu.VMEM),
        ],
        out_specs=[
            pl.BlockSpec(memory_space=pltpu.VMEM),
            pl.BlockSpec(memory_space=pltpu.VMEM),
        ],
        out_shape=[
            jax.ShapeDtypeStruct((3, rows, lanes), jnp.float32),
            jax.ShapeDtypeStruct((rows, lanes), jnp.float32),
        ],
        scratch_shapes=[pltpu.VMEM((count, rows, lanes), jnp.float32) for _ in range(3)],
        compiler_params=pltpu.CompilerParams(vmem_limit_bytes=48 * 1024 * 1024),
    )(table, flags, planes)


def body(volume, knot_pos, knot_color):
    depth_count = lax.axis_size("depth")
    brick_depth, brick_rows, row_width = volume.shape
    sigma_scale = 4.0 / (brick_depth * depth_count)
    planes = extended_volume(volume)
    d = lax.axis_index("depth")
    t = lax.axis_index("tile")
    flags = jnp.stack([d == 0, d == depth_count - 1, t == 0, t == lax.axis_size("tile") - 1])
    table = ramp_table(knot_pos, knot_color, sigma_scale)
    brick_color, optical_depth = render_block(
        table, flags.astype(jnp.int32), planes, brick_rows, knot_pos.shape[0] - 1)
    piece = row_width // depth_count
    weighted = jnp.concatenate([brick_color, optical_depth[None]], axis=0)
    weighted = weighted.reshape(4, brick_rows, depth_count, piece).transpose(2, 0, 1, 3)
    blocks = lax.all_to_all(weighted, "depth", 0, 0, tiled=True)
    ahead = jnp.zeros((brick_rows, piece), jnp.float32)
    image = jnp.zeros((3, brick_rows, piece), jnp.float32)
    for b in range(depth_count):
        image = image + blocks[b, :3] * jnp.exp(-ahead)[None]
        ahead = ahead + blocks[b, 3]
    return jnp.concatenate([image, (1.0 - jnp.exp(-ahead))[None]], axis=0)


def solution(mesh):
    in_specs = (P("depth", "tile", None), P(), P())
    out_specs = P(None, "tile", "depth")
    return jax.shard_map(body, mesh=mesh, in_specs=in_specs, out_specs=out_specs, check_vma=False)
```

```python
import jax
import jax.numpy as jnp
from jax import lax
from jax.experimental import pallas as pl
from jax.experimental.pallas import tpu as pltpu
from jax.sharding import PartitionSpec as P


def padded(block, sides, width):
    for axis, dim in sides:
        count = lax.axis_size(axis)
        forward = [(i, i + 1) for i in range(count - 1)]
        backward = [(target, source) for source, target in forward]
        low = lax.ppermute(
            lax.slice_in_dim(block, block.shape[dim] - width, None, axis=dim), axis, forward
        )
        high = lax.ppermute(lax.slice_in_dim(block, 0, width, axis=dim), axis, backward)
        block = jnp.concatenate([low, block, high], axis=dim)
    return block


def shifted(block, axes, moves):
    sizes = [lax.axis_size(a) for a in axes]
    pairs = []
    for index in range(sizes[0] * (sizes[1] if len(sizes) > 1 else 1)):
        coords = [index] if len(sizes) == 1 else [index // sizes[1], index % sizes[1]]
        target = [c + m for c, m in zip(coords, moves)]
        if all(0 <= c < s for c, s in zip(target, sizes)):
            flat = target[0] if len(sizes) == 1 else target[0] * sizes[1] + target[1]
            pairs.append((index, flat))
    return lax.ppermute(block, axes if len(axes) > 1 else axes[0], pairs)


def extended_volume(volume):
    depth, rows, width = volume.shape
    z_low = shifted(volume[depth - 2:], ("depth",), (1,))
    z_high = shifted(volume[:2], ("depth",), (-1,))
    edge = lambda a, b: jnp.concatenate([z_low[:, a:b], volume[:, a:b], z_high[:, a:b]], axis=0)
    x_low = shifted(edge(rows - 2, rows), ("tile",), (1,))
    x_high = shifted(edge(0, 2), ("tile",), (-1,))
    middle = jnp.concatenate([z_low, volume, z_high], axis=0)
    gap = jnp.zeros((depth + 4, 4, width), volume.dtype)
    return jnp.concatenate([middle, x_high, gap, x_low], axis=1).astype(jnp.float32)


def inside_mask(depth_len, rows):
    d = lax.axis_index("depth")
    t = lax.axis_index("tile")
    z = lax.broadcasted_iota(jnp.int32, (depth_len, rows, 1), 0)
    x = lax.broadcasted_iota(jnp.int32, (depth_len, rows, 1), 1)
    keep = jnp.ones((depth_len, rows, 1), jnp.bool_)
    keep = keep & ~((z == 0) & (d == 0))
    keep = keep & ~((z == depth_len - 1) & (d == lax.axis_size("depth") - 1))
    keep = keep & ~((x == 0) & (t == 0))
    keep = keep & ~((x == rows - 1) & (t == lax.axis_size("tile") - 1))
    return keep


def next_along(center):
    return jnp.pad(center[:, :, 1:], ((0, 0), (0, 0), (0, 1)))


def prior_along(center):
    return jnp.pad(center[:, :, :-1], ((0, 0), (0, 0), (1, 0)))


def smooth_block(extended):
    field = extended.astype(jnp.float32)
    center = field[1:-1, 1:-1]
    neighbours = field[2:, 1:-1] + field[:-2, 1:-1] + field[1:-1, 2:] + field[1:-1, :-2]
    neighbours = neighbours + next_along(center) + prior_along(center)
    return 0.4 * center + 0.1 * neighbours


def shade_lookup(smooth_ext, knot_pos):
    field = smooth_ext.astype(jnp.float32)
    center = field[1:-1, 1:-1]
    slope_z = 0.5 * (field[2:, 1:-1] - field[:-2, 1:-1])
    slope_x = 0.5 * (field[1:-1, 2:] - field[1:-1, :-2])
    slope_y = 0.5 * (next_along(center) - prior_along(center))
    facing = jnp.abs(0.6 * slope_z + 0.8 * slope_x)
    shading = 0.3 + 0.7 * facing / jnp.sqrt(
        slope_z * slope_z + slope_x * slope_x + slope_y * slope_y + 0.1
    )
    knot_float = knot_pos.astype(jnp.float32)
    lookup = jnp.clip(127.5 + 70.0 * center, knot_float[0], knot_float[-1])
    return shading, lookup


def ramp_table(knot_pos, knot_color, sigma_scale):
    knot_float = knot_pos.astype(jnp.float32)
    palette = knot_color.astype(jnp.float32) / 255.0
    palette = palette * jnp.array([1.0, 1.0, 1.0, sigma_scale], jnp.float32)[:, None]
    gaps = knot_float[1:] - knot_float[:-1]
    slopes = (palette[:, 1:] - palette[:, :-1]) / gaps[None]
    offsets = palette[:, :-1] - slopes * knot_float[None, :-1]
    count = knot_pos.shape[0]
    pad = lambda v: jnp.pad(v, (0, count - v.shape[0]))
    bounds = jnp.stack([knot_float[0], knot_float[-1]])
    rows = [knot_float] + [pad(offsets[c]) for c in range(4)] + [pad(slopes[c]) for c in range(4)]
    rows += [pad(bounds)]
    return jnp.stack(rows)


def render_kernel(table, flags, planes_ref, color_ref, depth_ref, smooth_ref, square_ref, facing_ref,
                  *, segments, rows, width):
    stack, tall, lanes = planes_ref.shape
    count = stack - 2
    row = lax.broadcasted_iota(jnp.int32, (tall, lanes), 0)
    keep_rows = ((row != tall - 1) | (flags[2] == 0)) & ((row != rows) | (flags[3] == 0))

    def y_prev(a):
        lane = lax.broadcasted_iota(jnp.int32, a.shape, 1)
        return jnp.where(lane == 0, 0.0, pltpu.roll(a, 1, 1))

    def y_next(a):
        lane = lax.broadcasted_iota(jnp.int32, a.shape, 1)
        return jnp.where(lane == lanes - 1, 0.0, pltpu.roll(a, lanes - 1, 1))

    def smooth_plane(i, carry):
        low = planes_ref[i]
        mid = planes_ref[i + 1]
        high = planes_ref[i + 2]
        x_prev = pltpu.roll(mid, 1, 0)
        x_next = pltpu.roll(mid, tall - 1, 0)
        near = low + high + x_next + x_prev
        near = near + y_prev(mid) + y_next(mid)
        smooth = 0.4 * mid + 0.1 * near
        inside = (i > 0) | (flags[0] == 0)
        inside = inside & ((i < count - 1) | (flags[1] == 0))
        smooth = jnp.where(keep_rows & inside, smooth, 0.0)
        smooth = smooth.astype(jnp.bfloat16).astype(jnp.float32)
        center = smooth[:rows]
        slope_x = 0.5 * (pltpu.roll(smooth, tall - 1, 0)[:rows] - pltpu.roll(smooth, 1, 0)[:rows])
        slope_y = 0.5 * (y_next(center) - y_prev(center))
        smooth_ref[i] = center
        square_ref[i] = slope_x * slope_x + slope_y * slope_y
        facing_ref[i] = 0.8 * slope_x
        return carry

    lax.fori_loop(0, count, smooth_plane, 0)

    knots = [table[0, k] for k in range(segments)]
    offsets = [[table[1 + c, k] for k in range(segments)] for c in range(4)]
    slopes = [[table[5 + c, k] for k in range(segments)] for c in range(4)]
    lo = table[9, 0]
    hi = table[9, 1]
    sub = 8
    for r0 in range(0, rows, sub):
        for c0 in range(0, lanes, width):
            rs = pl.ds(r0, sub)
            cs = pl.ds(c0, width)

            def step(z, carry):
                trans, acc0, acc1, acc2, total = carry
                center = smooth_ref[z + 1, rs, cs]
                slope_z = 0.5 * (smooth_ref[z + 2, rs, cs] - smooth_ref[z, rs, cs])
                facing = jnp.abs(0.6 * slope_z + facing_ref[z + 1, rs, cs])
                norm = slope_z * slope_z + square_ref[z + 1, rs, cs] + 0.1
                shade = 0.3 + 0.7 * facing * lax.rsqrt(norm)
                lookup = jnp.clip(127.5 + 70.0 * center, lo, hi)
                offset = [jnp.full_like(lookup, offsets[c][0]) for c in range(4)]
                slope = [jnp.full_like(lookup, slopes[c][0]) for c in range(4)]
                for k in range(1, segments):
                    above = lookup >= knots[k]
                    offset = [jnp.where(above, offsets[c][k], offset[c]) for c in range(4)]
                    slope = [jnp.where(above, slopes[c][k], slope[c]) for c in range(4)]
                chan = [offset[c] + slope[c] * lookup for c in range(4)]
                ext = chan[3]
                fade = jnp.exp(-ext)
                weight = shade * (1.0 - fade) * trans
                acc0 = acc0 + weight * chan[0]
                acc1 = acc1 + weight * chan[1]
                acc2 = acc2 + weight * chan[2]
                return (trans * fade, acc0, acc1, acc2, total + ext)

            zeros = jnp.zeros((sub, width), jnp.float32)
            init = (jnp.ones((sub, width), jnp.float32), zeros, zeros, zeros, zeros)
            _, acc0, acc1, acc2, total = lax.fori_loop(0, count - 2, step, init, unroll=2)
            color_ref[0, rs, cs] = acc0
            color_ref[1, rs, cs] = acc1
            color_ref[2, rs, cs] = acc2
            depth_ref[rs, cs] = total


def render_block(table, flags, planes, rows, segments):
    stack, tall, lanes = planes.shape
    count = stack - 2
    kernel = lambda *refs: render_kernel(*refs, segments=segments, rows=rows, width=256)
    return pl.pallas_call(
        kernel,
        in_specs=[
            pl.BlockSpec(memory_space=pltpu.SMEM),
            pl.BlockSpec(memory_space=pltpu.SMEM),
            pl.BlockSpec(memory_space=pltpu.VMEM),
        ],
        out_specs=[
            pl.BlockSpec(memory_space=pltpu.VMEM),
            pl.BlockSpec(memory_space=pltpu.VMEM),
        ],
        out_shape=[
            jax.ShapeDtypeStruct((3, rows, lanes), jnp.float32),
            jax.ShapeDtypeStruct((rows, lanes), jnp.float32),
        ],
        scratch_shapes=[pltpu.VMEM((count, rows, lanes), jnp.float32) for _ in range(3)],
        compiler_params=pltpu.CompilerParams(vmem_limit_bytes=48 * 1024 * 1024),
    )(table, flags, planes)


def body(volume, knot_pos, knot_color):
    depth_count = lax.axis_size("depth")
    brick_depth, brick_rows, row_width = volume.shape
    sigma_scale = 4.0 / (brick_depth * depth_count)
    planes = extended_volume(volume)
    d = lax.axis_index("depth")
    t = lax.axis_index("tile")
    flags = jnp.stack([d == 0, d == depth_count - 1, t == 0, t == lax.axis_size("tile") - 1])
    table = ramp_table(knot_pos, knot_color, sigma_scale)
    brick_color, optical_depth = render_block(
        table, flags.astype(jnp.int32), planes, brick_rows, knot_pos.shape[0] - 1)
    piece = row_width // depth_count
    weighted = jnp.concatenate([brick_color, optical_depth[None]], axis=0)
    weighted = weighted.reshape(4, brick_rows, depth_count, piece).transpose(2, 0, 1, 3)
    blocks = lax.all_to_all(weighted, "depth", 0, 0, tiled=True)
    ahead = jnp.zeros((brick_rows, piece), jnp.float32)
    image = jnp.zeros((3, brick_rows, piece), jnp.float32)
    for b in range(depth_count):
        image = image + blocks[b, :3] * jnp.exp(-ahead)[None]
        ahead = ahead + blocks[b, 3]
    return jnp.concatenate([image, (1.0 - jnp.exp(-ahead))[None]], axis=0)


def solution(mesh):
    in_specs = (P("depth", "tile", None), P(), P())
    out_specs = P(None, "tile", "depth")
    return jax.shard_map(body, mesh=mesh, in_specs=in_specs, out_specs=out_specs, check_vma=False)
```

```python
import jax
import jax.numpy as jnp
from jax import lax
from jax.experimental import pallas as pl
from jax.experimental.pallas import tpu as pltpu
from jax.sharding import PartitionSpec as P

TALL = 24
EDGE = 2


def shifted(block, axis, move):
    size = lax.axis_size(axis)
    pairs = [(i, i + move) for i in range(size) if 0 <= i + move < size]
    return lax.ppermute(block, axis, pairs)


def ramp_table(knot_pos, knot_color, sigma_scale):
    knot_float = knot_pos.astype(jnp.float32)
    palette = knot_color.astype(jnp.float32) / 255.0
    palette = palette * jnp.array([1.0, 1.0, 1.0, sigma_scale], jnp.float32)[:, None]
    gaps = knot_float[1:] - knot_float[:-1]
    slopes = (palette[:, 1:] - palette[:, :-1]) / gaps[None]
    offsets = palette[:, :-1] - slopes * knot_float[None, :-1]
    count = knot_pos.shape[0]
    pad = lambda v: jnp.pad(v, (0, count - v.shape[0]))
    bounds = jnp.stack([knot_float[0], knot_float[-1]])
    rows = [knot_float] + [pad(offsets[c]) for c in range(4)] + [pad(slopes[c]) for c in range(4)]
    rows += [pad(bounds)]
    return jnp.stack(rows)


def y_prev(a):
    lane = lax.broadcasted_iota(jnp.int32, a.shape, 1)
    return jnp.where(lane == 0, 0.0, pltpu.roll(a, 1, 1))


def y_next(a):
    lane = lax.broadcasted_iota(jnp.int32, a.shape, 1)
    return jnp.where(lane == a.shape[1] - 1, 0.0, pltpu.roll(a, a.shape[1] - 1, 1))


def smooth_plane(low, mid, high, keep, rows):
    tall = mid.shape[0]
    near = low + high + pltpu.roll(mid, tall - 1, 0) + pltpu.roll(mid, 1, 0)
    near = near + y_prev(mid) + y_next(mid)
    smooth = jnp.where(keep, 0.4 * mid + 0.1 * near, 0.0)
    smooth = smooth.astype(jnp.bfloat16).astype(jnp.float32)
    center = smooth[:rows]
    slope_x = 0.5 * (pltpu.roll(smooth, tall - 1, 0)[:rows] - pltpu.roll(smooth, 1, 0)[:rows])
    slope_y = 0.5 * (y_next(center) - y_prev(center))
    return center, slope_x * slope_x + slope_y * slope_y, 0.8 * slope_x


class Palette:
    def __init__(self, table, segments):
        self.knots = [table[0, k] for k in range(segments)]
        self.offsets = [[table[1 + c, k] for k in range(segments)] for c in range(4)]
        self.slopes = [[table[5 + c, k] for k in range(segments)] for c in range(4)]
        self.lo = table[9, 0]
        self.hi = table[9, 1]
        self.segments = segments

    def cell(self, before, center, after, square, facing):
        slope_z = 0.5 * (after - before)
        facing = jnp.abs(0.6 * slope_z + facing)
        norm = slope_z * slope_z + square + 0.1
        shade = 0.3 + 0.7 * facing * lax.rsqrt(norm)
        lookup = jnp.clip(127.5 + 70.0 * center, self.lo, self.hi)
        offset = [jnp.full_like(lookup, self.offsets[c][0]) for c in range(4)]
        slope = [jnp.full_like(lookup, self.slopes[c][0]) for c in range(4)]
        for k in range(1, self.segments):
            above = lookup >= self.knots[k]
            offset = [jnp.where(above, self.offsets[c][k], offset[c]) for c in range(4)]
            slope = [jnp.where(above, self.slopes[c][k], slope[c]) for c in range(4)]
        chan = [offset[c] + slope[c] * lookup for c in range(4)]
        return shade, chan


def row_keep(flags, tall, lanes, rows):
    row = lax.broadcasted_iota(jnp.int32, (tall, lanes), 0)
    return ((row != tall - 1) | (flags[2] == 0)) & ((row != rows) | (flags[3] == 0))


def middle_kernel(table, flags, planes_ref, color_ref, depth_ref, trans_ref,
                  smooth_ref, square_ref, facing_ref, *, segments, rows, width):
    depth, tall, lanes = planes_ref.shape
    keep = row_keep(flags, tall, lanes, rows)

    def plane(i, carry):
        center, square, facing = smooth_plane(
            planes_ref[i - 1], planes_ref[i], planes_ref[i + 1], keep, rows)
        smooth_ref[i] = center
        square_ref[i] = square
        facing_ref[i] = facing
        return carry

    lax.fori_loop(1, depth - 1, plane, 0)
    palette = Palette(table, segments)
    sub = 8
    for r0 in range(0, rows, sub):
        for c0 in range(0, lanes, width):
            rs = pl.ds(r0, sub)
            cs = pl.ds(c0, width)

            def step(z, carry):
                trans, acc0, acc1, acc2, total = carry
                shade, chan = palette.cell(
                    smooth_ref[z - 1, rs, cs], smooth_ref[z, rs, cs], smooth_ref[z + 1, rs, cs],
                    square_ref[z, rs, cs], facing_ref[z, rs, cs])
                ext = chan[3]
                fade = jnp.exp(-ext)
                weight = shade * (1.0 - fade) * trans
                acc0 = acc0 + weight * chan[0]
                acc1 = acc1 + weight * chan[1]
                acc2 = acc2 + weight * chan[2]
                return (trans * fade, acc0, acc1, acc2, total + ext)

            zeros = jnp.zeros((sub, width), jnp.float32)
            init = (jnp.ones((sub, width), jnp.float32), zeros, zeros, zeros, zeros)
            trans, acc0, acc1, acc2, total = lax.fori_loop(
                EDGE, depth - EDGE, step, init, unroll=2)
            color_ref[0, rs, cs] = acc0
            color_ref[1, rs, cs] = acc1
            color_ref[2, rs, cs] = acc2
            depth_ref[rs, cs] = total
            trans_ref[rs, cs] = trans


def edge_kernel(table, flags, front_ref, back_ref, color_ref, depth_ref, trans_ref,
                out_color_ref, out_depth_ref, *, segments, rows):
    span, tall, lanes = front_ref.shape
    keep = row_keep(flags, tall, lanes, rows)
    palette = Palette(table, segments)

    def side(ref, outside):
        smoothed = []
        for i in range(1, span - 1):
            inside = keep & ~outside(i)
            smoothed.append(smooth_plane(ref[i - 1], ref[i], ref[i + 1], inside, rows))
        cells = []
        for j in range(1, len(smoothed) - 1):
            cells.append(palette.cell(smoothed[j - 1][0], smoothed[j][0], smoothed[j + 1][0],
                                      smoothed[j][1], smoothed[j][2]))
        return cells

    front = side(front_ref, lambda i: (i == 1) & (flags[0] == 1))
    back = side(back_ref, lambda i: (i == span - 2) & (flags[1] == 1))
    mid_color = [color_ref[c] for c in range(3)]
    mid_depth = depth_ref[...]
    mid_trans = trans_ref[...]
    color = [jnp.zeros((rows, lanes), jnp.float32) for c in range(3)]
    total = jnp.zeros((rows, lanes), jnp.float32)
    trans = jnp.ones((rows, lanes), jnp.float32)

    def add_cells(cells, color, total, trans):
        for shade, chan in cells:
            fade = jnp.exp(-chan[3])
            weight = shade * (1.0 - fade) * trans
            color = [color[c] + weight * chan[c] for c in range(3)]
            total = total + chan[3]
            trans = trans * fade
        return color, total, trans

    color, total, trans = add_cells(front, color, total, trans)
    color = [color[c] + trans * mid_color[c] for c in range(3)]
    total = total + mid_depth
    trans = trans * mid_trans
    color, total, trans = add_cells(back, color, total, trans)
    for c in range(3):
        out_color_ref[c] = color[c]
    out_depth_ref[...] = total


def render_block(table, flags, planes, front, back, rows, segments):
    depth, tall, lanes = planes.shape
    smem = pl.BlockSpec(memory_space=pltpu.SMEM)
    vmem = pl.BlockSpec(memory_space=pltpu.VMEM)
    color_shape = jax.ShapeDtypeStruct((3, rows, lanes), jnp.float32)
    plane_shape = jax.ShapeDtypeStruct((rows, lanes), jnp.float32)
    middle = pl.pallas_call(
        lambda *refs: middle_kernel(*refs, segments=segments, rows=rows, width=256),
        in_specs=[smem, smem, vmem],
        out_specs=[vmem, vmem, vmem],
        out_shape=[color_shape, plane_shape, plane_shape],
        scratch_shapes=[pltpu.VMEM((depth, rows, lanes), jnp.float32) for _ in range(3)],
        compiler_params=pltpu.CompilerParams(vmem_limit_bytes=48 * 1024 * 1024),
    )(table, flags, planes)
    return pl.pallas_call(
        lambda *refs: edge_kernel(*refs, segments=segments, rows=rows),
        in_specs=[smem, smem] + [vmem] * 5,
        out_specs=[vmem, vmem],
        out_shape=[color_shape, plane_shape],
        compiler_params=pltpu.CompilerParams(vmem_limit_bytes=48 * 1024 * 1024),
    )(table, flags, front, back, *middle)


def body(volume, knot_pos, knot_color):
    depth_count = lax.axis_size("depth")
    depth, rows, width = volume.shape
    sigma_scale = 4.0 / (depth * depth_count)
    x_low = shifted(volume[:, rows - 2:], "tile", 1)
    x_high = shifted(volume[:, :2], "tile", -1)
    gap = jnp.zeros((depth, TALL - rows - 4, width), volume.dtype)
    planes = jnp.concatenate([volume, x_high, gap, x_low], axis=1).astype(jnp.float32)
    z_low = shifted(planes[depth - 2:], "depth", 1)
    z_high = shifted(planes[:2], "depth", -1)
    front = jnp.concatenate([z_low, planes[:EDGE + 2]], axis=0)
    back = jnp.concatenate([planes[depth - EDGE - 2:], z_high], axis=0)
    d = lax.axis_index("depth")
    t = lax.axis_index("tile")
    flags = jnp.stack([d == 0, d == depth_count - 1, t == 0, t == lax.axis_size("tile") - 1])
    table = ramp_table(knot_pos, knot_color, sigma_scale)
    brick_color, optical_depth = render_block(
        table, flags.astype(jnp.int32), planes, front, back, rows, knot_pos.shape[0] - 1)
    piece = width // depth_count
    weighted = jnp.concatenate([brick_color, optical_depth[None]], axis=0)
    weighted = weighted.reshape(4, rows, depth_count, piece).transpose(2, 0, 1, 3)
    blocks = lax.all_to_all(weighted, "depth", 0, 0, tiled=True)
    ahead = jnp.zeros((rows, piece), jnp.float32)
    image = jnp.zeros((3, rows, piece), jnp.float32)
    for b in range(depth_count):
        image = image + blocks[b, :3] * jnp.exp(-ahead)[None]
        ahead = ahead + blocks[b, 3]
    return jnp.concatenate([image, (1.0 - jnp.exp(-ahead))[None]], axis=0)


def solution(mesh):
    in_specs = (P("depth", "tile", None), P(), P())
    out_specs = P(None, "tile", "depth")
    return jax.shard_map(body, mesh=mesh, in_specs=in_specs, out_specs=out_specs, check_vma=False)
```

```python
import jax
import jax.numpy as jnp
from jax import lax
from jax.experimental import pallas as pl
from jax.experimental.pallas import tpu as pltpu
from jax.sharding import PartitionSpec as P

TALL = 24
EDGE = 2


def shifted(block, axis, move):
    size = lax.axis_size(axis)
    pairs = [(i, i + move) for i in range(size) if 0 <= i + move < size]
    return lax.ppermute(block, axis, pairs)


def ramp_table(knot_pos, knot_color, sigma_scale):
    knot_float = knot_pos.astype(jnp.float32)
    palette = knot_color.astype(jnp.float32) / 255.0
    palette = palette * jnp.array([1.0, 1.0, 1.0, sigma_scale], jnp.float32)[:, None]
    gaps = knot_float[1:] - knot_float[:-1]
    slopes = (palette[:, 1:] - palette[:, :-1]) / gaps[None]
    offsets = palette[:, :-1] - slopes * knot_float[None, :-1]
    count = knot_pos.shape[0]
    pad = lambda v: jnp.pad(v, (0, count - v.shape[0]))
    bounds = jnp.stack([knot_float[0], knot_float[-1]])
    rows = [knot_float] + [pad(offsets[c]) for c in range(4)] + [pad(slopes[c]) for c in range(4)]
    rows += [pad(bounds)]
    return jnp.stack(rows)


def y_prev(a):
    lane = lax.broadcasted_iota(jnp.int32, a.shape, 1)
    return jnp.where(lane == 0, 0.0, pltpu.roll(a, 1, 1))


def y_next(a):
    lane = lax.broadcasted_iota(jnp.int32, a.shape, 1)
    return jnp.where(lane == a.shape[1] - 1, 0.0, pltpu.roll(a, a.shape[1] - 1, 1))


def smooth_plane(low, mid, high, keep, rows):
    tall = mid.shape[0]
    near = low + high + pltpu.roll(mid, tall - 1, 0) + pltpu.roll(mid, 1, 0)
    near = near + y_prev(mid) + y_next(mid)
    smooth = jnp.where(keep, 0.4 * mid + 0.1 * near, 0.0)
    smooth = smooth.astype(jnp.bfloat16).astype(jnp.float32)
    center = smooth[:rows]
    slope_x = 0.5 * (pltpu.roll(smooth, tall - 1, 0)[:rows] - pltpu.roll(smooth, 1, 0)[:rows])
    slope_y = 0.5 * (y_next(center) - y_prev(center))
    return center, slope_x * slope_x + slope_y * slope_y, 0.8 * slope_x


class Palette:
    def __init__(self, table, segments):
        self.knots = [table[0, k] for k in range(segments)]
        self.offsets = [[table[1 + c, k] for k in range(segments)] for c in range(4)]
        self.slopes = [[table[5 + c, k] for k in range(segments)] for c in range(4)]
        self.lo = table[9, 0]
        self.hi = table[9, 1]
        self.segments = segments

    def cell(self, before, center, after, square, facing):
        slope_z = 0.5 * (after - before)
        facing = jnp.abs(0.6 * slope_z + facing)
        norm = slope_z * slope_z + square + 0.1
        shade = 0.3 + 0.7 * facing * lax.rsqrt(norm)
        lookup = jnp.clip(127.5 + 70.0 * center, self.lo, self.hi)
        offset = [jnp.full_like(lookup, self.offsets[c][0]) for c in range(4)]
        slope = [jnp.full_like(lookup, self.slopes[c][0]) for c in range(4)]
        for k in range(1, self.segments):
            above = lookup >= self.knots[k]
            offset = [jnp.where(above, self.offsets[c][k], offset[c]) for c in range(4)]
            slope = [jnp.where(above, self.slopes[c][k], slope[c]) for c in range(4)]
        chan = [offset[c] + slope[c] * lookup for c in range(4)]
        return shade, chan


def row_keep(flags, tall, lanes, rows):
    row = lax.broadcasted_iota(jnp.int32, (tall, lanes), 0)
    return ((row != tall - 1) | (flags[2] == 0)) & ((row != rows) | (flags[3] == 0))


def middle_kernel(table, flags, volume_ref, side_ref, color_ref, depth_ref, trans_ref,
                  smooth_ref, square_ref, facing_ref, *, segments, rows, width):
    depth, _, lanes = volume_ref.shape
    tall = rows + side_ref.shape[1]
    keep = row_keep(flags, tall, lanes, rows)

    def joined(i):
        return jnp.concatenate([volume_ref[i].astype(jnp.float32), side_ref[i]], axis=0)

    def plane(i, carry):
        center, square, facing = smooth_plane(joined(i - 1), joined(i), joined(i + 1), keep, rows)
        smooth_ref[i] = center
        square_ref[i] = square
        facing_ref[i] = facing
        return carry

    lax.fori_loop(1, depth - 1, plane, 0)
    palette = Palette(table, segments)
    sub = 8
    for r0 in range(0, rows, sub):
        for c0 in range(0, lanes, width):
            rs = pl.ds(r0, sub)
            cs = pl.ds(c0, width)

            def step(z, carry):
                trans, acc0, acc1, acc2, total = carry
                shade, chan = palette.cell(
                    smooth_ref[z - 1, rs, cs], smooth_ref[z, rs, cs], smooth_ref[z + 1, rs, cs],
                    square_ref[z, rs, cs], facing_ref[z, rs, cs])
                ext = chan[3]
                fade = jnp.exp(-ext)
                weight = shade * (1.0 - fade) * trans
                acc0 = acc0 + weight * chan[0]
                acc1 = acc1 + weight * chan[1]
                acc2 = acc2 + weight * chan[2]
                return (trans * fade, acc0, acc1, acc2, total + ext)

            zeros = jnp.zeros((sub, width), jnp.float32)
            init = (jnp.ones((sub, width), jnp.float32), zeros, zeros, zeros, zeros)
            trans, acc0, acc1, acc2, total = lax.fori_loop(
                EDGE, depth - EDGE, step, init, unroll=2)
            color_ref[0, rs, cs] = acc0
            color_ref[1, rs, cs] = acc1
            color_ref[2, rs, cs] = acc2
            depth_ref[rs, cs] = total
            trans_ref[rs, cs] = trans


def edge_kernel(table, flags, front_ref, back_ref, color_ref, depth_ref, trans_ref,
                out_color_ref, out_depth_ref, *, segments, rows):
    span, tall, lanes = front_ref.shape
    keep = row_keep(flags, tall, lanes, rows)
    palette = Palette(table, segments)

    def side(ref, outside):
        smoothed = []
        for i in range(1, span - 1):
            inside = keep & ~outside(i)
            smoothed.append(smooth_plane(ref[i - 1], ref[i], ref[i + 1], inside, rows))
        cells = []
        for j in range(1, len(smoothed) - 1):
            cells.append(palette.cell(smoothed[j - 1][0], smoothed[j][0], smoothed[j + 1][0],
                                      smoothed[j][1], smoothed[j][2]))
        return cells

    front = side(front_ref, lambda i: (i == 1) & (flags[0] == 1))
    back = side(back_ref, lambda i: (i == span - 2) & (flags[1] == 1))
    mid_color = [color_ref[c] for c in range(3)]
    mid_depth = depth_ref[...]
    mid_trans = trans_ref[...]
    color = [jnp.zeros((rows, lanes), jnp.float32) for c in range(3)]
    total = jnp.zeros((rows, lanes), jnp.float32)
    trans = jnp.ones((rows, lanes), jnp.float32)

    def add_cells(cells, color, total, trans):
        for shade, chan in cells:
            fade = jnp.exp(-chan[3])
            weight = shade * (1.0 - fade) * trans
            color = [color[c] + weight * chan[c] for c in range(3)]
            total = total + chan[3]
            trans = trans * fade
        return color, total, trans

    color, total, trans = add_cells(front, color, total, trans)
    color = [color[c] + trans * mid_color[c] for c in range(3)]
    total = total + mid_depth
    trans = trans * mid_trans
    color, total, trans = add_cells(back, color, total, trans)
    for c in range(3):
        out_color_ref[c] = color[c]
    out_depth_ref[...] = total


def render_block(table, flags, volume, side, front, back, rows, segments):
    depth, _, lanes = volume.shape
    smem = pl.BlockSpec(memory_space=pltpu.SMEM)
    vmem = pl.BlockSpec(memory_space=pltpu.VMEM)
    color_shape = jax.ShapeDtypeStruct((3, rows, lanes), jnp.float32)
    plane_shape = jax.ShapeDtypeStruct((rows, lanes), jnp.float32)
    middle = pl.pallas_call(
        lambda *refs: middle_kernel(*refs, segments=segments, rows=rows, width=256),
        in_specs=[smem, smem, vmem, vmem],
        out_specs=[vmem, vmem, vmem],
        out_shape=[color_shape, plane_shape, plane_shape],
        scratch_shapes=[pltpu.VMEM((depth, rows, lanes), jnp.float32) for _ in range(3)],
        compiler_params=pltpu.CompilerParams(vmem_limit_bytes=48 * 1024 * 1024),
    )(table, flags, volume, side)
    return pl.pallas_call(
        lambda *refs: edge_kernel(*refs, segments=segments, rows=rows),
        in_specs=[smem, smem] + [vmem] * 5,
        out_specs=[vmem, vmem],
        out_shape=[color_shape, plane_shape],
        compiler_params=pltpu.CompilerParams(vmem_limit_bytes=48 * 1024 * 1024),
    )(table, flags, front, back, *middle)


def body(volume, knot_pos, knot_color):
    depth_count = lax.axis_size("depth")
    depth, rows, width = volume.shape
    sigma_scale = 4.0 / (depth * depth_count)
    x_low = shifted(volume[:, rows - 2:], "tile", 1)
    x_high = shifted(volume[:, :2], "tile", -1)
    gap = jnp.zeros((depth, TALL - rows - 4, width), volume.dtype)
    side = jnp.concatenate([x_high, gap, x_low], axis=1).astype(jnp.float32)
    planes = lambda a, b: jnp.concatenate([volume[a:b].astype(jnp.float32), side[a:b]], axis=1)
    z_low = shifted(planes(depth - 2, depth), "depth", 1)
    z_high = shifted(planes(0, 2), "depth", -1)
    front = jnp.concatenate([z_low, planes(0, EDGE + 2)], axis=0)
    back = jnp.concatenate([planes(depth - EDGE - 2, depth), z_high], axis=0)
    d = lax.axis_index("depth")
    t = lax.axis_index("tile")
    flags = jnp.stack([d == 0, d == depth_count - 1, t == 0, t == lax.axis_size("tile") - 1])
    table = ramp_table(knot_pos, knot_color, sigma_scale)
    brick_color, optical_depth = render_block(
        table, flags.astype(jnp.int32), volume, side, front, back, rows, knot_pos.shape[0] - 1)
    piece = width // depth_count
    weighted = jnp.concatenate([brick_color, optical_depth[None]], axis=0)
    weighted = weighted.reshape(4, rows, depth_count, piece).transpose(2, 0, 1, 3)
    blocks = lax.all_to_all(weighted, "depth", 0, 0, tiled=True)
    ahead = jnp.zeros((rows, piece), jnp.float32)
    image = jnp.zeros((3, rows, piece), jnp.float32)
    for b in range(depth_count):
        image = image + blocks[b, :3] * jnp.exp(-ahead)[None]
        ahead = ahead + blocks[b, 3]
    return jnp.concatenate([image, (1.0 - jnp.exp(-ahead))[None]], axis=0)


def solution(mesh):
    in_specs = (P("depth", "tile", None), P(), P())
    out_specs = P(None, "tile", "depth")
    return jax.shard_map(body, mesh=mesh, in_specs=in_specs, out_specs=out_specs, check_vma=False)
```

```python
import jax
import jax.numpy as jnp
from jax import lax
from jax.experimental import pallas as pl
from jax.experimental.pallas import tpu as pltpu
from jax.sharding import PartitionSpec as P

TALL = 24
EDGE = 2


def shifted(block, axis, move):
    size = lax.axis_size(axis)
    pairs = [(i, i + move) for i in range(size) if 0 <= i + move < size]
    return lax.ppermute(block, axis, pairs)


def ramp_table(knot_pos, knot_color, sigma_scale):
    knot_float = knot_pos.astype(jnp.float32)
    palette = knot_color.astype(jnp.float32) / 255.0
    palette = palette * jnp.array([1.0, 1.0, 1.0, sigma_scale], jnp.float32)[:, None]
    gaps = knot_float[1:] - knot_float[:-1]
    slopes = (palette[:, 1:] - palette[:, :-1]) / gaps[None]
    offsets = palette[:, :-1] - slopes * knot_float[None, :-1]
    count = knot_pos.shape[0]
    pad = lambda v: jnp.pad(v, (0, count - v.shape[0]))
    bounds = jnp.stack([knot_float[0], knot_float[-1]])
    rows = [knot_float] + [pad(offsets[c]) for c in range(4)] + [pad(slopes[c]) for c in range(4)]
    rows += [pad(bounds)]
    return jnp.stack(rows)


def y_prev(a):
    rolled = pltpu.roll(a, 1, 1)
    lane = lax.broadcasted_iota(jnp.int32, (a.shape[0], 128), 1)
    first = jnp.where(lane == 0, 0.0, rolled[:, :128])
    return jnp.concatenate([first, rolled[:, 128:]], axis=1)


def y_next(a):
    rolled = pltpu.roll(a, a.shape[1] - 1, 1)
    lane = lax.broadcasted_iota(jnp.int32, (a.shape[0], 128), 1)
    last = jnp.where(lane == 127, 0.0, rolled[:, -128:])
    return jnp.concatenate([rolled[:, :-128], last], axis=1)


def smooth_plane(low, mid, high, keep, rows):
    tall = mid.shape[0]
    near = low + high + pltpu.roll(mid, tall - 1, 0) + pltpu.roll(mid, 1, 0)
    near = near + y_prev(mid) + y_next(mid)
    smooth = 0.4 * mid + 0.1 * near
    if keep.shape[0] == tall:
        smooth = jnp.where(keep, smooth, 0.0)
    else:
        smooth = jnp.concatenate([smooth[:rows], jnp.where(keep, smooth[rows:], 0.0)], axis=0)
    smooth = smooth.astype(jnp.bfloat16).astype(jnp.float32)
    center = smooth[:rows]
    slope_x = 0.5 * (pltpu.roll(smooth, tall - 1, 0)[:rows] - pltpu.roll(smooth, 1, 0)[:rows])
    slope_y = 0.5 * (y_next(center) - y_prev(center))
    return center, slope_x * slope_x + slope_y * slope_y, 0.8 * slope_x


class Palette:
    def __init__(self, table, segments):
        self.knots = [table[0, k] for k in range(segments)]
        self.offsets = [[table[1 + c, k] for k in range(segments)] for c in range(4)]
        self.slopes = [[table[5 + c, k] for k in range(segments)] for c in range(4)]
        self.lo = table[9, 0]
        self.hi = table[9, 1]
        self.segments = segments

    def cell(self, before, center, after, square, facing):
        slope_z = 0.5 * (after - before)
        facing = jnp.abs(0.6 * slope_z + facing)
        norm = slope_z * slope_z + square + 0.1
        shade = 0.3 + 0.7 * facing * lax.rsqrt(norm)
        lookup = jnp.clip(127.5 + 70.0 * center, self.lo, self.hi)
        offset = [jnp.full_like(lookup, self.offsets[c][0]) for c in range(4)]
        slope = [jnp.full_like(lookup, self.slopes[c][0]) for c in range(4)]
        for k in range(1, self.segments):
            above = lookup >= self.knots[k]
            offset = [jnp.where(above, self.offsets[c][k], offset[c]) for c in range(4)]
            slope = [jnp.where(above, self.slopes[c][k], slope[c]) for c in range(4)]
        chan = [offset[c] + slope[c] * lookup for c in range(4)]
        return shade, chan


def row_keep(flags, tall, lanes, rows):
    row = lax.broadcasted_iota(jnp.int32, (tall, lanes), 0)
    return ((row != tall - 1) | (flags[2] == 0)) & ((row != rows) | (flags[3] == 0))


def middle_kernel(table, flags, volume_ref, side_ref, color_ref, depth_ref, trans_ref,
                  smooth_ref, square_ref, facing_ref, *, segments, rows, width):
    depth, _, lanes = volume_ref.shape
    tall = rows + side_ref.shape[1]
    keep = row_keep(flags, tall, lanes, rows)[rows:]

    def joined(i):
        return jnp.concatenate([volume_ref[i].astype(jnp.float32), side_ref[i]], axis=0)

    def plane(i, carry):
        center, square, facing = smooth_plane(joined(i - 1), joined(i), joined(i + 1), keep, rows)
        smooth_ref[i] = center
        square_ref[i] = square
        facing_ref[i] = facing
        return carry

    lax.fori_loop(1, depth - 1, plane, 0, unroll=2)
    palette = Palette(table, segments)
    sub = 8
    for r0 in range(0, rows, sub):
        for c0 in range(0, lanes, width):
            rs = pl.ds(r0, sub)
            cs = pl.ds(c0, width)

            def step(z, carry):
                trans, acc0, acc1, acc2, total = carry
                shade, chan = palette.cell(
                    smooth_ref[z - 1, rs, cs], smooth_ref[z, rs, cs], smooth_ref[z + 1, rs, cs],
                    square_ref[z, rs, cs], facing_ref[z, rs, cs])
                ext = chan[3]
                fade = jnp.exp(-ext)
                weight = shade * (1.0 - fade) * trans
                acc0 = acc0 + weight * chan[0]
                acc1 = acc1 + weight * chan[1]
                acc2 = acc2 + weight * chan[2]
                return (trans * fade, acc0, acc1, acc2, total + ext)

            zeros = jnp.zeros((sub, width), jnp.float32)
            init = (jnp.ones((sub, width), jnp.float32), zeros, zeros, zeros, zeros)
            trans, acc0, acc1, acc2, total = lax.fori_loop(
                EDGE, depth - EDGE, step, init, unroll=2)
            color_ref[0, rs, cs] = acc0
            color_ref[1, rs, cs] = acc1
            color_ref[2, rs, cs] = acc2
            depth_ref[rs, cs] = total
            trans_ref[rs, cs] = trans


def edge_kernel(table, flags, front_ref, back_ref, color_ref, depth_ref, trans_ref,
                out_color_ref, out_depth_ref, *, segments, rows):
    span, tall, lanes = front_ref.shape
    keep = row_keep(flags, tall, lanes, rows)
    palette = Palette(table, segments)

    def side(ref, outside):
        smoothed = []
        for i in range(1, span - 1):
            inside = keep & ~outside(i)
            smoothed.append(smooth_plane(ref[i - 1], ref[i], ref[i + 1], inside, rows))
        cells = []
        for j in range(1, len(smoothed) - 1):
            cells.append(palette.cell(smoothed[j - 1][0], smoothed[j][0], smoothed[j + 1][0],
                                      smoothed[j][1], smoothed[j][2]))
        return cells

    front = side(front_ref, lambda i: (i == 1) & (flags[0] == 1))
    back = side(back_ref, lambda i: (i == span - 2) & (flags[1] == 1))
    mid_color = [color_ref[c] for c in range(3)]
    mid_depth = depth_ref[...]
    mid_trans = trans_ref[...]
    color = [jnp.zeros((rows, lanes), jnp.float32) for c in range(3)]
    total = jnp.zeros((rows, lanes), jnp.float32)
    trans = jnp.ones((rows, lanes), jnp.float32)

    def add_cells(cells, color, total, trans):
        for shade, chan in cells:
            fade = jnp.exp(-chan[3])
            weight = shade * (1.0 - fade) * trans
            color = [color[c] + weight * chan[c] for c in range(3)]
            total = total + chan[3]
            trans = trans * fade
        return color, total, trans

    color, total, trans = add_cells(front, color, total, trans)
    color = [color[c] + trans * mid_color[c] for c in range(3)]
    total = total + mid_depth
    trans = trans * mid_trans
    color, total, trans = add_cells(back, color, total, trans)
    for c in range(3):
        out_color_ref[c] = color[c]
    out_depth_ref[...] = total


def render_block(table, flags, volume, side, front, back, rows, segments):
    depth, _, lanes = volume.shape
    smem = pl.BlockSpec(memory_space=pltpu.SMEM)
    vmem = pl.BlockSpec(memory_space=pltpu.VMEM)
    color_shape = jax.ShapeDtypeStruct((3, rows, lanes), jnp.float32)
    plane_shape = jax.ShapeDtypeStruct((rows, lanes), jnp.float32)
    middle = pl.pallas_call(
        lambda *refs: middle_kernel(*refs, segments=segments, rows=rows, width=256),
        in_specs=[smem, smem, vmem, vmem],
        out_specs=[vmem, vmem, vmem],
        out_shape=[color_shape, plane_shape, plane_shape],
        scratch_shapes=[pltpu.VMEM((depth, rows, lanes), jnp.float32) for _ in range(3)],
        compiler_params=pltpu.CompilerParams(vmem_limit_bytes=48 * 1024 * 1024),
    )(table, flags, volume, side)
    return pl.pallas_call(
        lambda *refs: edge_kernel(*refs, segments=segments, rows=rows),
        in_specs=[smem, smem] + [vmem] * 5,
        out_specs=[vmem, vmem],
        out_shape=[color_shape, plane_shape],
        compiler_params=pltpu.CompilerParams(vmem_limit_bytes=48 * 1024 * 1024),
    )(table, flags, front, back, *middle)


def body(volume, knot_pos, knot_color):
    depth_count = lax.axis_size("depth")
    depth, rows, width = volume.shape
    sigma_scale = 4.0 / (depth * depth_count)
    x_low = shifted(volume[:, rows - 2:], "tile", 1)
    x_high = shifted(volume[:, :2], "tile", -1)
    gap = jnp.zeros((depth, TALL - rows - 4, width), volume.dtype)
    side = jnp.concatenate([x_high, gap, x_low], axis=1).astype(jnp.float32)
    planes = lambda a, b: jnp.concatenate([volume[a:b].astype(jnp.float32), side[a:b]], axis=1)
    z_low = shifted(planes(depth - 2, depth), "depth", 1)
    z_high = shifted(planes(0, 2), "depth", -1)
    front = jnp.concatenate([z_low, planes(0, EDGE + 2)], axis=0)
    back = jnp.concatenate([planes(depth - EDGE - 2, depth), z_high], axis=0)
    d = lax.axis_index("depth")
    t = lax.axis_index("tile")
    flags = jnp.stack([d == 0, d == depth_count - 1, t == 0, t == lax.axis_size("tile") - 1])
    table = ramp_table(knot_pos, knot_color, sigma_scale)
    brick_color, optical_depth = render_block(
        table, flags.astype(jnp.int32), volume, side, front, back, rows, knot_pos.shape[0] - 1)
    piece = width // depth_count
    weighted = jnp.concatenate([brick_color, optical_depth[None]], axis=0)
    weighted = weighted.reshape(4, rows, depth_count, piece).transpose(2, 0, 1, 3)
    blocks = lax.all_to_all(weighted, "depth", 0, 0, tiled=True)
    ahead = jnp.zeros((rows, piece), jnp.float32)
    image = jnp.zeros((3, rows, piece), jnp.float32)
    for b in range(depth_count):
        image = image + blocks[b, :3] * jnp.exp(-ahead)[None]
        ahead = ahead + blocks[b, 3]
    return jnp.concatenate([image, (1.0 - jnp.exp(-ahead))[None]], axis=0)


def solution(mesh):
    in_specs = (P("depth", "tile", None), P(), P())
    out_specs = P(None, "tile", "depth")
    return jax.shard_map(body, mesh=mesh, in_specs=in_specs, out_specs=out_specs, check_vma=False)
```

```python
import jax
import jax.numpy as jnp
from jax import lax
from jax.experimental import pallas as pl
from jax.experimental.pallas import tpu as pltpu
from jax.sharding import PartitionSpec as P

TALL = 24
EDGE = 2


def shifted(block, axis, move):
    size = lax.axis_size(axis)
    pairs = [(i, i + move) for i in range(size) if 0 <= i + move < size]
    return lax.ppermute(block, axis, pairs)


def ramp_table(knot_pos, knot_color, sigma_scale):
    knot_float = knot_pos.astype(jnp.float32)
    palette = knot_color.astype(jnp.float32) / 255.0
    palette = palette * jnp.array([1.0, 1.0, 1.0, sigma_scale], jnp.float32)[:, None]
    gaps = knot_float[1:] - knot_float[:-1]
    slopes = (palette[:, 1:] - palette[:, :-1]) / gaps[None]
    offsets = palette[:, :-1] - slopes * knot_float[None, :-1]
    count = knot_pos.shape[0]
    pad = lambda v: jnp.pad(v, (0, count - v.shape[0]))
    bounds = jnp.stack([knot_float[0], knot_float[-1]])
    rows = [knot_float] + [pad(offsets[c]) for c in range(4)] + [pad(slopes[c]) for c in range(4)]
    rows += [pad(bounds)]
    return jnp.stack(rows)


def y_prev(a):
    rolled = pltpu.roll(a, 1, 1)
    lane = lax.broadcasted_iota(jnp.int32, (a.shape[0], 128), 1)
    first = jnp.where(lane == 0, 0.0, rolled[:, :128])
    return jnp.concatenate([first, rolled[:, 128:]], axis=1)


def y_next(a):
    rolled = pltpu.roll(a, a.shape[1] - 1, 1)
    lane = lax.broadcasted_iota(jnp.int32, (a.shape[0], 128), 1)
    last = jnp.where(lane == 127, 0.0, rolled[:, -128:])
    return jnp.concatenate([rolled[:, :-128], last], axis=1)


def smooth_plane(low, mid, high, keep, rows):
    tall = mid.shape[0]
    near = low + high + pltpu.roll(mid, tall - 1, 0) + pltpu.roll(mid, 1, 0)
    near = near + y_prev(mid) + y_next(mid)
    smooth = 0.4 * mid + 0.1 * near
    if keep.shape[0] == tall:
        smooth = jnp.where(keep, smooth, 0.0)
    else:
        smooth = jnp.concatenate([smooth[:rows], jnp.where(keep, smooth[rows:], 0.0)], axis=0)
    smooth = smooth.astype(jnp.bfloat16).astype(jnp.float32)
    center = smooth[:rows]
    slope_x = 0.5 * (pltpu.roll(smooth, tall - 1, 0)[:rows] - pltpu.roll(smooth, 1, 0)[:rows])
    slope_y = 0.5 * (y_next(center) - y_prev(center))
    return center, slope_x * slope_x + slope_y * slope_y, 0.8 * slope_x


class Palette:
    def __init__(self, table, segments):
        self.knots = [table[0, k] for k in range(segments)]
        self.offsets = [[table[1 + c, k] for k in range(segments)] for c in range(4)]
        self.slopes = [[table[5 + c, k] for k in range(segments)] for c in range(4)]
        self.lo = table[9, 0]
        self.hi = table[9, 1]
        self.segments = segments

    def cell(self, before, center, after, square, facing):
        slope_z = 0.5 * (after - before)
        facing = jnp.abs(0.6 * slope_z + facing)
        norm = slope_z * slope_z + square + 0.1
        shade = 0.3 + 0.7 * facing * lax.rsqrt(norm)
        lookup = jnp.clip(127.5 + 70.0 * center, self.lo, self.hi)
        offset = [jnp.full_like(lookup, self.offsets[c][0]) for c in range(4)]
        slope = [jnp.full_like(lookup, self.slopes[c][0]) for c in range(4)]
        for k in range(1, self.segments):
            above = lookup >= self.knots[k]
            offset = [jnp.where(above, self.offsets[c][k], offset[c]) for c in range(4)]
            slope = [jnp.where(above, self.slopes[c][k], slope[c]) for c in range(4)]
        chan = [offset[c] + slope[c] * lookup for c in range(4)]
        return shade, chan


def row_keep(flags, tall, lanes, rows):
    row = lax.broadcasted_iota(jnp.int32, (tall, lanes), 0)
    return ((row != tall - 1) | (flags[2] == 0)) & ((row != rows) | (flags[3] == 0))


def middle_kernel(table, flags, volume_ref, side_ref, color_ref, depth_ref, trans_ref,
                  smooth_ref, square_ref, facing_ref, *, segments, rows, width):
    depth, _, lanes = volume_ref.shape
    tall = rows + side_ref.shape[1]
    keep = row_keep(flags, tall, lanes, rows)[rows:]

    def joined(i):
        return jnp.concatenate([volume_ref[i].astype(jnp.float32), side_ref[i]], axis=0)

    def plane(i, carry):
        center, square, facing = smooth_plane(joined(i - 1), joined(i), joined(i + 1), keep, rows)
        smooth_ref[i] = center
        square_ref[i] = square
        facing_ref[i] = facing
        return carry

    lax.fori_loop(1, depth - 1, plane, 0, unroll=2)
    palette = Palette(table, segments)
    sub = 8
    for r0 in range(0, rows, sub):
        for c0 in range(0, lanes, width):
            rs = pl.ds(r0, sub)
            cs = pl.ds(c0, width)

            def step(z, carry):
                trans, acc0, acc1, acc2, total = carry
                shade, chan = palette.cell(
                    smooth_ref[z - 1, rs, cs], smooth_ref[z, rs, cs], smooth_ref[z + 1, rs, cs],
                    square_ref[z, rs, cs], facing_ref[z, rs, cs])
                ext = chan[3]
                fade = jnp.exp(-ext)
                weight = shade * (1.0 - fade) * trans
                acc0 = acc0 + weight * chan[0]
                acc1 = acc1 + weight * chan[1]
                acc2 = acc2 + weight * chan[2]
                return (trans * fade, acc0, acc1, acc2, total + ext)

            zeros = jnp.zeros((sub, width), jnp.float32)
            init = (jnp.ones((sub, width), jnp.float32), zeros, zeros, zeros, zeros)
            trans, acc0, acc1, acc2, total = lax.fori_loop(
                EDGE, depth - EDGE, step, init, unroll=2)
            color_ref[0, rs, cs] = acc0
            color_ref[1, rs, cs] = acc1
            color_ref[2, rs, cs] = acc2
            depth_ref[rs, cs] = total
            trans_ref[rs, cs] = trans


def edge_kernel(table, flags, front_ref, back_ref, color_ref, depth_ref, trans_ref,
                out_color_ref, out_depth_ref, *, segments, rows):
    span, tall, lanes = front_ref.shape
    keep = row_keep(flags, tall, lanes, rows)
    palette = Palette(table, segments)

    def side(ref, outside):
        smoothed = []
        for i in range(1, span - 1):
            inside = keep & ~outside(i)
            smoothed.append(smooth_plane(ref[i - 1], ref[i], ref[i + 1], inside, rows))
        cells = []
        for j in range(1, len(smoothed) - 1):
            cells.append(palette.cell(smoothed[j - 1][0], smoothed[j][0], smoothed[j + 1][0],
                                      smoothed[j][1], smoothed[j][2]))
        return cells

    front = side(front_ref, lambda i: (i == 1) & (flags[0] == 1))
    back = side(back_ref, lambda i: (i == span - 2) & (flags[1] == 1))
    mid_color = [color_ref[c] for c in range(3)]
    mid_depth = depth_ref[...]
    mid_trans = trans_ref[...]
    color = [jnp.zeros((rows, lanes), jnp.float32) for c in range(3)]
    total = jnp.zeros((rows, lanes), jnp.float32)
    trans = jnp.ones((rows, lanes), jnp.float32)

    def add_cells(cells, color, total, trans):
        for shade, chan in cells:
            fade = jnp.exp(-chan[3])
            weight = shade * (1.0 - fade) * trans
            color = [color[c] + weight * chan[c] for c in range(3)]
            total = total + chan[3]
            trans = trans * fade
        return color, total, trans

    color, total, trans = add_cells(front, color, total, trans)
    color = [color[c] + trans * mid_color[c] for c in range(3)]
    total = total + mid_depth
    trans = trans * mid_trans
    color, total, trans = add_cells(back, color, total, trans)
    for c in range(3):
        out_color_ref[c] = color[c]
    out_depth_ref[...] = total


def render_block(table, flags, volume, side, front, back, rows, segments):
    depth, _, lanes = volume.shape
    smem = pl.BlockSpec(memory_space=pltpu.SMEM)
    vmem = pl.BlockSpec(memory_space=pltpu.VMEM)
    color_shape = jax.ShapeDtypeStruct((3, rows, lanes), jnp.float32)
    plane_shape = jax.ShapeDtypeStruct((rows, lanes), jnp.float32)
    middle = pl.pallas_call(
        lambda *refs: middle_kernel(*refs, segments=segments, rows=rows, width=256),
        in_specs=[smem, smem, vmem, vmem],
        out_specs=[vmem, vmem, vmem],
        out_shape=[color_shape, plane_shape, plane_shape],
        scratch_shapes=[pltpu.VMEM((depth, rows, lanes), jnp.float32) for _ in range(3)],
        compiler_params=pltpu.CompilerParams(vmem_limit_bytes=48 * 1024 * 1024),
    )(table, flags, volume, side)
    return pl.pallas_call(
        lambda *refs: edge_kernel(*refs, segments=segments, rows=rows),
        in_specs=[smem, smem] + [vmem] * 5,
        out_specs=[vmem, vmem],
        out_shape=[color_shape, plane_shape],
        compiler_params=pltpu.CompilerParams(vmem_limit_bytes=48 * 1024 * 1024),
    )(table, flags, front, back, *middle)


def body(volume, knot_pos, knot_color):
    depth_count = lax.axis_size("depth")
    depth, rows, width = volume.shape
    sigma_scale = 4.0 / (depth * depth_count)
    x_low = shifted(volume[:, rows - 2:], "tile", 1)
    x_high = shifted(volume[:, :2], "tile", -1)
    gap = jnp.zeros((depth, TALL - rows - 4, width), volume.dtype)
    side = jnp.concatenate([x_high, gap, x_low], axis=1).astype(jnp.float32)
    planes = lambda a, b: jnp.concatenate([volume[a:b].astype(jnp.float32), side[a:b]], axis=1)
    sides = jnp.concatenate([x_high, gap, x_low], axis=1)
    narrow = lambda a, b: jnp.concatenate([volume[a:b], sides[a:b]], axis=1)
    z_low = shifted(narrow(depth - 2, depth), "depth", 1).astype(jnp.float32)
    z_high = shifted(narrow(0, 2), "depth", -1).astype(jnp.float32)
    front = jnp.concatenate([z_low, planes(0, EDGE + 2)], axis=0)
    back = jnp.concatenate([planes(depth - EDGE - 2, depth), z_high], axis=0)
    d = lax.axis_index("depth")
    t = lax.axis_index("tile")
    flags = jnp.stack([d == 0, d == depth_count - 1, t == 0, t == lax.axis_size("tile") - 1])
    table = ramp_table(knot_pos, knot_color, sigma_scale)
    brick_color, optical_depth = render_block(
        table, flags.astype(jnp.int32), volume, side, front, back, rows, knot_pos.shape[0] - 1)
    piece = width // depth_count
    weighted = jnp.concatenate([brick_color, optical_depth[None]], axis=0)
    weighted = weighted.reshape(4, rows, depth_count, piece).transpose(2, 0, 1, 3)
    blocks = lax.all_to_all(weighted, "depth", 0, 0, tiled=True)
    ahead = jnp.zeros((rows, piece), jnp.float32)
    image = jnp.zeros((3, rows, piece), jnp.float32)
    for b in range(depth_count):
        image = image + blocks[b, :3] * jnp.exp(-ahead)[None]
        ahead = ahead + blocks[b, 3]
    return jnp.concatenate([image, (1.0 - jnp.exp(-ahead))[None]], axis=0)


def solution(mesh):
    in_specs = (P("depth", "tile", None), P(), P())
    out_specs = P(None, "tile", "depth")
    return jax.shard_map(body, mesh=mesh, in_specs=in_specs, out_specs=out_specs, check_vma=False)
```

```python
import jax
import jax.numpy as jnp
from jax import lax
from jax.experimental import pallas as pl
from jax.experimental.pallas import tpu as pltpu
from jax.sharding import PartitionSpec as P

TALL = 24
EDGE = 2


def shifted(block, axis, move):
    size = lax.axis_size(axis)
    pairs = [(i, i + move) for i in range(size) if 0 <= i + move < size]
    return lax.ppermute(block, axis, pairs)


def ramp_table(knot_pos, knot_color, sigma_scale):
    knot_float = knot_pos.astype(jnp.float32)
    palette = knot_color.astype(jnp.float32) / 255.0
    palette = palette * jnp.array([1.0, 1.0, 1.0, sigma_scale], jnp.float32)[:, None]
    gaps = knot_float[1:] - knot_float[:-1]
    slopes = (palette[:, 1:] - palette[:, :-1]) / gaps[None]
    offsets = palette[:, :-1] - slopes * knot_float[None, :-1]
    count = knot_pos.shape[0]
    pad = lambda v: jnp.pad(v, (0, count - v.shape[0]))
    bounds = jnp.stack([knot_float[0], knot_float[-1]])
    rows = [knot_float] + [pad(offsets[c]) for c in range(4)] + [pad(slopes[c]) for c in range(4)]
    rows += [pad(bounds)]
    return jnp.stack(rows)


def y_prev(a):
    rolled = pltpu.roll(a, 1, 1)
    lane = lax.broadcasted_iota(jnp.int32, (a.shape[0], 128), 1)
    first = jnp.where(lane == 0, 0.0, rolled[:, :128])
    return jnp.concatenate([first, rolled[:, 128:]], axis=1)


def y_next(a):
    rolled = pltpu.roll(a, a.shape[1] - 1, 1)
    lane = lax.broadcasted_iota(jnp.int32, (a.shape[0], 128), 1)
    last = jnp.where(lane == 127, 0.0, rolled[:, -128:])
    return jnp.concatenate([rolled[:, :-128], last], axis=1)


def smooth_plane(low, mid, high, keep, rows):
    tall = mid.shape[0]
    near = low + high + pltpu.roll(mid, tall - 1, 0) + pltpu.roll(mid, 1, 0)
    near = near + y_prev(mid) + y_next(mid)
    smooth = 0.4 * mid + 0.1 * near
    if keep.shape[0] == tall:
        smooth = jnp.where(keep, smooth, 0.0)
    else:
        smooth = jnp.concatenate([smooth[:rows], jnp.where(keep, smooth[rows:], 0.0)], axis=0)
    smooth = smooth.astype(jnp.bfloat16).astype(jnp.float32)
    center = smooth[:rows]
    slope_x = 0.5 * (pltpu.roll(smooth, tall - 1, 0)[:rows] - pltpu.roll(smooth, 1, 0)[:rows])
    slope_y = 0.5 * (y_next(center) - y_prev(center))
    return center, slope_x * slope_x + slope_y * slope_y, 0.8 * slope_x


class Palette:
    def __init__(self, table, segments):
        self.knots = [table[0, k] for k in range(segments)]
        self.offsets = [[table[1 + c, k] for k in range(segments)] for c in range(4)]
        self.slopes = [[table[5 + c, k] for k in range(segments)] for c in range(4)]
        self.lo = table[9, 0]
        self.hi = table[9, 1]
        self.segments = segments

    def cell(self, before, center, after, square, facing):
        slope_z = 0.5 * (after - before)
        facing = jnp.abs(0.6 * slope_z + facing)
        norm = slope_z * slope_z + square + 0.1
        shade = 0.3 + 0.7 * facing * lax.rsqrt(norm)
        lookup = jnp.clip(127.5 + 70.0 * center, self.lo, self.hi)
        offset = [jnp.full_like(lookup, self.offsets[c][0]) for c in range(4)]
        slope = [jnp.full_like(lookup, self.slopes[c][0]) for c in range(4)]
        for k in range(1, self.segments):
            above = lookup >= self.knots[k]
            offset = [jnp.where(above, self.offsets[c][k], offset[c]) for c in range(4)]
            slope = [jnp.where(above, self.slopes[c][k], slope[c]) for c in range(4)]
        chan = [offset[c] + slope[c] * lookup for c in range(4)]
        return shade, chan


def row_keep(flags, tall, lanes, rows):
    row = lax.broadcasted_iota(jnp.int32, (tall, lanes), 0)
    return ((row != tall - 1) | (flags[2] == 0)) & ((row != rows) | (flags[3] == 0))


def middle_kernel(table, flags, volume_ref, side_ref, color_ref, depth_ref, trans_ref,
                  smooth_ref, square_ref, facing_ref, *, segments, rows, width):
    depth, _, lanes = volume_ref.shape
    tall = rows + side_ref.shape[1]
    keep = row_keep(flags, tall, lanes, rows)[rows:]

    def joined(i):
        return jnp.concatenate([volume_ref[i].astype(jnp.float32), side_ref[i]], axis=0)

    def plane(i, carry):
        center, square, facing = smooth_plane(joined(i - 1), joined(i), joined(i + 1), keep, rows)
        smooth_ref[i] = center
        square_ref[i] = square
        facing_ref[i] = facing
        return carry

    lax.fori_loop(1, depth - 1, plane, 0, unroll=2)
    palette = Palette(table, segments)
    sub = 8
    for r0 in range(0, rows, sub):
        for c0 in range(0, lanes, width):
            rs = pl.ds(r0, sub)
            cs = pl.ds(c0, width)

            def step(z, carry):
                trans, acc0, acc1, acc2, total = carry
                shade, chan = palette.cell(
                    smooth_ref[z - 1, rs, cs], smooth_ref[z, rs, cs], smooth_ref[z + 1, rs, cs],
                    square_ref[z, rs, cs], facing_ref[z, rs, cs])
                ext = chan[3]
                fade = jnp.exp(-ext)
                weight = shade * (1.0 - fade) * trans
                acc0 = acc0 + weight * chan[0]
                acc1 = acc1 + weight * chan[1]
                acc2 = acc2 + weight * chan[2]
                return (trans * fade, acc0, acc1, acc2, total + ext)

            zeros = jnp.zeros((sub, width), jnp.float32)
            init = (jnp.ones((sub, width), jnp.float32), zeros, zeros, zeros, zeros)
            trans, acc0, acc1, acc2, total = lax.fori_loop(
                EDGE, depth - EDGE, step, init, unroll=2)
            color_ref[0, rs, cs] = acc0
            color_ref[1, rs, cs] = acc1
            color_ref[2, rs, cs] = acc2
            depth_ref[rs, cs] = total
            trans_ref[rs, cs] = trans


def edge_kernel(table, flags, front_ref, back_ref, color_ref, depth_ref, trans_ref,
                out_color_ref, out_depth_ref, *, segments, rows):
    tall, lanes = front_ref.shape[1:]
    keep = row_keep(flags, tall, lanes, rows)
    palette = Palette(table, segments)

    def cells_of(ref, outside):
        smoothed = []
        for i in range(1, ref.shape[0] - 1):
            inside = keep & ~outside(i)
            smoothed.append(smooth_plane(ref[i - 1], ref[i], ref[i + 1], inside, rows))
        cells = []
        for j in range(1, len(smoothed) - 1):
            cells.append(palette.cell(smoothed[j - 1][0], smoothed[j][0], smoothed[j + 1][0],
                                      smoothed[j][1], smoothed[j][2]))
        return cells

    def segment(cells):
        color = [jnp.zeros((rows, lanes), jnp.float32) for c in range(3)]
        total = jnp.zeros((rows, lanes), jnp.float32)
        trans = jnp.ones((rows, lanes), jnp.float32)
        for shade, chan in cells:
            fade = jnp.exp(-chan[3])
            weight = shade * (1.0 - fade) * trans
            color = [color[c] + weight * chan[c] for c in range(3)]
            total = total + chan[3]
            trans = trans * fade
        return color, total, trans

    def join(a, b):
        return ([a[0][c] + a[2] * b[0][c] for c in range(3)], a[1] + b[1], a[2] * b[2])

    def only_if(flag, seg):
        color, total, trans = seg
        return ([jnp.where(flag, color[c], 0.0) for c in range(3)],
                jnp.where(flag, total, 0.0), jnp.where(flag, trans, 1.0))

    first = flags[0] == 1
    last = flags[1] == 1
    front = segment(cells_of(front_ref, lambda i: i == 1))
    span = back_ref.shape[0]
    back_cells = cells_of(back_ref, lambda i: (i >= span - 4) & last)
    own_back = segment(back_cells[:EDGE])
    next_front = segment(back_cells[EDGE:])
    middle = ([color_ref[c] for c in range(3)], depth_ref[...], trans_ref[...])
    result = join(only_if(first, front), middle)
    result = join(result, own_back)
    result = join(result, only_if(~last, next_front))
    for c in range(3):
        out_color_ref[c] = result[0][c]
    out_depth_ref[...] = result[1]


def render_block(table, flags, volume, side, front, back, rows, segments):
    depth, _, lanes = volume.shape
    smem = pl.BlockSpec(memory_space=pltpu.SMEM)
    vmem = pl.BlockSpec(memory_space=pltpu.VMEM)
    color_shape = jax.ShapeDtypeStruct((3, rows, lanes), jnp.float32)
    plane_shape = jax.ShapeDtypeStruct((rows, lanes), jnp.float32)
    middle = pl.pallas_call(
        lambda *refs: middle_kernel(*refs, segments=segments, rows=rows, width=256),
        in_specs=[smem, smem, vmem, vmem],
        out_specs=[vmem, vmem, vmem],
        out_shape=[color_shape, plane_shape, plane_shape],
        scratch_shapes=[pltpu.VMEM((depth, rows, lanes), jnp.float32) for _ in range(3)],
        compiler_params=pltpu.CompilerParams(vmem_limit_bytes=48 * 1024 * 1024),
    )(table, flags, volume, side)
    return pl.pallas_call(
        lambda *refs: edge_kernel(*refs, segments=segments, rows=rows),
        in_specs=[smem, smem] + [vmem] * 5,
        out_specs=[vmem, vmem],
        out_shape=[color_shape, plane_shape],
        compiler_params=pltpu.CompilerParams(vmem_limit_bytes=48 * 1024 * 1024),
    )(table, flags, front, back, *middle)


def body(volume, knot_pos, knot_color):
    depth_count = lax.axis_size("depth")
    depth, rows, width = volume.shape
    sigma_scale = 4.0 / (depth * depth_count)
    x_low = shifted(volume[:, rows - 2:], "tile", 1)
    x_high = shifted(volume[:, :2], "tile", -1)
    gap = jnp.zeros((depth, TALL - rows - 4, width), volume.dtype)
    side = jnp.concatenate([x_high, gap, x_low], axis=1).astype(jnp.float32)
    planes = lambda a, b: jnp.concatenate([volume[a:b].astype(jnp.float32), side[a:b]], axis=1)
    sides = jnp.concatenate([x_high, gap, x_low], axis=1)
    narrow = lambda a, b: jnp.concatenate([volume[a:b], sides[a:b]], axis=1)
    z_next = shifted(narrow(0, 2 * EDGE), "depth", -1).astype(jnp.float32)
    front = jnp.concatenate([jnp.zeros_like(z_next[:2]), planes(0, EDGE + 2)], axis=0)
    back = jnp.concatenate([planes(depth - 2 * EDGE, depth), z_next], axis=0)
    d = lax.axis_index("depth")
    t = lax.axis_index("tile")
    flags = jnp.stack([d == 0, d == depth_count - 1, t == 0, t == lax.axis_size("tile") - 1])
    table = ramp_table(knot_pos, knot_color, sigma_scale)
    brick_color, optical_depth = render_block(
        table, flags.astype(jnp.int32), volume, side, front, back, rows, knot_pos.shape[0] - 1)
    piece = width // depth_count
    weighted = jnp.concatenate([brick_color, optical_depth[None]], axis=0)
    weighted = weighted.reshape(4, rows, depth_count, piece).transpose(2, 0, 1, 3)
    blocks = lax.all_to_all(weighted, "depth", 0, 0, tiled=True)
    ahead = jnp.zeros((rows, piece), jnp.float32)
    image = jnp.zeros((3, rows, piece), jnp.float32)
    for b in range(depth_count):
        image = image + blocks[b, :3] * jnp.exp(-ahead)[None]
        ahead = ahead + blocks[b, 3]
    return jnp.concatenate([image, (1.0 - jnp.exp(-ahead))[None]], axis=0)


def solution(mesh):
    in_specs = (P("depth", "tile", None), P(), P())
    out_specs = P(None, "tile", "depth")
    return jax.shard_map(body, mesh=mesh, in_specs=in_specs, out_specs=out_specs, check_vma=False)
```

```python
import jax
import jax.numpy as jnp
from jax import lax
from jax.experimental import pallas as pl
from jax.experimental.pallas import tpu as pltpu
from jax.sharding import PartitionSpec as P

TALL = 24
EDGE = 2


def shifted(block, axis, move):
    size = lax.axis_size(axis)
    pairs = [(i, i + move) for i in range(size) if 0 <= i + move < size]
    return lax.ppermute(block, axis, pairs)


def ramp_table(knot_pos, knot_color, sigma_scale):
    knot_float = knot_pos.astype(jnp.float32)
    palette = knot_color.astype(jnp.float32) / 255.0
    palette = palette * jnp.array([1.0, 1.0, 1.0, sigma_scale], jnp.float32)[:, None]
    gaps = knot_float[1:] - knot_float[:-1]
    slopes = (palette[:, 1:] - palette[:, :-1]) / gaps[None]
    offsets = palette[:, :-1] - slopes * knot_float[None, :-1]
    count = knot_pos.shape[0]
    pad = lambda v: jnp.pad(v, (0, count - v.shape[0]))
    bounds = jnp.stack([knot_float[0], knot_float[-1]])
    rows = [knot_float] + [pad(offsets[c]) for c in range(4)] + [pad(slopes[c]) for c in range(4)]
    rows += [pad(bounds)]
    return jnp.stack(rows)


def y_prev(a):
    rolled = pltpu.roll(a, 1, 1)
    lane = lax.broadcasted_iota(jnp.int32, (a.shape[0], 128), 1)
    first = jnp.where(lane == 0, 0.0, rolled[:, :128])
    return jnp.concatenate([first, rolled[:, 128:]], axis=1)


def y_next(a):
    rolled = pltpu.roll(a, a.shape[1] - 1, 1)
    lane = lax.broadcasted_iota(jnp.int32, (a.shape[0], 128), 1)
    last = jnp.where(lane == 127, 0.0, rolled[:, -128:])
    return jnp.concatenate([rolled[:, :-128], last], axis=1)


def smooth_plane(low, mid, high, keep, rows):
    tall = mid.shape[0]
    near = low + high + pltpu.roll(mid, tall - 1, 0) + pltpu.roll(mid, 1, 0)
    near = near + y_prev(mid) + y_next(mid)
    smooth = 0.4 * mid + 0.1 * near
    if keep.shape[0] == tall:
        smooth = jnp.where(keep, smooth, 0.0)
    else:
        smooth = jnp.concatenate([smooth[:rows], jnp.where(keep, smooth[rows:], 0.0)], axis=0)
    smooth = smooth.astype(jnp.bfloat16).astype(jnp.float32)
    center = smooth[:rows]
    slope_x = 0.5 * (pltpu.roll(smooth, tall - 1, 0)[:rows] - pltpu.roll(smooth, 1, 0)[:rows])
    slope_y = 0.5 * (y_next(center) - y_prev(center))
    return center, slope_x * slope_x + slope_y * slope_y, 0.8 * slope_x


class Palette:
    def __init__(self, table, segments):
        self.knots = [table[0, k] for k in range(segments)]
        self.offsets = [[table[1 + c, k] for k in range(segments)] for c in range(4)]
        self.slopes = [[table[5 + c, k] for k in range(segments)] for c in range(4)]
        self.lo = table[9, 0]
        self.hi = table[9, 1]
        self.segments = segments

    def cell(self, before, center, after, square, facing):
        slope_z = 0.5 * (after - before)
        facing = jnp.abs(0.6 * slope_z + facing)
        norm = slope_z * slope_z + square + 0.1
        shade = 0.3 + 0.7 * facing * lax.rsqrt(norm)
        lookup = jnp.clip(127.5 + 70.0 * center, self.lo, self.hi)
        offset = [jnp.full_like(lookup, self.offsets[c][0]) for c in range(4)]
        slope = [jnp.full_like(lookup, self.slopes[c][0]) for c in range(4)]
        for k in range(1, self.segments):
            above = lookup >= self.knots[k]
            offset = [jnp.where(above, self.offsets[c][k], offset[c]) for c in range(4)]
            slope = [jnp.where(above, self.slopes[c][k], slope[c]) for c in range(4)]
        chan = [offset[c] + slope[c] * lookup for c in range(4)]
        return shade, chan


def row_keep(flags, tall, lanes, rows):
    row = lax.broadcasted_iota(jnp.int32, (tall, lanes), 0)
    return ((row != tall - 1) | (flags[2] == 0)) & ((row != rows) | (flags[3] == 0))


def middle_kernel(table, flags, volume_ref, side_ref, color_ref, depth_ref, trans_ref,
                  kept_ref, terms_ref, smooth_ref, square_ref, facing_ref, *, segments, rows, width):
    depth, _, lanes = volume_ref.shape
    tall = rows + side_ref.shape[1]
    keep = row_keep(flags, tall, lanes, rows)[rows:]

    def joined(i):
        return jnp.concatenate([volume_ref[i].astype(jnp.float32), side_ref[i]], axis=0)

    def plane(i, carry):
        center, square, facing = smooth_plane(joined(i - 1), joined(i), joined(i + 1), keep, rows)
        smooth_ref[i] = center
        square_ref[i] = square
        facing_ref[i] = facing
        return carry

    lax.fori_loop(1, depth - 1, plane, 0, unroll=2)
    for n, i in enumerate((1, 2, depth - 3, depth - 2)):
        kept_ref[n] = smooth_ref[i]
    for n, i in enumerate((1, depth - 2)):
        terms_ref[2 * n] = square_ref[i]
        terms_ref[2 * n + 1] = facing_ref[i]
    palette = Palette(table, segments)
    sub = 8
    for r0 in range(0, rows, sub):
        for c0 in range(0, lanes, width):
            rs = pl.ds(r0, sub)
            cs = pl.ds(c0, width)

            def step(z, carry):
                trans, acc0, acc1, acc2, total = carry
                shade, chan = palette.cell(
                    smooth_ref[z - 1, rs, cs], smooth_ref[z, rs, cs], smooth_ref[z + 1, rs, cs],
                    square_ref[z, rs, cs], facing_ref[z, rs, cs])
                ext = chan[3]
                fade = jnp.exp(-ext)
                weight = shade * (1.0 - fade) * trans
                acc0 = acc0 + weight * chan[0]
                acc1 = acc1 + weight * chan[1]
                acc2 = acc2 + weight * chan[2]
                return (trans * fade, acc0, acc1, acc2, total + ext)

            zeros = jnp.zeros((sub, width), jnp.float32)
            init = (jnp.ones((sub, width), jnp.float32), zeros, zeros, zeros, zeros)
            trans, acc0, acc1, acc2, total = lax.fori_loop(
                EDGE, depth - EDGE, step, init, unroll=2)
            color_ref[0, rs, cs] = acc0
            color_ref[1, rs, cs] = acc1
            color_ref[2, rs, cs] = acc2
            depth_ref[rs, cs] = total
            trans_ref[rs, cs] = trans


def edge_kernel(table, flags, front_ref, back_ref, kept_ref, terms_ref, color_ref, depth_ref,
                trans_ref, out_color_ref, out_depth_ref, *, segments, rows):
    tall, lanes = front_ref.shape[1:]
    keep = row_keep(flags, tall, lanes, rows)
    palette = Palette(table, segments)
    first = flags[0] == 1
    last = flags[1] == 1
    zero = jnp.zeros((rows, lanes), jnp.float32)
    s0, q0, f0 = smooth_plane(jnp.zeros((tall, lanes), jnp.float32), front_ref[0], front_ref[1],
                              keep, rows)
    s1, s2, s61, s62 = [kept_ref[n] for n in range(4)]
    q1, f1, q62, f62 = [terms_ref[n] for n in range(4)]
    front_cells = [palette.cell(zero, s0, s1, q0, f0), palette.cell(s0, s1, s2, q1, f1)]
    smoothed = [(s61, None, None), (s62, q62, f62)]
    for i in range(1, back_ref.shape[0] - 1):
        inside = keep & ~((i >= 2) & last)
        smoothed.append(smooth_plane(back_ref[i - 1], back_ref[i], back_ref[i + 1], inside, rows))
    back_cells = []
    for j in range(1, len(smoothed) - 1):
        back_cells.append(palette.cell(smoothed[j - 1][0], smoothed[j][0], smoothed[j + 1][0],
                                       smoothed[j][1], smoothed[j][2]))

    def segment(cells):
        color = [jnp.zeros((rows, lanes), jnp.float32) for c in range(3)]
        total = jnp.zeros((rows, lanes), jnp.float32)
        trans = jnp.ones((rows, lanes), jnp.float32)
        for shade, chan in cells:
            fade = jnp.exp(-chan[3])
            weight = shade * (1.0 - fade) * trans
            color = [color[c] + weight * chan[c] for c in range(3)]
            total = total + chan[3]
            trans = trans * fade
        return color, total, trans

    def join(a, b):
        return ([a[0][c] + a[2] * b[0][c] for c in range(3)], a[1] + b[1], a[2] * b[2])

    def only_if(flag, seg):
        color, total, trans = seg
        return ([jnp.where(flag, color[c], 0.0) for c in range(3)],
                jnp.where(flag, total, 0.0), jnp.where(flag, trans, 1.0))

    front = segment(front_cells)
    own_back = segment(back_cells[:EDGE])
    next_front = segment(back_cells[EDGE:])
    middle = ([color_ref[c] for c in range(3)], depth_ref[...], trans_ref[...])
    result = join(only_if(first, front), middle)
    result = join(result, own_back)
    result = join(result, only_if(~last, next_front))
    for c in range(3):
        out_color_ref[c] = result[0][c]
    out_depth_ref[...] = result[1]


def render_block(table, flags, volume, side, front, back, rows, segments):
    depth, _, lanes = volume.shape
    smem = pl.BlockSpec(memory_space=pltpu.SMEM)
    vmem = pl.BlockSpec(memory_space=pltpu.VMEM)
    color_shape = jax.ShapeDtypeStruct((3, rows, lanes), jnp.float32)
    plane_shape = jax.ShapeDtypeStruct((rows, lanes), jnp.float32)
    middle = pl.pallas_call(
        lambda *refs: middle_kernel(*refs, segments=segments, rows=rows, width=256),
        in_specs=[smem, smem, vmem, vmem],
        out_specs=[vmem] * 5,
        out_shape=[color_shape, plane_shape, plane_shape,
                   jax.ShapeDtypeStruct((4, rows, lanes), jnp.float32),
                   jax.ShapeDtypeStruct((4, rows, lanes), jnp.float32)],
        scratch_shapes=[pltpu.VMEM((depth, rows, lanes), jnp.float32) for _ in range(3)],
        compiler_params=pltpu.CompilerParams(vmem_limit_bytes=48 * 1024 * 1024),
    )(table, flags, volume, side)
    return pl.pallas_call(
        lambda *refs: edge_kernel(*refs, segments=segments, rows=rows),
        in_specs=[smem, smem] + [vmem] * 7,
        out_specs=[vmem, vmem],
        out_shape=[color_shape, plane_shape],
        compiler_params=pltpu.CompilerParams(vmem_limit_bytes=48 * 1024 * 1024),
    )(table, flags, front, back, middle[3], middle[4], *middle[:3])


def body(volume, knot_pos, knot_color):
    depth_count = lax.axis_size("depth")
    depth, rows, width = volume.shape
    sigma_scale = 4.0 / (depth * depth_count)
    x_low = shifted(volume[:, rows - 2:], "tile", 1)
    x_high = shifted(volume[:, :2], "tile", -1)
    gap = jnp.zeros((depth, TALL - rows - 4, width), volume.dtype)
    side = jnp.concatenate([x_high, gap, x_low], axis=1).astype(jnp.float32)
    planes = lambda a, b: jnp.concatenate([volume[a:b].astype(jnp.float32), side[a:b]], axis=1)
    sides = jnp.concatenate([x_high, gap, x_low], axis=1)
    narrow = lambda a, b: jnp.concatenate([volume[a:b], sides[a:b]], axis=1)
    z_next = shifted(narrow(0, 2 * EDGE), "depth", -1).astype(jnp.float32)
    front = planes(0, 2)
    back = jnp.concatenate([planes(depth - 2, depth), z_next], axis=0)
    d = lax.axis_index("depth")
    t = lax.axis_index("tile")
    flags = jnp.stack([d == 0, d == depth_count - 1, t == 0, t == lax.axis_size("tile") - 1])
    table = ramp_table(knot_pos, knot_color, sigma_scale)
    brick_color, optical_depth = render_block(
        table, flags.astype(jnp.int32), volume, side, front, back, rows, knot_pos.shape[0] - 1)
    piece = width // depth_count
    weighted = jnp.concatenate([brick_color, optical_depth[None]], axis=0)
    weighted = weighted.reshape(4, rows, depth_count, piece).transpose(2, 0, 1, 3)
    blocks = lax.all_to_all(weighted, "depth", 0, 0, tiled=True)
    ahead = jnp.zeros((rows, piece), jnp.float32)
    image = jnp.zeros((3, rows, piece), jnp.float32)
    for b in range(depth_count):
        image = image + blocks[b, :3] * jnp.exp(-ahead)[None]
        ahead = ahead + blocks[b, 3]
    return jnp.concatenate([image, (1.0 - jnp.exp(-ahead))[None]], axis=0)


def solution(mesh):
    in_specs = (P("depth", "tile", None), P(), P())
    out_specs = P(None, "tile", "depth")
    return jax.shard_map(body, mesh=mesh, in_specs=in_specs, out_specs=out_specs, check_vma=False)
```

```python
import jax
import jax.numpy as jnp
from jax import lax
from jax.experimental import pallas as pl
from jax.experimental.pallas import tpu as pltpu
from jax.sharding import PartitionSpec as P

TALL = 24
EDGE = 2


def shifted(block, axis, move):
    size = lax.axis_size(axis)
    pairs = [(i, i + move) for i in range(size) if 0 <= i + move < size]
    return lax.ppermute(block, axis, pairs)


def ramp_table(knot_pos, knot_color, sigma_scale):
    knot_float = knot_pos.astype(jnp.float32)
    palette = knot_color.astype(jnp.float32) / 255.0
    palette = palette * jnp.array([1.0, 1.0, 1.0, sigma_scale], jnp.float32)[:, None]
    gaps = knot_float[1:] - knot_float[:-1]
    slopes = (palette[:, 1:] - palette[:, :-1]) / gaps[None]
    offsets = palette[:, :-1] - slopes * knot_float[None, :-1]
    count = knot_pos.shape[0]
    pad = lambda v: jnp.pad(v, (0, count - v.shape[0]))
    bounds = jnp.stack([knot_float[0], knot_float[-1]])
    rows = [knot_float] + [pad(offsets[c]) for c in range(4)] + [pad(slopes[c]) for c in range(4)]
    rows += [pad(bounds)]
    return jnp.stack(rows)


def y_prev(a):
    rolled = pltpu.roll(a, 1, 1)
    lane = lax.broadcasted_iota(jnp.int32, (a.shape[0], 128), 1)
    first = jnp.where(lane == 0, 0.0, rolled[:, :128])
    return jnp.concatenate([first, rolled[:, 128:]], axis=1)


def y_next(a):
    rolled = pltpu.roll(a, a.shape[1] - 1, 1)
    lane = lax.broadcasted_iota(jnp.int32, (a.shape[0], 128), 1)
    last = jnp.where(lane == 127, 0.0, rolled[:, -128:])
    return jnp.concatenate([rolled[:, :-128], last], axis=1)


def smooth_plane(low, mid, high, keep, rows):
    tall = mid.shape[0]
    near = low + high + pltpu.roll(mid, tall - 1, 0) + pltpu.roll(mid, 1, 0)
    near = near + y_prev(mid) + y_next(mid)
    smooth = 0.4 * mid + 0.1 * near
    if keep.shape[0] == tall:
        smooth = jnp.where(keep, smooth, 0.0)
    else:
        smooth = jnp.concatenate([smooth[:rows], jnp.where(keep, smooth[rows:], 0.0)], axis=0)
    smooth = smooth.astype(jnp.bfloat16).astype(jnp.float32)
    center = smooth[:rows]
    slope_x = 0.5 * (pltpu.roll(smooth, tall - 1, 0)[:rows] - pltpu.roll(smooth, 1, 0)[:rows])
    slope_y = 0.5 * (y_next(center) - y_prev(center))
    return center, slope_x * slope_x + slope_y * slope_y, 0.8 * slope_x


class Palette:
    def __init__(self, table, segments):
        self.knots = [table[0, k] for k in range(segments)]
        self.offsets = [[table[1 + c, k] for k in range(segments)] for c in range(4)]
        self.slopes = [[table[5 + c, k] for k in range(segments)] for c in range(4)]
        self.lo = table[9, 0]
        self.hi = table[9, 1]
        self.segments = segments

    def cell(self, before, center, after, square, facing):
        slope_z = 0.5 * (after - before)
        facing = jnp.abs(0.6 * slope_z + facing)
        norm = slope_z * slope_z + square + 0.1
        shade = 0.3 + 0.7 * facing * lax.rsqrt(norm)
        lookup = jnp.clip(127.5 + 70.0 * center, self.lo, self.hi)
        offset = [jnp.full_like(lookup, self.offsets[c][0]) for c in range(4)]
        slope = [jnp.full_like(lookup, self.slopes[c][0]) for c in range(4)]
        for k in range(1, self.segments):
            above = lookup >= self.knots[k]
            offset = [jnp.where(above, self.offsets[c][k], offset[c]) for c in range(4)]
            slope = [jnp.where(above, self.slopes[c][k], slope[c]) for c in range(4)]
        chan = [offset[c] + slope[c] * lookup for c in range(4)]
        return shade, chan


def row_keep(flags, tall, lanes, rows):
    row = lax.broadcasted_iota(jnp.int32, (tall, lanes), 0)
    return ((row != tall - 1) | (flags[2] == 0)) & ((row != rows) | (flags[3] == 0))


def middle_kernel(table, flags, volume_ref, side_ref, color_ref, depth_ref, trans_ref,
                  kept_ref, terms_ref, smooth_ref, square_ref, facing_ref, *, segments, rows, width):
    depth, _, lanes = volume_ref.shape
    tall = rows + side_ref.shape[1]
    keep = row_keep(flags, tall, lanes, rows)[rows:]

    def joined(i):
        return jnp.concatenate([volume_ref[i].astype(jnp.float32), side_ref[i]], axis=0)

    def plane(i, carry):
        center, square, facing = smooth_plane(joined(i - 1), joined(i), joined(i + 1), keep, rows)
        smooth_ref[i] = center
        square_ref[i] = square
        facing_ref[i] = facing
        return carry

    lax.fori_loop(1, depth - 1, plane, 0, unroll=2)
    for n, i in enumerate((1, 2, depth - 3, depth - 2)):
        kept_ref[n] = smooth_ref[i]
    for n, i in enumerate((1, depth - 2)):
        terms_ref[2 * n] = square_ref[i]
        terms_ref[2 * n + 1] = facing_ref[i]
    palette = Palette(table, segments)
    sub = 8
    for r0 in range(0, rows, sub):
        for c0 in range(0, lanes, width):
            rs = pl.ds(r0, sub)
            cs = pl.ds(c0, width)

            def step(z, carry):
                trans, acc0, acc1, acc2, total = carry
                shade, chan = palette.cell(
                    smooth_ref[z - 1, rs, cs], smooth_ref[z, rs, cs], smooth_ref[z + 1, rs, cs],
                    square_ref[z, rs, cs], facing_ref[z, rs, cs])
                ext = chan[3]
                fade = jnp.exp(-ext)
                weight = shade * (1.0 - fade) * trans
                acc0 = acc0 + weight * chan[0]
                acc1 = acc1 + weight * chan[1]
                acc2 = acc2 + weight * chan[2]
                return (trans * fade, acc0, acc1, acc2, total + ext)

            zeros = jnp.zeros((sub, width), jnp.float32)
            init = (jnp.ones((sub, width), jnp.float32), zeros, zeros, zeros, zeros)
            trans, acc0, acc1, acc2, total = lax.fori_loop(
                EDGE, depth - EDGE, step, init, unroll=2)
            color_ref[0, rs, cs] = acc0
            color_ref[1, rs, cs] = acc1
            color_ref[2, rs, cs] = acc2
            depth_ref[rs, cs] = total
            trans_ref[rs, cs] = trans


def edge_kernel(table, flags, front_ref, back_ref, kept_ref, terms_ref, color_ref, depth_ref,
                trans_ref, out_color_ref, out_depth_ref, *, segments, rows):
    tall, lanes = front_ref.shape[1:]
    keep = row_keep(flags, tall, lanes, rows)
    palette = Palette(table, segments)
    first = flags[0] == 1
    last = flags[1] == 1
    zero = jnp.zeros((rows, lanes), jnp.float32)
    s0, q0, f0 = smooth_plane(jnp.zeros((tall, lanes), jnp.float32), front_ref[0], front_ref[1],
                              keep, rows)
    s1, s2, s61, s62 = [kept_ref[n] for n in range(4)]
    q1, f1, q62, f62 = [terms_ref[n] for n in range(4)]
    front_cells = [palette.cell(zero, s0, s1, q0, f0), palette.cell(s0, s1, s2, q1, f1)]
    smoothed = [(s61, None, None), (s62, q62, f62)]
    for i in range(1, back_ref.shape[0] - 1):
        inside = keep & ~((i >= 2) & last)
        smoothed.append(smooth_plane(back_ref[i - 1], back_ref[i], back_ref[i + 1], inside, rows))
    back_cells = []
    for j in range(1, len(smoothed) - 1):
        back_cells.append(palette.cell(smoothed[j - 1][0], smoothed[j][0], smoothed[j + 1][0],
                                       smoothed[j][1], smoothed[j][2]))

    def segment(cells):
        color = [jnp.zeros((rows, lanes), jnp.float32) for c in range(3)]
        total = jnp.zeros((rows, lanes), jnp.float32)
        trans = jnp.ones((rows, lanes), jnp.float32)
        for shade, chan in cells:
            fade = jnp.exp(-chan[3])
            weight = shade * (1.0 - fade) * trans
            color = [color[c] + weight * chan[c] for c in range(3)]
            total = total + chan[3]
            trans = trans * fade
        return color, total, trans

    def join(a, b):
        return ([a[0][c] + a[2] * b[0][c] for c in range(3)], a[1] + b[1], a[2] * b[2])

    def only_if(flag, seg):
        color, total, trans = seg
        return ([jnp.where(flag, color[c], 0.0) for c in range(3)],
                jnp.where(flag, total, 0.0), jnp.where(flag, trans, 1.0))

    front = segment(front_cells)
    own_back = segment(back_cells[:EDGE])
    next_front = segment(back_cells[EDGE:])
    middle = ([color_ref[c] for c in range(3)], depth_ref[...], trans_ref[...])
    result = join(only_if(first, front), middle)
    result = join(result, own_back)
    result = join(result, only_if(~last, next_front))
    for c in range(3):
        out_color_ref[c] = result[0][c]
    out_depth_ref[...] = result[1]


def render_block(table, flags, volume, side, front, back, rows, segments):
    depth, _, lanes = volume.shape
    smem = pl.BlockSpec(memory_space=pltpu.SMEM)
    vmem = pl.BlockSpec(memory_space=pltpu.VMEM)
    color_shape = jax.ShapeDtypeStruct((3, rows, lanes), jnp.float32)
    plane_shape = jax.ShapeDtypeStruct((rows, lanes), jnp.float32)
    middle = pl.pallas_call(
        lambda *refs: middle_kernel(*refs, segments=segments, rows=rows, width=256),
        in_specs=[smem, smem, vmem, vmem],
        out_specs=[vmem] * 5,
        out_shape=[color_shape, plane_shape, plane_shape,
                   jax.ShapeDtypeStruct((4, rows, lanes), jnp.float32),
                   jax.ShapeDtypeStruct((4, rows, lanes), jnp.float32)],
        scratch_shapes=[pltpu.VMEM((depth, rows, lanes), jnp.float32) for _ in range(3)],
        compiler_params=pltpu.CompilerParams(vmem_limit_bytes=48 * 1024 * 1024),
    )(table, flags, volume, side)
    return pl.pallas_call(
        lambda *refs: edge_kernel(*refs, segments=segments, rows=rows),
        in_specs=[smem, smem] + [vmem] * 7,
        out_specs=[vmem, vmem],
        out_shape=[color_shape, plane_shape],
        compiler_params=pltpu.CompilerParams(vmem_limit_bytes=48 * 1024 * 1024),
    )(table, flags, front, back, middle[3], middle[4], *middle[:3])


def body(volume, knot_pos, knot_color):
    depth_count = lax.axis_size("depth")
    depth, rows, width = volume.shape
    sigma_scale = 4.0 / (depth * depth_count)
    x_low = shifted(volume[:, rows - 2:].transpose(1, 0, 2), "tile", 1).transpose(1, 0, 2)
    x_high = shifted(volume[:, :2].transpose(1, 0, 2), "tile", -1).transpose(1, 0, 2)
    gap = jnp.zeros((depth, TALL - rows - 4, width), volume.dtype)
    side = jnp.concatenate([x_high, gap, x_low], axis=1).astype(jnp.float32)
    planes = lambda a, b: jnp.concatenate([volume[a:b].astype(jnp.float32), side[a:b]], axis=1)
    sides = jnp.concatenate([x_high, gap, x_low], axis=1)
    narrow = lambda a, b: jnp.concatenate([volume[a:b], sides[a:b]], axis=1)
    z_next = shifted(narrow(0, 2 * EDGE), "depth", -1).astype(jnp.float32)
    front = planes(0, 2)
    back = jnp.concatenate([planes(depth - 2, depth), z_next], axis=0)
    d = lax.axis_index("depth")
    t = lax.axis_index("tile")
    flags = jnp.stack([d == 0, d == depth_count - 1, t == 0, t == lax.axis_size("tile") - 1])
    table = ramp_table(knot_pos, knot_color, sigma_scale)
    brick_color, optical_depth = render_block(
        table, flags.astype(jnp.int32), volume, side, front, back, rows, knot_pos.shape[0] - 1)
    piece = width // depth_count
    weighted = jnp.concatenate([brick_color, optical_depth[None]], axis=0)
    weighted = weighted.reshape(4, rows, depth_count, piece).transpose(2, 0, 1, 3)
    blocks = lax.all_to_all(weighted, "depth", 0, 0, tiled=True)
    ahead = jnp.zeros((rows, piece), jnp.float32)
    image = jnp.zeros((3, rows, piece), jnp.float32)
    for b in range(depth_count):
        image = image + blocks[b, :3] * jnp.exp(-ahead)[None]
        ahead = ahead + blocks[b, 3]
    return jnp.concatenate([image, (1.0 - jnp.exp(-ahead))[None]], axis=0)


def solution(mesh):
    in_specs = (P("depth", "tile", None), P(), P())
    out_specs = P(None, "tile", "depth")
    return jax.shard_map(body, mesh=mesh, in_specs=in_specs, out_specs=out_specs, check_vma=False)
```

```python
import jax
import jax.numpy as jnp
from jax import lax
from jax.experimental import pallas as pl
from jax.experimental.pallas import tpu as pltpu
from jax.sharding import PartitionSpec as P

TALL = 24
EDGE = 2


def shifted(block, axis, move):
    size = lax.axis_size(axis)
    pairs = [(i, i + move) for i in range(size) if 0 <= i + move < size]
    return lax.ppermute(block, axis, pairs)


def ramp_table(knot_pos, knot_color, sigma_scale):
    knot_float = knot_pos.astype(jnp.float32)
    palette = knot_color.astype(jnp.float32) / 255.0
    palette = palette * jnp.array([1.0, 1.0, 1.0, sigma_scale], jnp.float32)[:, None]
    gaps = knot_float[1:] - knot_float[:-1]
    slopes = (palette[:, 1:] - palette[:, :-1]) / gaps[None]
    offsets = palette[:, :-1] - slopes * knot_float[None, :-1]
    count = knot_pos.shape[0]
    pad = lambda v: jnp.pad(v, (0, count - v.shape[0]))
    bounds = jnp.stack([knot_float[0], knot_float[-1]])
    rows = [knot_float] + [pad(offsets[c]) for c in range(4)] + [pad(slopes[c]) for c in range(4)]
    rows += [pad(bounds)]
    return jnp.stack(rows)


def y_prev(a):
    rolled = pltpu.roll(a, 1, 1)
    lane = lax.broadcasted_iota(jnp.int32, (a.shape[0], 128), 1)
    first = jnp.where(lane == 0, 0.0, rolled[:, :128])
    return jnp.concatenate([first, rolled[:, 128:]], axis=1)


def y_next(a):
    rolled = pltpu.roll(a, a.shape[1] - 1, 1)
    lane = lax.broadcasted_iota(jnp.int32, (a.shape[0], 128), 1)
    last = jnp.where(lane == 127, 0.0, rolled[:, -128:])
    return jnp.concatenate([rolled[:, :-128], last], axis=1)


def smooth_plane(low, mid, high, keep, rows):
    tall = mid.shape[0]
    near = low + high + pltpu.roll(mid, tall - 1, 0) + pltpu.roll(mid, 1, 0)
    near = near + y_prev(mid) + y_next(mid)
    smooth = 0.4 * mid + 0.1 * near
    if keep.shape[0] == tall:
        smooth = jnp.where(keep, smooth, 0.0)
    else:
        smooth = jnp.concatenate([smooth[:rows], jnp.where(keep, smooth[rows:], 0.0)], axis=0)
    smooth = smooth.astype(jnp.bfloat16).astype(jnp.float32)
    center = smooth[:rows]
    slope_x = 0.5 * (pltpu.roll(smooth, tall - 1, 0)[:rows] - pltpu.roll(smooth, 1, 0)[:rows])
    slope_y = 0.5 * (y_next(center) - y_prev(center))
    return center, slope_x * slope_x + slope_y * slope_y, 0.8 * slope_x


class Palette:
    def __init__(self, table, segments):
        self.knots = [table[0, k] for k in range(segments)]
        self.offsets = [[table[1 + c, k] for k in range(segments)] for c in range(4)]
        self.slopes = [[table[5 + c, k] for k in range(segments)] for c in range(4)]
        self.lo = table[9, 0]
        self.hi = table[9, 1]
        self.segments = segments

    def cell(self, before, center, after, square, facing):
        slope_z = 0.5 * (after - before)
        facing = jnp.abs(0.6 * slope_z + facing)
        norm = slope_z * slope_z + square + 0.1
        shade = 0.3 + 0.7 * facing * lax.rsqrt(norm)
        lookup = jnp.clip(127.5 + 70.0 * center, self.lo, self.hi)
        offset = [jnp.full_like(lookup, self.offsets[c][0]) for c in range(4)]
        slope = [jnp.full_like(lookup, self.slopes[c][0]) for c in range(4)]
        for k in range(1, self.segments):
            above = lookup >= self.knots[k]
            offset = [jnp.where(above, self.offsets[c][k], offset[c]) for c in range(4)]
            slope = [jnp.where(above, self.slopes[c][k], slope[c]) for c in range(4)]
        chan = [offset[c] + slope[c] * lookup for c in range(4)]
        return shade, chan


def row_keep(flags, tall, lanes, rows):
    row = lax.broadcasted_iota(jnp.int32, (tall, lanes), 0)
    return ((row != tall - 1) | (flags[2] == 0)) & ((row != rows) | (flags[3] == 0))


def middle_kernel(table, flags, volume_ref, side_ref, color_ref, depth_ref, trans_ref,
                  kept_ref, terms_ref, smooth_ref, square_ref, facing_ref, *, segments, rows, width):
    depth, _, lanes = volume_ref.shape
    tall = rows + side_ref.shape[1]
    keep = row_keep(flags, tall, lanes, rows)[rows:]

    def joined(i):
        return jnp.concatenate([volume_ref[i], side_ref[i]], axis=0)

    def plane(i, carry):
        center, square, facing = smooth_plane(joined(i - 1), joined(i), joined(i + 1), keep, rows)
        smooth_ref[i] = center
        square_ref[i] = square
        facing_ref[i] = facing
        return carry

    lax.fori_loop(1, depth - 1, plane, 0, unroll=2)
    for n, i in enumerate((1, 2, depth - 3, depth - 2)):
        kept_ref[n] = smooth_ref[i]
    for n, i in enumerate((1, depth - 2)):
        terms_ref[2 * n] = square_ref[i]
        terms_ref[2 * n + 1] = facing_ref[i]
    palette = Palette(table, segments)
    sub = 8
    for r0 in range(0, rows, sub):
        for c0 in range(0, lanes, width):
            rs = pl.ds(r0, sub)
            cs = pl.ds(c0, width)

            def step(z, carry):
                trans, acc0, acc1, acc2, total = carry
                shade, chan = palette.cell(
                    smooth_ref[z - 1, rs, cs], smooth_ref[z, rs, cs], smooth_ref[z + 1, rs, cs],
                    square_ref[z, rs, cs], facing_ref[z, rs, cs])
                ext = chan[3]
                fade = jnp.exp(-ext)
                weight = shade * (1.0 - fade) * trans
                acc0 = acc0 + weight * chan[0]
                acc1 = acc1 + weight * chan[1]
                acc2 = acc2 + weight * chan[2]
                return (trans * fade, acc0, acc1, acc2, total + ext)

            zeros = jnp.zeros((sub, width), jnp.float32)
            init = (jnp.ones((sub, width), jnp.float32), zeros, zeros, zeros, zeros)
            trans, acc0, acc1, acc2, total = lax.fori_loop(
                EDGE, depth - EDGE, step, init, unroll=2)
            color_ref[0, rs, cs] = acc0
            color_ref[1, rs, cs] = acc1
            color_ref[2, rs, cs] = acc2
            depth_ref[rs, cs] = total
            trans_ref[rs, cs] = trans


def edge_kernel(table, flags, front_ref, back_ref, kept_ref, terms_ref, color_ref, depth_ref,
                trans_ref, out_color_ref, out_depth_ref, *, segments, rows):
    tall, lanes = front_ref.shape[1:]
    keep = row_keep(flags, tall, lanes, rows)
    palette = Palette(table, segments)
    first = flags[0] == 1
    last = flags[1] == 1
    zero = jnp.zeros((rows, lanes), jnp.float32)
    s0, q0, f0 = smooth_plane(jnp.zeros((tall, lanes), jnp.float32), front_ref[0], front_ref[1],
                              keep, rows)
    s1, s2, s61, s62 = [kept_ref[n] for n in range(4)]
    q1, f1, q62, f62 = [terms_ref[n] for n in range(4)]
    front_cells = [palette.cell(zero, s0, s1, q0, f0), palette.cell(s0, s1, s2, q1, f1)]
    smoothed = [(s61, None, None), (s62, q62, f62)]
    for i in range(1, back_ref.shape[0] - 1):
        inside = keep & ~((i >= 2) & last)
        smoothed.append(smooth_plane(back_ref[i - 1], back_ref[i], back_ref[i + 1], inside, rows))
    back_cells = []
    for j in range(1, len(smoothed) - 1):
        back_cells.append(palette.cell(smoothed[j - 1][0], smoothed[j][0], smoothed[j + 1][0],
                                       smoothed[j][1], smoothed[j][2]))

    def segment(cells):
        color = [jnp.zeros((rows, lanes), jnp.float32) for c in range(3)]
        total = jnp.zeros((rows, lanes), jnp.float32)
        trans = jnp.ones((rows, lanes), jnp.float32)
        for shade, chan in cells:
            fade = jnp.exp(-chan[3])
            weight = shade * (1.0 - fade) * trans
            color = [color[c] + weight * chan[c] for c in range(3)]
            total = total + chan[3]
            trans = trans * fade
        return color, total, trans

    def join(a, b):
        return ([a[0][c] + a[2] * b[0][c] for c in range(3)], a[1] + b[1], a[2] * b[2])

    def only_if(flag, seg):
        color, total, trans = seg
        return ([jnp.where(flag, color[c], 0.0) for c in range(3)],
                jnp.where(flag, total, 0.0), jnp.where(flag, trans, 1.0))

    front = segment(front_cells)
    own_back = segment(back_cells[:EDGE])
    next_front = segment(back_cells[EDGE:])
    middle = ([color_ref[c] for c in range(3)], depth_ref[...], trans_ref[...])
    result = join(only_if(first, front), middle)
    result = join(result, own_back)
    result = join(result, only_if(~last, next_front))
    for c in range(3):
        out_color_ref[c] = result[0][c]
    out_depth_ref[...] = result[1]


def render_block(table, flags, volume, side, front, back, rows, segments):
    depth, _, lanes = volume.shape
    smem = pl.BlockSpec(memory_space=pltpu.SMEM)
    vmem = pl.BlockSpec(memory_space=pltpu.VMEM)
    color_shape = jax.ShapeDtypeStruct((3, rows, lanes), jnp.float32)
    plane_shape = jax.ShapeDtypeStruct((rows, lanes), jnp.float32)
    middle = pl.pallas_call(
        lambda *refs: middle_kernel(*refs, segments=segments, rows=rows, width=256),
        in_specs=[smem, smem, vmem, vmem],
        out_specs=[vmem] * 5,
        out_shape=[color_shape, plane_shape, plane_shape,
                   jax.ShapeDtypeStruct((4, rows, lanes), jnp.float32),
                   jax.ShapeDtypeStruct((4, rows, lanes), jnp.float32)],
        scratch_shapes=[pltpu.VMEM((depth, rows, lanes), jnp.float32) for _ in range(3)],
        compiler_params=pltpu.CompilerParams(vmem_limit_bytes=48 * 1024 * 1024),
    )(table, flags, volume.astype(jnp.float32), side)
    return pl.pallas_call(
        lambda *refs: edge_kernel(*refs, segments=segments, rows=rows),
        in_specs=[smem, smem] + [vmem] * 7,
        out_specs=[vmem, vmem],
        out_shape=[color_shape, plane_shape],
        compiler_params=pltpu.CompilerParams(vmem_limit_bytes=48 * 1024 * 1024),
    )(table, flags, front, back, middle[3], middle[4], *middle[:3])


def body(volume, knot_pos, knot_color):
    depth_count = lax.axis_size("depth")
    depth, rows, width = volume.shape
    sigma_scale = 4.0 / (depth * depth_count)
    x_low = shifted(volume[:, rows - 2:], "tile", 1)
    x_high = shifted(volume[:, :2], "tile", -1)
    gap = jnp.zeros((depth, TALL - rows - 4, width), volume.dtype)
    side = jnp.concatenate([x_high, gap, x_low], axis=1).astype(jnp.float32)
    planes = lambda a, b: jnp.concatenate([volume[a:b].astype(jnp.float32), side[a:b]], axis=1)
    sides = jnp.concatenate([x_high, gap, x_low], axis=1)
    narrow = lambda a, b: jnp.concatenate([volume[a:b], sides[a:b]], axis=1)
    z_next = shifted(narrow(0, 2 * EDGE), "depth", -1).astype(jnp.float32)
    front = planes(0, 2)
    back = jnp.concatenate([planes(depth - 2, depth), z_next], axis=0)
    d = lax.axis_index("depth")
    t = lax.axis_index("tile")
    flags = jnp.stack([d == 0, d == depth_count - 1, t == 0, t == lax.axis_size("tile") - 1])
    table = ramp_table(knot_pos, knot_color, sigma_scale)
    brick_color, optical_depth = render_block(
        table, flags.astype(jnp.int32), volume, side, front, back, rows, knot_pos.shape[0] - 1)
    piece = width // depth_count
    weighted = jnp.concatenate([brick_color, optical_depth[None]], axis=0)
    weighted = weighted.reshape(4, rows, depth_count, piece).transpose(2, 0, 1, 3)
    blocks = lax.all_to_all(weighted, "depth", 0, 0, tiled=True)
    ahead = jnp.zeros((rows, piece), jnp.float32)
    image = jnp.zeros((3, rows, piece), jnp.float32)
    for b in range(depth_count):
        image = image + blocks[b, :3] * jnp.exp(-ahead)[None]
        ahead = ahead + blocks[b, 3]
    return jnp.concatenate([image, (1.0 - jnp.exp(-ahead))[None]], axis=0)


def solution(mesh):
    in_specs = (P("depth", "tile", None), P(), P())
    out_specs = P(None, "tile", "depth")
    return jax.shard_map(body, mesh=mesh, in_specs=in_specs, out_specs=out_specs, check_vma=False)
```

```python
import jax
import jax.numpy as jnp
from jax import lax
from jax.experimental import pallas as pl
from jax.experimental.pallas import tpu as pltpu
from jax.sharding import PartitionSpec as P

TALL = 24
EDGE = 2


def shifted(block, axis, move):
    size = lax.axis_size(axis)
    pairs = [(i, i + move) for i in range(size) if 0 <= i + move < size]
    return lax.ppermute(block, axis, pairs)


def ramp_table(knot_pos, knot_color, sigma_scale):
    knot_float = knot_pos.astype(jnp.float32)
    palette = knot_color.astype(jnp.float32) / 255.0
    palette = palette * jnp.array([1.0, 1.0, 1.0, sigma_scale], jnp.float32)[:, None]
    gaps = knot_float[1:] - knot_float[:-1]
    slopes = (palette[:, 1:] - palette[:, :-1]) / gaps[None]
    offsets = palette[:, :-1] - slopes * knot_float[None, :-1]
    count = knot_pos.shape[0]
    pad = lambda v: jnp.pad(v, (0, count - v.shape[0]))
    bounds = jnp.stack([knot_float[0], knot_float[-1]])
    rows = [knot_float] + [pad(offsets[c]) for c in range(4)] + [pad(slopes[c]) for c in range(4)]
    rows += [pad(bounds)]
    return jnp.stack(rows)


def y_prev(a):
    rolled = pltpu.roll(a, 1, 1)
    lane = lax.broadcasted_iota(jnp.int32, (a.shape[0], 128), 1)
    first = jnp.where(lane == 0, 0.0, rolled[:, :128])
    return jnp.concatenate([first, rolled[:, 128:]], axis=1)


def y_next(a):
    rolled = pltpu.roll(a, a.shape[1] - 1, 1)
    lane = lax.broadcasted_iota(jnp.int32, (a.shape[0], 128), 1)
    last = jnp.where(lane == 127, 0.0, rolled[:, -128:])
    return jnp.concatenate([rolled[:, :-128], last], axis=1)


def smooth_plane(low, mid, high, keep, rows):
    tall = mid.shape[0]
    near = low + high + pltpu.roll(mid, tall - 1, 0) + pltpu.roll(mid, 1, 0)
    near = near + y_prev(mid) + y_next(mid)
    smooth = 0.4 * mid + 0.1 * near
    if keep.shape[0] == tall:
        smooth = jnp.where(keep, smooth, 0.0)
    else:
        smooth = jnp.concatenate([smooth[:rows], jnp.where(keep, smooth[rows:], 0.0)], axis=0)
    smooth = smooth.astype(jnp.bfloat16).astype(jnp.float32)
    center = smooth[:rows]
    slope_x = 0.5 * (pltpu.roll(smooth, tall - 1, 0)[:rows] - pltpu.roll(smooth, 1, 0)[:rows])
    slope_y = 0.5 * (y_next(center) - y_prev(center))
    return center, slope_x * slope_x + slope_y * slope_y, 0.8 * slope_x


class Palette:
    def __init__(self, table, segments):
        self.knots = [table[0, k] for k in range(segments)]
        self.offsets = [[table[1 + c, k] for k in range(segments)] for c in range(4)]
        self.slopes = [[table[5 + c, k] for k in range(segments)] for c in range(4)]
        self.lo = table[9, 0]
        self.hi = table[9, 1]
        self.segments = segments

    def cell(self, before, center, after, square, facing):
        slope_z = 0.5 * (after - before)
        facing = jnp.abs(0.6 * slope_z + facing)
        norm = slope_z * slope_z + square + 0.1
        shade = 0.3 + 0.7 * facing * lax.rsqrt(norm)
        lookup = jnp.clip(127.5 + 70.0 * center, self.lo, self.hi)
        offset = [jnp.full_like(lookup, self.offsets[c][0]) for c in range(4)]
        slope = [jnp.full_like(lookup, self.slopes[c][0]) for c in range(4)]
        for k in range(1, self.segments):
            above = lookup >= self.knots[k]
            offset = [jnp.where(above, self.offsets[c][k], offset[c]) for c in range(4)]
            slope = [jnp.where(above, self.slopes[c][k], slope[c]) for c in range(4)]
        chan = [offset[c] + slope[c] * lookup for c in range(4)]
        return shade, chan


def row_keep(flags, tall, lanes, rows):
    row = lax.broadcasted_iota(jnp.int32, (tall, lanes), 0)
    return ((row != tall - 1) | (flags[2] == 0)) & ((row != rows) | (flags[3] == 0))


def middle_kernel(table, flags, volume_ref, side_ref, color_ref, depth_ref, trans_ref,
                  kept_ref, terms_ref, smooth_ref, square_ref, facing_ref, *, segments, rows, width):
    depth, _, lanes = volume_ref.shape
    tall = rows + side_ref.shape[1]
    keep = row_keep(flags, tall, lanes, rows)[rows:]

    def joined(i):
        return jnp.concatenate([volume_ref[i].astype(jnp.float32), side_ref[i]], axis=0)

    def plane(i, carry):
        center, square, facing = smooth_plane(joined(i - 1), joined(i), joined(i + 1), keep, rows)
        smooth_ref[i] = center
        square_ref[i] = square
        facing_ref[i] = facing
        return carry

    lax.fori_loop(1, depth - 1, plane, 0, unroll=4)
    for n, i in enumerate((1, 2, depth - 3, depth - 2)):
        kept_ref[n] = smooth_ref[i]
    for n, i in enumerate((1, depth - 2)):
        terms_ref[2 * n] = square_ref[i]
        terms_ref[2 * n + 1] = facing_ref[i]
    palette = Palette(table, segments)
    sub = 8
    for r0 in range(0, rows, sub):
        for c0 in range(0, lanes, width):
            rs = pl.ds(r0, sub)
            cs = pl.ds(c0, width)

            def step(z, carry):
                trans, acc0, acc1, acc2, total = carry
                shade, chan = palette.cell(
                    smooth_ref[z - 1, rs, cs], smooth_ref[z, rs, cs], smooth_ref[z + 1, rs, cs],
                    square_ref[z, rs, cs], facing_ref[z, rs, cs])
                ext = chan[3]
                fade = jnp.exp(-ext)
                weight = shade * (1.0 - fade) * trans
                acc0 = acc0 + weight * chan[0]
                acc1 = acc1 + weight * chan[1]
                acc2 = acc2 + weight * chan[2]
                return (trans * fade, acc0, acc1, acc2, total + ext)

            zeros = jnp.zeros((sub, width), jnp.float32)
            init = (jnp.ones((sub, width), jnp.float32), zeros, zeros, zeros, zeros)
            trans, acc0, acc1, acc2, total = lax.fori_loop(
                EDGE, depth - EDGE, step, init, unroll=2)
            color_ref[0, rs, cs] = acc0
            color_ref[1, rs, cs] = acc1
            color_ref[2, rs, cs] = acc2
            depth_ref[rs, cs] = total
            trans_ref[rs, cs] = trans


def edge_kernel(table, flags, front_ref, back_ref, kept_ref, terms_ref, color_ref, depth_ref,
                trans_ref, out_color_ref, out_depth_ref, *, segments, rows):
    tall, lanes = front_ref.shape[1:]
    keep = row_keep(flags, tall, lanes, rows)
    palette = Palette(table, segments)
    first = flags[0] == 1
    last = flags[1] == 1
    zero = jnp.zeros((rows, lanes), jnp.float32)
    s0, q0, f0 = smooth_plane(jnp.zeros((tall, lanes), jnp.float32), front_ref[0], front_ref[1],
                              keep, rows)
    s1, s2, s61, s62 = [kept_ref[n] for n in range(4)]
    q1, f1, q62, f62 = [terms_ref[n] for n in range(4)]
    front_cells = [palette.cell(zero, s0, s1, q0, f0), palette.cell(s0, s1, s2, q1, f1)]
    smoothed = [(s61, None, None), (s62, q62, f62)]
    for i in range(1, back_ref.shape[0] - 1):
        inside = keep & ~((i >= 2) & last)
        smoothed.append(smooth_plane(back_ref[i - 1], back_ref[i], back_ref[i + 1], inside, rows))
    back_cells = []
    for j in range(1, len(smoothed) - 1):
        back_cells.append(palette.cell(smoothed[j - 1][0], smoothed[j][0], smoothed[j + 1][0],
                                       smoothed[j][1], smoothed[j][2]))

    def segment(cells):
        color = [jnp.zeros((rows, lanes), jnp.float32) for c in range(3)]
        total = jnp.zeros((rows, lanes), jnp.float32)
        trans = jnp.ones((rows, lanes), jnp.float32)
        for shade, chan in cells:
            fade = jnp.exp(-chan[3])
            weight = shade * (1.0 - fade) * trans
            color = [color[c] + weight * chan[c] for c in range(3)]
            total = total + chan[3]
            trans = trans * fade
        return color, total, trans

    def join(a, b):
        return ([a[0][c] + a[2] * b[0][c] for c in range(3)], a[1] + b[1], a[2] * b[2])

    def only_if(flag, seg):
        color, total, trans = seg
        return ([jnp.where(flag, color[c], 0.0) for c in range(3)],
                jnp.where(flag, total, 0.0), jnp.where(flag, trans, 1.0))

    front = segment(front_cells)
    own_back = segment(back_cells[:EDGE])
    next_front = segment(back_cells[EDGE:])
    middle = ([color_ref[c] for c in range(3)], depth_ref[...], trans_ref[...])
    result = join(only_if(first, front), middle)
    result = join(result, own_back)
    result = join(result, only_if(~last, next_front))
    for c in range(3):
        out_color_ref[c] = result[0][c]
    out_depth_ref[...] = result[1]


def render_block(table, flags, volume, side, front, back, rows, segments):
    depth, _, lanes = volume.shape
    smem = pl.BlockSpec(memory_space=pltpu.SMEM)
    vmem = pl.BlockSpec(memory_space=pltpu.VMEM)
    color_shape = jax.ShapeDtypeStruct((3, rows, lanes), jnp.float32)
    plane_shape = jax.ShapeDtypeStruct((rows, lanes), jnp.float32)
    middle = pl.pallas_call(
        lambda *refs: middle_kernel(*refs, segments=segments, rows=rows, width=256),
        in_specs=[smem, smem, vmem, vmem],
        out_specs=[vmem] * 5,
        out_shape=[color_shape, plane_shape, plane_shape,
                   jax.ShapeDtypeStruct((4, rows, lanes), jnp.float32),
                   jax.ShapeDtypeStruct((4, rows, lanes), jnp.float32)],
        scratch_shapes=[pltpu.VMEM((depth, rows, lanes), jnp.float32) for _ in range(3)],
        compiler_params=pltpu.CompilerParams(vmem_limit_bytes=48 * 1024 * 1024),
    )(table, flags, volume, side)
    return pl.pallas_call(
        lambda *refs: edge_kernel(*refs, segments=segments, rows=rows),
        in_specs=[smem, smem] + [vmem] * 7,
        out_specs=[vmem, vmem],
        out_shape=[color_shape, plane_shape],
        compiler_params=pltpu.CompilerParams(vmem_limit_bytes=48 * 1024 * 1024),
    )(table, flags, front, back, middle[3], middle[4], *middle[:3])


def body(volume, knot_pos, knot_color):
    depth_count = lax.axis_size("depth")
    depth, rows, width = volume.shape
    sigma_scale = 4.0 / (depth * depth_count)
    x_low = shifted(volume[:, rows - 2:], "tile", 1)
    x_high = shifted(volume[:, :2], "tile", -1)
    gap = jnp.zeros((depth, TALL - rows - 4, width), volume.dtype)
    side = jnp.concatenate([x_high, gap, x_low], axis=1).astype(jnp.float32)
    planes = lambda a, b: jnp.concatenate([volume[a:b].astype(jnp.float32), side[a:b]], axis=1)
    sides = jnp.concatenate([x_high, gap, x_low], axis=1)
    narrow = lambda a, b: jnp.concatenate([volume[a:b], sides[a:b]], axis=1)
    z_next = shifted(narrow(0, 2 * EDGE), "depth", -1).astype(jnp.float32)
    front = planes(0, 2)
    back = jnp.concatenate([planes(depth - 2, depth), z_next], axis=0)
    d = lax.axis_index("depth")
    t = lax.axis_index("tile")
    flags = jnp.stack([d == 0, d == depth_count - 1, t == 0, t == lax.axis_size("tile") - 1])
    table = ramp_table(knot_pos, knot_color, sigma_scale)
    brick_color, optical_depth = render_block(
        table, flags.astype(jnp.int32), volume, side, front, back, rows, knot_pos.shape[0] - 1)
    piece = width // depth_count
    weighted = jnp.concatenate([brick_color, optical_depth[None]], axis=0)
    weighted = weighted.reshape(4, rows, depth_count, piece).transpose(2, 0, 1, 3)
    blocks = lax.all_to_all(weighted, "depth", 0, 0, tiled=True)
    ahead = jnp.zeros((rows, piece), jnp.float32)
    image = jnp.zeros((3, rows, piece), jnp.float32)
    for b in range(depth_count):
        image = image + blocks[b, :3] * jnp.exp(-ahead)[None]
        ahead = ahead + blocks[b, 3]
    return jnp.concatenate([image, (1.0 - jnp.exp(-ahead))[None]], axis=0)


def solution(mesh):
    in_specs = (P("depth", "tile", None), P(), P())
    out_specs = P(None, "tile", "depth")
    return jax.shard_map(body, mesh=mesh, in_specs=in_specs, out_specs=out_specs, check_vma=False)
```

```python
import jax
import jax.numpy as jnp
from jax import lax
from jax.experimental import pallas as pl
from jax.experimental.pallas import tpu as pltpu
from jax.sharding import PartitionSpec as P

TALL = 24
EDGE = 2


def shifted(block, axis, move):
    size = lax.axis_size(axis)
    pairs = [(i, i + move) for i in range(size) if 0 <= i + move < size]
    return lax.ppermute(block, axis, pairs)


def ramp_table(knot_pos, knot_color, sigma_scale):
    knot_float = knot_pos.astype(jnp.float32)
    palette = knot_color.astype(jnp.float32) / 255.0
    palette = palette * jnp.array([1.0, 1.0, 1.0, sigma_scale], jnp.float32)[:, None]
    gaps = knot_float[1:] - knot_float[:-1]
    slopes = (palette[:, 1:] - palette[:, :-1]) / gaps[None]
    offsets = palette[:, :-1] - slopes * knot_float[None, :-1]
    count = knot_pos.shape[0]
    pad = lambda v: jnp.pad(v, (0, count - v.shape[0]))
    bounds = jnp.stack([knot_float[0], knot_float[-1]])
    rows = [knot_float] + [pad(offsets[c]) for c in range(4)] + [pad(slopes[c]) for c in range(4)]
    rows += [pad(bounds)]
    return jnp.stack(rows)


def y_prev(a):
    rolled = pltpu.roll(a, 1, 1)
    lane = lax.broadcasted_iota(jnp.int32, (a.shape[0], 128), 1)
    first = jnp.where(lane == 0, 0.0, rolled[:, :128])
    return jnp.concatenate([first, rolled[:, 128:]], axis=1)


def y_next(a):
    rolled = pltpu.roll(a, a.shape[1] - 1, 1)
    lane = lax.broadcasted_iota(jnp.int32, (a.shape[0], 128), 1)
    last = jnp.where(lane == 127, 0.0, rolled[:, -128:])
    return jnp.concatenate([rolled[:, :-128], last], axis=1)


def smooth_plane(low, mid, high, keep, rows):
    tall = mid.shape[0]
    near = low + high + pltpu.roll(mid, tall - 1, 0) + pltpu.roll(mid, 1, 0)
    near = near + y_prev(mid) + y_next(mid)
    smooth = 0.4 * mid + 0.1 * near
    if keep.shape[0] == tall:
        smooth = jnp.where(keep, smooth, 0.0)
    else:
        smooth = jnp.concatenate([smooth[:rows], jnp.where(keep, smooth[rows:], 0.0)], axis=0)
    smooth = smooth.astype(jnp.bfloat16).astype(jnp.float32)
    center = smooth[:rows]
    slope_x = 0.5 * (pltpu.roll(smooth, tall - 1, 0)[:rows] - pltpu.roll(smooth, 1, 0)[:rows])
    slope_y = 0.5 * (y_next(center) - y_prev(center))
    return center, slope_x * slope_x + slope_y * slope_y + 0.1, 0.56 * slope_x


class Palette:
    def __init__(self, table, segments):
        self.knots = [table[0, k] for k in range(segments)]
        self.offsets = [[table[1 + c, k] for k in range(segments)] for c in range(4)]
        self.slopes = [[table[5 + c, k] for k in range(segments)] for c in range(4)]
        self.lo = table[9, 0]
        self.hi = table[9, 1]
        self.segments = segments

    def cell(self, before, center, after, square, facing):
        step = after - before
        facing = jnp.abs(0.21 * step + facing)
        norm = 0.25 * (step * step) + square
        shade = 0.3 + facing * lax.rsqrt(norm)
        lookup = jnp.clip(127.5 + 70.0 * center, self.lo, self.hi)
        offset = [jnp.full_like(lookup, self.offsets[c][0]) for c in range(4)]
        slope = [jnp.full_like(lookup, self.slopes[c][0]) for c in range(4)]
        for k in range(1, self.segments):
            above = lookup >= self.knots[k]
            offset = [jnp.where(above, self.offsets[c][k], offset[c]) for c in range(4)]
            slope = [jnp.where(above, self.slopes[c][k], slope[c]) for c in range(4)]
        chan = [offset[c] + slope[c] * lookup for c in range(4)]
        return shade, chan


def row_keep(flags, tall, lanes, rows):
    row = lax.broadcasted_iota(jnp.int32, (tall, lanes), 0)
    return ((row != tall - 1) | (flags[2] == 0)) & ((row != rows) | (flags[3] == 0))


def middle_kernel(table, flags, volume_ref, side_ref, color_ref, depth_ref, trans_ref,
                  kept_ref, terms_ref, smooth_ref, square_ref, facing_ref, *, segments, rows, width):
    depth, _, lanes = volume_ref.shape
    tall = rows + side_ref.shape[1]
    keep = row_keep(flags, tall, lanes, rows)[rows:]

    def joined(i):
        return jnp.concatenate([volume_ref[i].astype(jnp.float32), side_ref[i]], axis=0)

    def plane(i, carry):
        center, square, facing = smooth_plane(joined(i - 1), joined(i), joined(i + 1), keep, rows)
        smooth_ref[i] = center
        square_ref[i] = square
        facing_ref[i] = facing
        return carry

    lax.fori_loop(1, depth - 1, plane, 0, unroll=2)
    for n, i in enumerate((1, 2, depth - 3, depth - 2)):
        kept_ref[n] = smooth_ref[i]
    for n, i in enumerate((1, depth - 2)):
        terms_ref[2 * n] = square_ref[i]
        terms_ref[2 * n + 1] = facing_ref[i]
    palette = Palette(table, segments)
    sub = 8
    for r0 in range(0, rows, sub):
        for c0 in range(0, lanes, width):
            rs = pl.ds(r0, sub)
            cs = pl.ds(c0, width)

            def step(z, carry):
                trans, acc0, acc1, acc2, total = carry
                shade, chan = palette.cell(
                    smooth_ref[z - 1, rs, cs], smooth_ref[z, rs, cs], smooth_ref[z + 1, rs, cs],
                    square_ref[z, rs, cs], facing_ref[z, rs, cs])
                ext = chan[3]
                fade = jnp.exp(-ext)
                weight = shade * (1.0 - fade) * trans
                acc0 = acc0 + weight * chan[0]
                acc1 = acc1 + weight * chan[1]
                acc2 = acc2 + weight * chan[2]
                return (trans * fade, acc0, acc1, acc2, total + ext)

            zeros = jnp.zeros((sub, width), jnp.float32)
            init = (jnp.ones((sub, width), jnp.float32), zeros, zeros, zeros, zeros)
            trans, acc0, acc1, acc2, total = lax.fori_loop(
                EDGE, depth - EDGE, step, init, unroll=2)
            color_ref[0, rs, cs] = acc0
            color_ref[1, rs, cs] = acc1
            color_ref[2, rs, cs] = acc2
            depth_ref[rs, cs] = total
            trans_ref[rs, cs] = trans


def edge_kernel(table, flags, front_ref, back_ref, kept_ref, terms_ref, color_ref, depth_ref,
                trans_ref, out_color_ref, out_depth_ref, *, segments, rows):
    tall, lanes = front_ref.shape[1:]
    keep = row_keep(flags, tall, lanes, rows)
    palette = Palette(table, segments)
    first = flags[0] == 1
    last = flags[1] == 1
    zero = jnp.zeros((rows, lanes), jnp.float32)
    s0, q0, f0 = smooth_plane(jnp.zeros((tall, lanes), jnp.float32), front_ref[0], front_ref[1],
                              keep, rows)
    s1, s2, s61, s62 = [kept_ref[n] for n in range(4)]
    q1, f1, q62, f62 = [terms_ref[n] for n in range(4)]
    front_cells = [palette.cell(zero, s0, s1, q0, f0), palette.cell(s0, s1, s2, q1, f1)]
    smoothed = [(s61, None, None), (s62, q62, f62)]
    for i in range(1, back_ref.shape[0] - 1):
        inside = keep & ~((i >= 2) & last)
        smoothed.append(smooth_plane(back_ref[i - 1], back_ref[i], back_ref[i + 1], inside, rows))
    back_cells = []
    for j in range(1, len(smoothed) - 1):
        back_cells.append(palette.cell(smoothed[j - 1][0], smoothed[j][0], smoothed[j + 1][0],
                                       smoothed[j][1], smoothed[j][2]))

    def segment(cells):
        color = [jnp.zeros((rows, lanes), jnp.float32) for c in range(3)]
        total = jnp.zeros((rows, lanes), jnp.float32)
        trans = jnp.ones((rows, lanes), jnp.float32)
        for shade, chan in cells:
            fade = jnp.exp(-chan[3])
            weight = shade * (1.0 - fade) * trans
            color = [color[c] + weight * chan[c] for c in range(3)]
            total = total + chan[3]
            trans = trans * fade
        return color, total, trans

    def join(a, b):
        return ([a[0][c] + a[2] * b[0][c] for c in range(3)], a[1] + b[1], a[2] * b[2])

    def only_if(flag, seg):
        color, total, trans = seg
        return ([jnp.where(flag, color[c], 0.0) for c in range(3)],
                jnp.where(flag, total, 0.0), jnp.where(flag, trans, 1.0))

    front = segment(front_cells)
    own_back = segment(back_cells[:EDGE])
    next_front = segment(back_cells[EDGE:])
    middle = ([color_ref[c] for c in range(3)], depth_ref[...], trans_ref[...])
    result = join(only_if(first, front), middle)
    result = join(result, own_back)
    result = join(result, only_if(~last, next_front))
    for c in range(3):
        out_color_ref[c] = result[0][c]
    out_depth_ref[...] = result[1]


def render_block(table, flags, volume, side, front, back, rows, segments):
    depth, _, lanes = volume.shape
    smem = pl.BlockSpec(memory_space=pltpu.SMEM)
    vmem = pl.BlockSpec(memory_space=pltpu.VMEM)
    color_shape = jax.ShapeDtypeStruct((3, rows, lanes), jnp.float32)
    plane_shape = jax.ShapeDtypeStruct((rows, lanes), jnp.float32)
    middle = pl.pallas_call(
        lambda *refs: middle_kernel(*refs, segments=segments, rows=rows, width=256),
        in_specs=[smem, smem, vmem, vmem],
        out_specs=[vmem] * 5,
        out_shape=[color_shape, plane_shape, plane_shape,
                   jax.ShapeDtypeStruct((4, rows, lanes), jnp.float32),
                   jax.ShapeDtypeStruct((4, rows, lanes), jnp.float32)],
        scratch_shapes=[pltpu.VMEM((depth, rows, lanes), jnp.float32) for _ in range(3)],
        compiler_params=pltpu.CompilerParams(vmem_limit_bytes=48 * 1024 * 1024),
    )(table, flags, volume, side)
    return pl.pallas_call(
        lambda *refs: edge_kernel(*refs, segments=segments, rows=rows),
        in_specs=[smem, smem] + [vmem] * 7,
        out_specs=[vmem, vmem],
        out_shape=[color_shape, plane_shape],
        compiler_params=pltpu.CompilerParams(vmem_limit_bytes=48 * 1024 * 1024),
    )(table, flags, front, back, middle[3], middle[4], *middle[:3])


def body(volume, knot_pos, knot_color):
    depth_count = lax.axis_size("depth")
    depth, rows, width = volume.shape
    sigma_scale = 4.0 / (depth * depth_count)
    x_low = shifted(volume[:, rows - 2:], "tile", 1)
    x_high = shifted(volume[:, :2], "tile", -1)
    gap = jnp.zeros((depth, TALL - rows - 4, width), volume.dtype)
    side = jnp.concatenate([x_high, gap, x_low], axis=1).astype(jnp.float32)
    planes = lambda a, b: jnp.concatenate([volume[a:b].astype(jnp.float32), side[a:b]], axis=1)
    sides = jnp.concatenate([x_high, gap, x_low], axis=1)
    narrow = lambda a, b: jnp.concatenate([volume[a:b], sides[a:b]], axis=1)
    z_next = shifted(narrow(0, 2 * EDGE), "depth", -1).astype(jnp.float32)
    front = planes(0, 2)
    back = jnp.concatenate([planes(depth - 2, depth), z_next], axis=0)
    d = lax.axis_index("depth")
    t = lax.axis_index("tile")
    flags = jnp.stack([d == 0, d == depth_count - 1, t == 0, t == lax.axis_size("tile") - 1])
    table = ramp_table(knot_pos, knot_color, sigma_scale)
    brick_color, optical_depth = render_block(
        table, flags.astype(jnp.int32), volume, side, front, back, rows, knot_pos.shape[0] - 1)
    piece = width // depth_count
    weighted = jnp.concatenate([brick_color, optical_depth[None]], axis=0)
    weighted = weighted.reshape(4, rows, depth_count, piece).transpose(2, 0, 1, 3)
    blocks = lax.all_to_all(weighted, "depth", 0, 0, tiled=True)
    ahead = jnp.zeros((rows, piece), jnp.float32)
    image = jnp.zeros((3, rows, piece), jnp.float32)
    for b in range(depth_count):
        image = image + blocks[b, :3] * jnp.exp(-ahead)[None]
        ahead = ahead + blocks[b, 3]
    return jnp.concatenate([image, (1.0 - jnp.exp(-ahead))[None]], axis=0)


def solution(mesh):
    in_specs = (P("depth", "tile", None), P(), P())
    out_specs = P(None, "tile", "depth")
    return jax.shard_map(body, mesh=mesh, in_specs=in_specs, out_specs=out_specs, check_vma=False)
```

```python
import jax
import jax.numpy as jnp
from jax import lax
from jax.experimental import pallas as pl
from jax.experimental.pallas import tpu as pltpu
from jax.sharding import PartitionSpec as P

TALL = 24
EDGE = 2


def shifted(block, axis, move):
    size = lax.axis_size(axis)
    pairs = [(i, i + move) for i in range(size) if 0 <= i + move < size]
    return lax.ppermute(block, axis, pairs)


def ramp_table(knot_pos, knot_color, sigma_scale):
    knot_float = knot_pos.astype(jnp.float32)
    palette = knot_color.astype(jnp.float32) / 255.0
    palette = palette * jnp.array([1.0, 1.0, 1.0, sigma_scale], jnp.float32)[:, None]
    gaps = knot_float[1:] - knot_float[:-1]
    slopes = (palette[:, 1:] - palette[:, :-1]) / gaps[None]
    offsets = palette[:, :-1] - slopes * knot_float[None, :-1]
    count = knot_pos.shape[0]
    pad = lambda v: jnp.pad(v, (0, count - v.shape[0]))
    bounds = jnp.stack([knot_float[0], knot_float[-1]])
    rows = [knot_float] + [pad(offsets[c]) for c in range(4)] + [pad(slopes[c]) for c in range(4)]
    rows += [pad(bounds)]
    return jnp.stack(rows)


def y_prev(a):
    rolled = pltpu.roll(a, 1, 1)
    lane = lax.broadcasted_iota(jnp.int32, (a.shape[0], 128), 1)
    first = jnp.where(lane == 0, 0.0, rolled[:, :128])
    return jnp.concatenate([first, rolled[:, 128:]], axis=1)


def y_next(a):
    rolled = pltpu.roll(a, a.shape[1] - 1, 1)
    lane = lax.broadcasted_iota(jnp.int32, (a.shape[0], 128), 1)
    last = jnp.where(lane == 127, 0.0, rolled[:, -128:])
    return jnp.concatenate([rolled[:, :-128], last], axis=1)


def smooth_plane(low, mid, high, keep, rows):
    tall = mid.shape[0]
    near = low + high + pltpu.roll(mid, tall - 1, 0) + pltpu.roll(mid, 1, 0)
    near = near + y_prev(mid) + y_next(mid)
    smooth = 0.4 * mid + 0.1 * near
    if keep.shape[0] == tall:
        smooth = jnp.where(keep, smooth, 0.0)
    else:
        smooth = jnp.concatenate([smooth[:rows], jnp.where(keep, smooth[rows:], 0.0)], axis=0)
    smooth = smooth.astype(jnp.bfloat16).astype(jnp.float32)
    center = smooth[:rows]
    slope_x = 0.5 * (pltpu.roll(smooth, tall - 1, 0)[:rows] - pltpu.roll(smooth, 1, 0)[:rows])
    slope_y = 0.5 * (y_next(center) - y_prev(center))
    return center, slope_x * slope_x + slope_y * slope_y, 0.8 * slope_x


class Palette:
    def __init__(self, table, segments):
        self.knots = [table[0, k] for k in range(segments)]
        self.offsets = [[table[1 + c, k] for k in range(segments)] for c in range(4)]
        self.slopes = [[table[5 + c, k] for k in range(segments)] for c in range(4)]
        self.lo = table[9, 0]
        self.hi = table[9, 1]
        self.segments = segments

    def cell(self, before, center, after, square, facing):
        slope_z = 0.5 * (after - before)
        facing = jnp.abs(0.6 * slope_z + facing)
        norm = slope_z * slope_z + square + 0.1
        shade = 0.3 + 0.7 * facing * lax.rsqrt(norm)
        lookup = jnp.clip(127.5 + 70.0 * center, self.lo, self.hi)
        offset = [jnp.full_like(lookup, self.offsets[c][0]) for c in range(4)]
        slope = [jnp.full_like(lookup, self.slopes[c][0]) for c in range(4)]
        for k in range(1, self.segments):
            above = lookup >= self.knots[k]
            offset = [jnp.where(above, self.offsets[c][k], offset[c]) for c in range(4)]
            slope = [jnp.where(above, self.slopes[c][k], slope[c]) for c in range(4)]
        chan = [offset[c] + slope[c] * lookup for c in range(4)]
        return shade, chan


def row_keep(flags, tall, lanes, rows):
    row = lax.broadcasted_iota(jnp.int32, (tall, lanes), 0)
    return ((row != tall - 1) | (flags[2] == 0)) & ((row != rows) | (flags[3] == 0))


def middle_kernel(table, flags, volume_ref, side_ref, color_ref, depth_ref, trans_ref,
                  kept_ref, terms_ref, smooth_ref, square_ref, facing_ref, *, segments, rows, width):
    depth, _, lanes = volume_ref.shape
    tall = rows + side_ref.shape[1]
    keep = row_keep(flags, tall, lanes, rows)[rows:]

    def joined(i):
        return jnp.concatenate([volume_ref[i].astype(jnp.float32), side_ref[i]], axis=0)

    def plane(i, carry):
        center, square, facing = smooth_plane(joined(i - 1), joined(i), joined(i + 1), keep, rows)
        smooth_ref[i] = center
        square_ref[i] = square
        facing_ref[i] = facing
        return carry

    lax.fori_loop(1, depth - 1, plane, 0, unroll=2)
    for n, i in enumerate((1, 2, depth - 3, depth - 2)):
        kept_ref[n] = smooth_ref[i]
    for n, i in enumerate((1, depth - 2)):
        terms_ref[2 * n] = square_ref[i]
        terms_ref[2 * n + 1] = facing_ref[i]
    palette = Palette(table, segments)
    sub = 8
    for r0 in range(0, rows, sub):
        for c0 in range(0, lanes, width):
            rs = pl.ds(r0, sub)
            cs = pl.ds(c0, width)

            def step(z, carry):
                trans, acc0, acc1, acc2, total = carry
                shade, chan = palette.cell(
                    smooth_ref[z - 1, rs, cs], smooth_ref[z, rs, cs], smooth_ref[z + 1, rs, cs],
                    square_ref[z, rs, cs], facing_ref[z, rs, cs])
                ext = chan[3]
                fade = jnp.exp(-ext)
                weight = shade * (1.0 - fade) * trans
                acc0 = acc0 + weight * chan[0]
                acc1 = acc1 + weight * chan[1]
                acc2 = acc2 + weight * chan[2]
                return (trans * fade, acc0, acc1, acc2, total + ext)

            zeros = jnp.zeros((sub, width), jnp.float32)
            init = (jnp.ones((sub, width), jnp.float32), zeros, zeros, zeros, zeros)
            trans, acc0, acc1, acc2, total = lax.fori_loop(
                EDGE, depth - EDGE, step, init, unroll=2)
            color_ref[0, rs, cs] = acc0
            color_ref[1, rs, cs] = acc1
            color_ref[2, rs, cs] = acc2
            depth_ref[rs, cs] = total
            trans_ref[rs, cs] = trans


def edge_kernel(table, flags, front_ref, back_ref, kept_ref, terms_ref, color_ref, depth_ref,
                trans_ref, out_color_ref, out_depth_ref, stash_ref, *, segments, rows):
    tall, lanes = front_ref.shape[1:]
    keep = row_keep(flags, tall, lanes, rows)
    palette = Palette(table, segments)
    first = flags[0] == 1
    last = flags[1] == 1
    s0, q0, f0 = smooth_plane(jnp.zeros((tall, lanes), jnp.float32), front_ref[0], front_ref[1],
                              keep, rows)
    stash_ref[0] = jnp.zeros((rows, lanes), jnp.float32)
    stash_ref[1] = s0
    stash_ref[2] = kept_ref[0]
    stash_ref[3] = kept_ref[1]
    stash_ref[4] = q0
    stash_ref[5] = f0
    stash_ref[6] = terms_ref[0]
    stash_ref[7] = terms_ref[1]
    stash_ref[8] = kept_ref[2]
    stash_ref[9] = kept_ref[3]
    stash_ref[14] = terms_ref[2]
    stash_ref[18] = terms_ref[3]
    for i in range(1, back_ref.shape[0] - 1):
        inside = keep & ~((i >= 2) & last)
        s, q, f = smooth_plane(back_ref[i - 1], back_ref[i], back_ref[i + 1], inside, rows)
        stash_ref[9 + i] = s
        if i < 4:
            stash_ref[14 + i] = q
            stash_ref[18 + i] = f

    def segment(cells, shape):
        color = [jnp.zeros(shape, jnp.float32) for c in range(3)]
        total = jnp.zeros(shape, jnp.float32)
        trans = jnp.ones(shape, jnp.float32)
        for shade, chan in cells:
            fade = jnp.exp(-chan[3])
            weight = shade * (1.0 - fade) * trans
            color = [color[c] + weight * chan[c] for c in range(3)]
            total = total + chan[3]
            trans = trans * fade
        return color, total, trans

    def join(a, b):
        return ([a[0][c] + a[2] * b[0][c] for c in range(3)], a[1] + b[1], a[2] * b[2])

    def only_if(flag, seg):
        color, total, trans = seg
        return ([jnp.where(flag, color[c], 0.0) for c in range(3)],
                jnp.where(flag, total, 0.0), jnp.where(flag, trans, 1.0))

    sub, width = 8, 256
    for r0 in range(0, rows, sub):
        for c0 in range(0, lanes, width):
            rs = pl.ds(r0, sub)
            cs = pl.ds(c0, width)
            get = lambda n: stash_ref[n, rs, cs]
            front_cells = [palette.cell(get(0), get(1), get(2), get(4), get(5)),
                           palette.cell(get(1), get(2), get(3), get(6), get(7))]
            back_cells = [palette.cell(get(7 + j), get(8 + j), get(9 + j), get(14 + j - 1),
                                       get(18 + j - 1)) for j in range(1, 5)]
            shape = (sub, width)
            front = segment(front_cells, shape)
            own_back = segment(back_cells[:EDGE], shape)
            next_front = segment(back_cells[EDGE:], shape)
            middle = ([color_ref[c, rs, cs] for c in range(3)], depth_ref[rs, cs], trans_ref[rs, cs])
            result = join(only_if(first, front), middle)
            result = join(result, own_back)
            result = join(result, only_if(~last, next_front))
            for c in range(3):
                out_color_ref[c, rs, cs] = result[0][c]
            out_depth_ref[rs, cs] = result[1]


def render_block(table, flags, volume, side, front, back, rows, segments):
    depth, _, lanes = volume.shape
    smem = pl.BlockSpec(memory_space=pltpu.SMEM)
    vmem = pl.BlockSpec(memory_space=pltpu.VMEM)
    color_shape = jax.ShapeDtypeStruct((3, rows, lanes), jnp.float32)
    plane_shape = jax.ShapeDtypeStruct((rows, lanes), jnp.float32)
    middle = pl.pallas_call(
        lambda *refs: middle_kernel(*refs, segments=segments, rows=rows, width=256),
        in_specs=[smem, smem, vmem, vmem],
        out_specs=[vmem] * 5,
        out_shape=[color_shape, plane_shape, plane_shape,
                   jax.ShapeDtypeStruct((4, rows, lanes), jnp.float32),
                   jax.ShapeDtypeStruct((4, rows, lanes), jnp.float32)],
        scratch_shapes=[pltpu.VMEM((depth, rows, lanes), jnp.float32) for _ in range(3)],
        compiler_params=pltpu.CompilerParams(vmem_limit_bytes=48 * 1024 * 1024),
    )(table, flags, volume, side)
    return pl.pallas_call(
        lambda *refs: edge_kernel(*refs, segments=segments, rows=rows),
        in_specs=[smem, smem] + [vmem] * 7,
        out_specs=[vmem, vmem],
        out_shape=[color_shape, plane_shape],
        scratch_shapes=[pltpu.VMEM((22, rows, lanes), jnp.float32)],
        compiler_params=pltpu.CompilerParams(vmem_limit_bytes=48 * 1024 * 1024),
    )(table, flags, front, back, middle[3], middle[4], *middle[:3])


def body(volume, knot_pos, knot_color):
    depth_count = lax.axis_size("depth")
    depth, rows, width = volume.shape
    sigma_scale = 4.0 / (depth * depth_count)
    x_low = shifted(volume[:, rows - 2:], "tile", 1)
    x_high = shifted(volume[:, :2], "tile", -1)
    gap = jnp.zeros((depth, TALL - rows - 4, width), volume.dtype)
    side = jnp.concatenate([x_high, gap, x_low], axis=1).astype(jnp.float32)
    planes = lambda a, b: jnp.concatenate([volume[a:b].astype(jnp.float32), side[a:b]], axis=1)
    sides = jnp.concatenate([x_high, gap, x_low], axis=1)
    narrow = lambda a, b: jnp.concatenate([volume[a:b], sides[a:b]], axis=1)
    z_next = shifted(narrow(0, 2 * EDGE), "depth", -1).astype(jnp.float32)
    front = planes(0, 2)
    back = jnp.concatenate([planes(depth - 2, depth), z_next], axis=0)
    d = lax.axis_index("depth")
    t = lax.axis_index("tile")
    flags = jnp.stack([d == 0, d == depth_count - 1, t == 0, t == lax.axis_size("tile") - 1])
    table = ramp_table(knot_pos, knot_color, sigma_scale)
    brick_color, optical_depth = render_block(
        table, flags.astype(jnp.int32), volume, side, front, back, rows, knot_pos.shape[0] - 1)
    piece = width // depth_count
    weighted = jnp.concatenate([brick_color, optical_depth[None]], axis=0)
    weighted = weighted.reshape(4, rows, depth_count, piece).transpose(2, 0, 1, 3)
    blocks = lax.all_to_all(weighted, "depth", 0, 0, tiled=True)
    ahead = jnp.zeros((rows, piece), jnp.float32)
    image = jnp.zeros((3, rows, piece), jnp.float32)
    for b in range(depth_count):
        image = image + blocks[b, :3] * jnp.exp(-ahead)[None]
        ahead = ahead + blocks[b, 3]
    return jnp.concatenate([image, (1.0 - jnp.exp(-ahead))[None]], axis=0)


def solution(mesh):
    in_specs = (P("depth", "tile", None), P(), P())
    out_specs = P(None, "tile", "depth")
    return jax.shard_map(body, mesh=mesh, in_specs=in_specs, out_specs=out_specs, check_vma=False)
```

```python
import jax
import jax.numpy as jnp
from jax import lax
from jax.experimental import pallas as pl
from jax.experimental.pallas import tpu as pltpu
from jax.sharding import PartitionSpec as P

TALL = 24
EDGE = 2


def shifted(block, axis, move):
    size = lax.axis_size(axis)
    pairs = [(i, i + move) for i in range(size) if 0 <= i + move < size]
    return lax.ppermute(block, axis, pairs)


def ramp_table(knot_pos, knot_color, sigma_scale):
    knot_float = knot_pos.astype(jnp.float32)
    palette = knot_color.astype(jnp.float32) / 255.0
    palette = palette * jnp.array([1.0, 1.0, 1.0, sigma_scale], jnp.float32)[:, None]
    gaps = knot_float[1:] - knot_float[:-1]
    slopes = (palette[:, 1:] - palette[:, :-1]) / gaps[None]
    offsets = palette[:, :-1] - slopes * knot_float[None, :-1]
    count = knot_pos.shape[0]
    pad = lambda v: jnp.pad(v, (0, count - v.shape[0]))
    bounds = jnp.stack([knot_float[0], knot_float[-1]])
    rows = [knot_float] + [pad(offsets[c]) for c in range(4)] + [pad(slopes[c]) for c in range(4)]
    rows += [pad(bounds)]
    return jnp.stack(rows)


def y_prev(a):
    rolled = pltpu.roll(a, 1, 1)
    lane = lax.broadcasted_iota(jnp.int32, (a.shape[0], 128), 1)
    first = jnp.where(lane == 0, 0.0, rolled[:, :128])
    return jnp.concatenate([first, rolled[:, 128:]], axis=1)


def y_next(a):
    rolled = pltpu.roll(a, a.shape[1] - 1, 1)
    lane = lax.broadcasted_iota(jnp.int32, (a.shape[0], 128), 1)
    last = jnp.where(lane == 127, 0.0, rolled[:, -128:])
    return jnp.concatenate([rolled[:, :-128], last], axis=1)


def smooth_plane(low, mid, high, keep, rows):
    tall = mid.shape[0]
    near = low + high + pltpu.roll(mid, tall - 1, 0) + pltpu.roll(mid, 1, 0)
    near = near + y_prev(mid) + y_next(mid)
    smooth = 0.4 * mid + 0.1 * near
    if keep.shape[0] == tall:
        smooth = jnp.where(keep, smooth, 0.0)
    else:
        smooth = jnp.concatenate([smooth[:rows], jnp.where(keep, smooth[rows:], 0.0)], axis=0)
    smooth = smooth.astype(jnp.bfloat16).astype(jnp.float32)
    center = smooth[:rows]
    slope_x = 0.5 * (pltpu.roll(smooth, tall - 1, 0)[:rows] - pltpu.roll(smooth, 1, 0)[:rows])
    slope_y = 0.5 * (y_next(center) - y_prev(center))
    return center, slope_x * slope_x + slope_y * slope_y, 0.8 * slope_x


class Palette:
    def __init__(self, table, segments):
        self.knots = [table[0, k] for k in range(segments)]
        self.offsets = [[table[1 + c, k] for k in range(segments)] for c in range(4)]
        self.slopes = [[table[5 + c, k] for k in range(segments)] for c in range(4)]
        self.lo = table[9, 0]
        self.hi = table[9, 1]
        self.segments = segments

    def cell(self, before, center, after, square, facing):
        slope_z = 0.5 * (after - before)
        facing = jnp.abs(0.6 * slope_z + facing)
        norm = slope_z * slope_z + square + 0.1
        shade = 0.3 + 0.7 * facing * lax.rsqrt(norm)
        lookup = jnp.clip(127.5 + 70.0 * center, self.lo, self.hi)
        offset = [jnp.full_like(lookup, self.offsets[c][0]) for c in range(4)]
        slope = [jnp.full_like(lookup, self.slopes[c][0]) for c in range(4)]
        for k in range(1, self.segments):
            above = lookup >= self.knots[k]
            offset = [jnp.where(above, self.offsets[c][k], offset[c]) for c in range(4)]
            slope = [jnp.where(above, self.slopes[c][k], slope[c]) for c in range(4)]
        chan = [offset[c] + slope[c] * lookup for c in range(4)]
        return shade, chan


def row_keep(flags, tall, lanes, rows):
    row = lax.broadcasted_iota(jnp.int32, (tall, lanes), 0)
    return ((row != tall - 1) | (flags[2] == 0)) & ((row != rows) | (flags[3] == 0))


def middle_kernel(table, flags, volume_ref, side_ref, color_ref, depth_ref, trans_ref,
                  kept_ref, terms_ref, smooth_ref, square_ref, facing_ref, *, segments, rows, width):
    depth, _, lanes = volume_ref.shape
    tall = rows + side_ref.shape[1]
    keep = row_keep(flags, tall, lanes, rows)[rows:]

    def joined(i):
        return jnp.concatenate([volume_ref[i].astype(jnp.float32), side_ref[i]], axis=0)

    def plane(i, carry):
        center, square, facing = smooth_plane(joined(i - 1), joined(i), joined(i + 1), keep, rows)
        smooth_ref[i] = center
        square_ref[i] = square
        facing_ref[i] = facing
        return carry

    lax.fori_loop(1, depth - 1, plane, 0, unroll=2)
    for n, i in enumerate((1, 2, depth - 3, depth - 2)):
        kept_ref[n] = smooth_ref[i]
    for n, i in enumerate((1, depth - 2)):
        terms_ref[2 * n] = square_ref[i]
        terms_ref[2 * n + 1] = facing_ref[i]
    palette = Palette(table, segments)
    sub = 8
    for r0 in range(0, rows, sub):
        for c0 in range(0, lanes, width):
            rs = pl.ds(r0, sub)
            cs = pl.ds(c0, width)

            def step(z, carry):
                trans, acc0, acc1, acc2, total = carry
                shade, chan = palette.cell(
                    smooth_ref[z - 1, rs, cs], smooth_ref[z, rs, cs], smooth_ref[z + 1, rs, cs],
                    square_ref[z, rs, cs], facing_ref[z, rs, cs])
                ext = chan[3]
                fade = jnp.exp(-ext)
                weight = shade * (1.0 - fade) * trans
                acc0 = acc0 + weight * chan[0]
                acc1 = acc1 + weight * chan[1]
                acc2 = acc2 + weight * chan[2]
                return (trans * fade, acc0, acc1, acc2, total + ext)

            zeros = jnp.zeros((sub, width), jnp.float32)
            init = (jnp.ones((sub, width), jnp.float32), zeros, zeros, zeros, zeros)
            trans, acc0, acc1, acc2, total = lax.fori_loop(
                EDGE, depth - EDGE, step, init, unroll=4)
            color_ref[0, rs, cs] = acc0
            color_ref[1, rs, cs] = acc1
            color_ref[2, rs, cs] = acc2
            depth_ref[rs, cs] = total
            trans_ref[rs, cs] = trans


def edge_kernel(table, flags, front_ref, back_ref, kept_ref, terms_ref, color_ref, depth_ref,
                trans_ref, out_color_ref, out_depth_ref, *, segments, rows):
    tall, lanes = front_ref.shape[1:]
    keep = row_keep(flags, tall, lanes, rows)
    palette = Palette(table, segments)
    first = flags[0] == 1
    last = flags[1] == 1
    zero = jnp.zeros((rows, lanes), jnp.float32)
    s0, q0, f0 = smooth_plane(jnp.zeros((tall, lanes), jnp.float32), front_ref[0], front_ref[1],
                              keep, rows)
    s1, s2, s61, s62 = [kept_ref[n] for n in range(4)]
    q1, f1, q62, f62 = [terms_ref[n] for n in range(4)]
    front_cells = [palette.cell(zero, s0, s1, q0, f0), palette.cell(s0, s1, s2, q1, f1)]
    smoothed = [(s61, None, None), (s62, q62, f62)]
    for i in range(1, back_ref.shape[0] - 1):
        inside = keep & ~((i >= 2) & last)
        smoothed.append(smooth_plane(back_ref[i - 1], back_ref[i], back_ref[i + 1], inside, rows))
    back_cells = []
    for j in range(1, len(smoothed) - 1):
        back_cells.append(palette.cell(smoothed[j - 1][0], smoothed[j][0], smoothed[j + 1][0],
                                       smoothed[j][1], smoothed[j][2]))

    def segment(cells):
        color = [jnp.zeros((rows, lanes), jnp.float32) for c in range(3)]
        total = jnp.zeros((rows, lanes), jnp.float32)
        trans = jnp.ones((rows, lanes), jnp.float32)
        for shade, chan in cells:
            fade = jnp.exp(-chan[3])
            weight = shade * (1.0 - fade) * trans
            color = [color[c] + weight * chan[c] for c in range(3)]
            total = total + chan[3]
            trans = trans * fade
        return color, total, trans

    def join(a, b):
        return ([a[0][c] + a[2] * b[0][c] for c in range(3)], a[1] + b[1], a[2] * b[2])

    def only_if(flag, seg):
        color, total, trans = seg
        return ([jnp.where(flag, color[c], 0.0) for c in range(3)],
                jnp.where(flag, total, 0.0), jnp.where(flag, trans, 1.0))

    front = segment(front_cells)
    own_back = segment(back_cells[:EDGE])
    next_front = segment(back_cells[EDGE:])
    middle = ([color_ref[c] for c in range(3)], depth_ref[...], trans_ref[...])
    result = join(only_if(first, front), middle)
    result = join(result, own_back)
    result = join(result, only_if(~last, next_front))
    for c in range(3):
        out_color_ref[c] = result[0][c]
    out_depth_ref[...] = result[1]


def render_block(table, flags, volume, side, front, back, rows, segments):
    depth, _, lanes = volume.shape
    smem = pl.BlockSpec(memory_space=pltpu.SMEM)
    vmem = pl.BlockSpec(memory_space=pltpu.VMEM)
    color_shape = jax.ShapeDtypeStruct((3, rows, lanes), jnp.float32)
    plane_shape = jax.ShapeDtypeStruct((rows, lanes), jnp.float32)
    middle = pl.pallas_call(
        lambda *refs: middle_kernel(*refs, segments=segments, rows=rows, width=256),
        in_specs=[smem, smem, vmem, vmem],
        out_specs=[vmem] * 5,
        out_shape=[color_shape, plane_shape, plane_shape,
                   jax.ShapeDtypeStruct((4, rows, lanes), jnp.float32),
                   jax.ShapeDtypeStruct((4, rows, lanes), jnp.float32)],
        scratch_shapes=[pltpu.VMEM((depth, rows, lanes), jnp.float32) for _ in range(3)],
        compiler_params=pltpu.CompilerParams(vmem_limit_bytes=48 * 1024 * 1024),
    )(table, flags, volume, side)
    return pl.pallas_call(
        lambda *refs: edge_kernel(*refs, segments=segments, rows=rows),
        in_specs=[smem, smem] + [vmem] * 7,
        out_specs=[vmem, vmem],
        out_shape=[color_shape, plane_shape],
        compiler_params=pltpu.CompilerParams(vmem_limit_bytes=48 * 1024 * 1024),
    )(table, flags, front, back, middle[3], middle[4], *middle[:3])


def body(volume, knot_pos, knot_color):
    depth_count = lax.axis_size("depth")
    depth, rows, width = volume.shape
    sigma_scale = 4.0 / (depth * depth_count)
    x_low = shifted(volume[:, rows - 2:], "tile", 1)
    x_high = shifted(volume[:, :2], "tile", -1)
    gap = jnp.zeros((depth, TALL - rows - 4, width), volume.dtype)
    side = jnp.concatenate([x_high, gap, x_low], axis=1).astype(jnp.float32)
    planes = lambda a, b: jnp.concatenate([volume[a:b].astype(jnp.float32), side[a:b]], axis=1)
    sides = jnp.concatenate([x_high, gap, x_low], axis=1)
    narrow = lambda a, b: jnp.concatenate([volume[a:b], sides[a:b]], axis=1)
    z_next = shifted(narrow(0, 2 * EDGE), "depth", -1).astype(jnp.float32)
    front = planes(0, 2)
    back = jnp.concatenate([planes(depth - 2, depth), z_next], axis=0)
    d = lax.axis_index("depth")
    t = lax.axis_index("tile")
    flags = jnp.stack([d == 0, d == depth_count - 1, t == 0, t == lax.axis_size("tile") - 1])
    table = ramp_table(knot_pos, knot_color, sigma_scale)
    brick_color, optical_depth = render_block(
        table, flags.astype(jnp.int32), volume, side, front, back, rows, knot_pos.shape[0] - 1)
    piece = width // depth_count
    weighted = jnp.concatenate([brick_color, optical_depth[None]], axis=0)
    weighted = weighted.reshape(4, rows, depth_count, piece).transpose(2, 0, 1, 3)
    blocks = lax.all_to_all(weighted, "depth", 0, 0, tiled=True)
    ahead = jnp.zeros((rows, piece), jnp.float32)
    image = jnp.zeros((3, rows, piece), jnp.float32)
    for b in range(depth_count):
        image = image + blocks[b, :3] * jnp.exp(-ahead)[None]
        ahead = ahead + blocks[b, 3]
    return jnp.concatenate([image, (1.0 - jnp.exp(-ahead))[None]], axis=0)


def solution(mesh):
    in_specs = (P("depth", "tile", None), P(), P())
    out_specs = P(None, "tile", "depth")
    return jax.shard_map(body, mesh=mesh, in_specs=in_specs, out_specs=out_specs, check_vma=False)
```
